256 devices in a mesh: turb: 8 (over x, core), age: 8 (over z), span: 4 (over y).
Axes of the slice: x: 4, y: 4, z: 8, core: 2. Of those that a mesh axis runs over, the one named last changes fastest.
Arguments:
- positions: float32 [3, 16, 3, 64, 1024], P(None, 'turb', None, 'span', 'age'), may hold values from -6 to 6
- strengths: float32 [2, 16, 3, 64, 1024], P(None, 'turb', None, 'span', 'age'), may hold values from -12 to 12
- core_radius: float32 [16, 3, 64, 1024], P('turb', None, 'span', 'age'), may hold values from 0.3 to 1.5
- adjoint_seed: float32 [3, 16, 3, 64, 1024], P(None, 'turb', None, 'span', 'age'), may hold values from -6 to 6
- pair_target: int32 [8, 8, 4, 128], P('turb', 'age', 'span'), may hold values from 0 to 95
- pair_owner: int32 [8, 8, 4, 128], P('turb', 'age', 'span'), may hold values from 0 to 63, as said below
- pair_source: int32 [8, 8, 4, 128], P('turb', 'age', 'span'), may hold values from 0 to 95
Outputs:
- advected: float32 [3, 16, 3, 64, 1024], P(None, 'turb', None, 'span', 'age')
- grad_positions: float32 [3, 16, 3, 64, 1024], P(None, 'turb', None, 'span', 'age')
- grad_strengths: float32 [2, 16, 3, 64, 1024], P(None, 'turb', None, 'span', 'age')
The draws below stay inside these ranges and needn't reach their ends.
Inputs may be any that keep to these rules, and one draw needn't show every extreme that they name: `pair_owner`: at most 4 of the pairs of one device name one owner. One owner, the same for all devices, is named by exactly 4 pairs of every device.
All inputs are finite; a program needn't handle non-finite values.
Results may differ from the reference program's by a relative error of at most 0.0003.
Values sent between devices are 32-bit elements; how exact they have to be, the bound alone decides.
No kernel may reach another device: no remote copies, remote signals or barrier semaphores. Data moves between devices by JAX's collectives and lax.ppermute only.
A program may use at most 64 MiB of HBM per device.

```python
import math
import jax
import jax.numpy as jnp
from jax import lax

TURB_DEV = 2
BLADES = 3
STA_DEV = 16
AGE_DEV = 128
REACH = 8
PAIRS = 128
NTURB = 16
STATIONS = 64
AGES = 1024
GROUP = 64
CAP = 4
BLK = 96
N_TURB = 8
N_AGE = 8
N_SPAN = 4


def draw_pair_owner(key, part):
    hottest = jax.random.randint(jax.random.fold_in(key, 11), (), 0, GROUP)
    devices = N_TURB * N_AGE * N_SPAN
    keys = jax.random.split(jax.random.fold_in(key, 23), devices)

    def one_device(device_key):
        first_key, second_key = jax.random.split(device_key)
        others = jnp.arange((GROUP - 1) * CAP, dtype=jnp.int32) // CAP
        others = jnp.where(others >= hottest, others + 1, others)
        picked = jax.random.permutation(first_key, others)[:PAIRS - CAP]
        listed = jnp.concatenate([jnp.full((CAP,), hottest, dtype=jnp.int32), picked.astype(jnp.int32)])
        return jax.random.permutation(second_key, listed)
    return jax.vmap(one_device)(keys).reshape(N_TURB, N_AGE, N_SPAN, PAIRS).astype(jnp.int32)


def with_ends(entries, own_key, least, top_value):
    dims = entries.shape
    index_at = [jax.random.randint(jax.random.fold_in(own_key, axis), (), 0, dims[axis]) for axis in range(len(dims))]
    entries = entries.at[tuple(index_at)].set(least)
    longest = dims.index(max(dims))
    index_at[longest] = (index_at[longest] + 1) % dims[longest]
    return entries.at[tuple(index_at)].set(top_value)


def shard_levels(own_key, dims, pieces, low, high):
    def one(axis_at, parts):
        heights = jax.random.uniform(jax.random.fold_in(jax.random.fold_in(own_key, 6), axis_at), (parts,), jnp.float32, low / len(pieces), high / len(pieces))
        return jnp.repeat(jnp.exp(heights), dims[axis_at] // parts).reshape((-1,) + (1,) * (len(dims) - axis_at - 1))

    gain = one(*pieces[0])
    for cut in pieces[1:]:
        gain = gain * one(*cut)
    return gain


def centred(own_key, shape, width, bound, cuts=(), kind=jnp.bfloat16):
    loudness = shard_levels(own_key, shape, cuts, -0.22, 0.18) if cuts else 1.0
    entries = jax.random.normal(own_key, shape, jnp.float32) * width * loudness
    return jnp.minimum(jnp.maximum(entries, -bound), bound).astype(kind)


def setup_inputs(seed: int = 0) -> dict:
    streams_of = jax.random.split(jax.random.key(seed), 8)
    return {
        "positions": centred(streams_of[0], (3, NTURB, BLADES, STATIONS, AGES), 1.0, 6.0, ((1, 8), (3, 4), (4, 8)), jnp.float32),
        "strengths": centred(streams_of[1], (2, NTURB, BLADES, STATIONS, AGES), 2.0, 12.0, ((1, 8), (3, 4), (4, 8)), jnp.float32),
        "core_radius": jnp.clip(jnp.exp(math.log(1.5) - 1.60943787 * jax.random.uniform(streams_of[2], (NTURB, BLADES, STATIONS, AGES), jnp.float32) ** shard_levels(streams_of[2], (NTURB, BLADES, STATIONS, AGES), ((0, 8), (2, 4), (3, 8)), -0.2, 0.2)), 0.3, 1.5),
        "adjoint_seed": centred(streams_of[3], (3, NTURB, BLADES, STATIONS, AGES), 1.0, 6.0, ((1, 8), (3, 4), (4, 8)), jnp.float32),
        "pair_target": with_ends(jax.random.randint(streams_of[4], (N_TURB, N_AGE, N_SPAN, PAIRS), 0, BLK), jax.random.fold_in(streams_of[4], 1), 0, BLK - 1).astype(jnp.int32),
        "pair_owner": draw_pair_owner(jax.random.fold_in(streams_of[7], 71), 0),
        "pair_source": with_ends(jax.random.randint(streams_of[6], (N_TURB, N_AGE, N_SPAN, PAIRS), 0, BLK), jax.random.fold_in(streams_of[6], 1), 0, BLK - 1).astype(jnp.int32),
    }


time_step = 0.5
four_pi = 4.0 * math.pi
batch_rows = 128

def windows(payload):
    age_count = payload.shape[-1]
    padded = jnp.pad(payload, ((0, 0), (0, 0), (REACH, REACH)))
    stacked = jnp.stack([padded[:, :, REACH + offset:REACH + offset + age_count] for offset in range(-REACH, REACH)])
    shifted = jnp.arange(-REACH, REACH, dtype=jnp.int32)[:, None] + jnp.arange(age_count, dtype=jnp.int32)[None, :]
    inside = ((shifted >= 0) & (shifted < age_count)).astype(payload.dtype)
    return (stacked, inside)

def induced(targets, payload):
    stacked, inside = windows(payload)
    begins = stacked[:, :, 0:3]
    end_points = jnp.stack([stacked[:, :, 3:6], stacked[:, :, 6:9]])
    gammas = jnp.stack([stacked[:, :, 9], stacked[:, :, 10]]) * inside[None, :, None, :]
    core = jnp.where(inside[:, None, :] > 0, stacked[:, :, 11], 1.0)
    core_sq = core * core
    core_quad = core_sq * core_sq
    from_begin = targets[None] - begins
    from_end = targets[None, None] - end_points
    along = end_points - begins[None]
    near = from_begin[None]
    cross_x = near[..., 1, :] * from_end[..., 2, :] - near[..., 2, :] * from_end[..., 1, :]
    cross_y = near[..., 2, :] * from_end[..., 0, :] - near[..., 0, :] * from_end[..., 2, :]
    cross_z = near[..., 0, :] * from_end[..., 1, :] - near[..., 1, :] * from_end[..., 0, :]
    cross_sq = cross_x * cross_x + cross_y * cross_y + cross_z * cross_z
    length_sq = lax.optimization_barrier(jnp.sum(along * along, axis=-2)) + core_sq
    dist_begin = jnp.sqrt(lax.optimization_barrier(jnp.sum(from_begin * from_begin, axis=-2)) + core_sq)
    dist_end = jnp.sqrt(lax.optimization_barrier(jnp.sum(from_end * from_end, axis=-2)) + core_sq)
    projected = lax.optimization_barrier(jnp.sum(along * (near / dist_begin[None, :, :, None, :] - from_end / dist_end[..., None, :]), axis=-2))
    factor = gammas * projected / (four_pi * jnp.sqrt(cross_sq * cross_sq + core_quad * length_sq * length_sq))
    return jnp.stack([lax.optimization_barrier(jnp.sum(cross_x * factor, axis=(0, 1))), lax.optimization_barrier(jnp.sum(cross_y * factor, axis=(0, 1))), lax.optimization_barrier(jnp.sum(cross_z * factor, axis=(0, 1)))], axis=1)

def to_blocks(array):
    rows = array.shape[0]
    split = array.reshape(rows, N_TURB, TURB_DEV, BLADES, N_SPAN, STA_DEV, N_AGE, AGE_DEV)
    return jnp.transpose(split, (1, 6, 4, 2, 3, 5, 0, 7)).reshape(-1, rows, AGE_DEV)

def from_blocks(blocks):
    rows = blocks.shape[1]
    split = blocks.reshape(N_TURB, N_AGE, N_SPAN, TURB_DEV, BLADES, STA_DEV, rows, AGE_DEV)
    return jnp.transpose(split, (6, 0, 3, 4, 2, 5, 1, 7)).reshape(rows, N_TURB * TURB_DEV, BLADES, N_SPAN * STA_DEV, N_AGE * AGE_DEV)

def segment_data(nodes, circulation, core_radius):
    age_count = nodes.shape[-1]
    station_count = nodes.shape[3]
    trail_end = jnp.concatenate([nodes[..., 1:], jnp.zeros_like(nodes[..., :1])], axis=-1)
    shed_end = jnp.concatenate([nodes[:, :, :, 1:, :], jnp.zeros_like(nodes[:, :, :, :1, :])], axis=3)
    age_keep = (jnp.arange(age_count, dtype=jnp.int32) < age_count - 1).astype(nodes.dtype)
    station_keep = (jnp.arange(station_count, dtype=jnp.int32) < station_count - 1).astype(nodes.dtype)
    trail_gamma = circulation[0] * age_keep
    shed_gamma = circulation[1] * station_keep[:, None]
    return jnp.concatenate([nodes, trail_end, shed_end, trail_gamma[None], shed_gamma[None], core_radius[None]], axis=0)

def reference(positions, strengths, core_radius, adjoint_seed, pair_target, pair_owner, pair_source):
    devices = N_TURB * N_AGE * N_SPAN
    blocks_dev = TURB_DEV * BLADES * STA_DEV
    device_ids = jnp.arange(devices, dtype=jnp.int32)[:, None]
    target_index = (device_ids * blocks_dev + pair_target.reshape(devices, -1).astype(jnp.int32)).reshape(-1)
    span_ids = device_ids % N_SPAN
    source_index = ((pair_owner.reshape(devices, -1).astype(jnp.int32) * N_SPAN + span_ids) * blocks_dev + pair_source.reshape(devices, -1).astype(jnp.int32)).reshape(-1)
    total = target_index.shape[0]

    def batch_velocity(operands):
        return induced(operands[0], operands[1])

    def advect(nodes, circulation):
        payload = to_blocks(segment_data(nodes, circulation, core_radius))
        targets = to_blocks(nodes)
        pair_targets = targets[target_index].reshape(total // batch_rows, batch_rows, 3, AGE_DEV)
        pair_payload = payload[source_index].reshape(total // batch_rows, batch_rows, 12, AGE_DEV)
        velocity = lax.map(jax.checkpoint(batch_velocity), (pair_targets, pair_payload))
        summed = jnp.zeros_like(targets).at[target_index].add(velocity.reshape(total, 3, AGE_DEV))
        moved = nodes + time_step * from_blocks(summed)
        return moved.at[0].add(time_step)
    advected, pullback = jax.vjp(advect, positions, strengths)
    grad_positions, grad_strengths = pullback(adjoint_seed)
    return (advected, grad_positions, grad_strengths)
```

```python
import math

import jax
import jax.numpy as jnp
from jax import lax
from jax.sharding import PartitionSpec as P
from jax.experimental import pallas as pl
from jax.experimental.pallas import tpu as pltpu

REACH = 8


time_step = 0.5
four_pi = 4.0 * math.pi
batch_rows = 16


def shifted_2(value, axis, steps):
    count = lax.axis_size(axis)
    leading, last = (max(0, -steps), min(count, count - steps))
    return lax.ppermute(value, axis, [(source, source + steps) for source in range(leading, last)])


def windows(payload):
    age_count = payload.shape[-1]
    padded = jnp.pad(payload, ((0, 0), (0, 0), (REACH, REACH)))
    stacked = jnp.stack(
        [
            padded[:, :, REACH + offset : REACH + offset + age_count]
            for offset in range(-REACH, REACH)
        ]
    )
    shifted = (
        jnp.arange(-REACH, REACH, dtype=jnp.int32)[:, None]
        + jnp.arange(age_count, dtype=jnp.int32)[None, :]
    )
    inside = ((shifted >= 0) & (shifted < age_count)).astype(payload.dtype)
    return (stacked, inside)


def induced(targets, payload):
    stacked, inside = windows(payload)
    begins = stacked[:, :, 0:3]
    end_points = jnp.stack([stacked[:, :, 3:6], stacked[:, :, 6:9]])
    gammas = jnp.stack([stacked[:, :, 9], stacked[:, :, 10]]) * inside[None, :, None, :]
    core = jnp.where(inside[:, None, :] > 0, stacked[:, :, 11], 1.0)
    core_sq = core * core
    core_quad = core_sq * core_sq
    from_begin = targets[None] - begins
    from_end = targets[None, None] - end_points
    along = end_points - begins[None]
    near = from_begin[None]
    cross_x = near[..., 1, :] * from_end[..., 2, :] - near[..., 2, :] * from_end[..., 1, :]
    cross_y = near[..., 2, :] * from_end[..., 0, :] - near[..., 0, :] * from_end[..., 2, :]
    cross_z = near[..., 0, :] * from_end[..., 1, :] - near[..., 1, :] * from_end[..., 0, :]
    cross_sq = cross_x * cross_x + cross_y * cross_y + cross_z * cross_z
    length_sq = jnp.sum(along * along, axis=-2) + core_sq
    dist_begin = jnp.sqrt(jnp.sum(from_begin * from_begin, axis=-2) + core_sq)
    dist_end = jnp.sqrt(jnp.sum(from_end * from_end, axis=-2) + core_sq)
    projected = jnp.sum(
        along * (near / dist_begin[None, :, :, None, :] - from_end / dist_end[..., None, :]),
        axis=-2,
    )
    factor = (
        gammas
        * projected
        / (four_pi * jnp.sqrt(cross_sq * cross_sq + core_quad * length_sq * length_sq))
    )
    return jnp.stack(
        [
            jnp.sum(cross_x * factor, axis=(0, 1)),
            jnp.sum(cross_y * factor, axis=(0, 1)),
            jnp.sum(cross_z * factor, axis=(0, 1)),
        ],
        axis=1,
    )


GROUP_PAIRS = 8


def segment_pair(target, begin, trail_end, shed_end, trail_gamma, shed_gamma, core, inside):
    core_sq = core * core
    core_quad = core_sq * core_sq
    near = [target[i] - begin[i] for i in range(3)]
    begin_sq = near[0] * near[0] + near[1] * near[1] + near[2] * near[2]
    dist_begin = jnp.sqrt(begin_sq + core_sq)
    total = [0.0, 0.0, 0.0]
    for end_point, gamma in ((trail_end, trail_gamma), (shed_end, shed_gamma)):
        far = [target[i] - end_point[i] for i in range(3)]
        along = [end_point[i] - begin[i] for i in range(3)]
        cross_x = near[1] * far[2] - near[2] * far[1]
        cross_y = near[2] * far[0] - near[0] * far[2]
        cross_z = near[0] * far[1] - near[1] * far[0]
        cross_sq = cross_x * cross_x + cross_y * cross_y + cross_z * cross_z
        length_sq = along[0] * along[0] + along[1] * along[1] + along[2] * along[2] + core_sq
        dist_end = jnp.sqrt(far[0] * far[0] + far[1] * far[1] + far[2] * far[2] + core_sq)
        projected = (
            along[0] * (near[0] / dist_begin - far[0] / dist_end)
            + along[1] * (near[1] / dist_begin - far[1] / dist_end)
            + along[2] * (near[2] / dist_begin - far[2] / dist_end)
        )
        masked = jnp.where(inside, gamma, 0.0)
        factor = (
            masked
            * projected
            / (four_pi * jnp.sqrt(cross_sq * cross_sq + core_quad * length_sq * length_sq))
        )
        total = [total[0] + cross_x * factor, total[1] + cross_y * factor, total[2] + cross_z * factor]
    return tuple(total)


def pair_kernel(t_ref, s_ref, c_ref, v_ref, gt_ref, gs_ref):
    shape = t_ref.shape[1:]
    age_count = shape[-1]
    lane = lax.broadcasted_iota(jnp.int32, shape, 1)
    target = tuple(t_ref[i] for i in range(3))
    cotangent = tuple(c_ref[i] for i in range(3))
    rows = [s_ref[i] for i in range(12)]
    zero = jnp.zeros(shape, jnp.float32)
    velocity = [zero] * 3
    grad_target = [zero] * 3
    grad_rows = [zero] * 11
    for offset in range(-REACH, REACH):
        amount = (-offset) % age_count
        moved = [pltpu.roll(r, amount, 1) if amount else r for r in rows]
        inside = (lane + offset >= 0) & (lane + offset < age_count)
        core = moved[11]

        def field(t, b, te, se, tg, sg):
            return segment_pair(t, b, te, se, tg, sg, core, inside)

        u, pullback = jax.vjp(
            field,
            target,
            tuple(moved[0:3]),
            tuple(moved[3:6]),
            tuple(moved[6:9]),
            moved[9],
            moved[10],
        )
        d_t, d_b, d_te, d_se, d_tg, d_sg = pullback(cotangent)
        grads = list(d_b) + list(d_te) + list(d_se) + [d_tg, d_sg]
        back = (offset) % age_count
        for i in range(3):
            velocity[i] = velocity[i] + u[i]
            grad_target[i] = grad_target[i] + d_t[i]
        for i in range(11):
            g = pltpu.roll(grads[i], back, 1) if back else grads[i]
            grad_rows[i] = grad_rows[i] + g
    for i in range(3):
        v_ref[i] = velocity[i]
        gt_ref[i] = grad_target[i]
    for i in range(11):
        gs_ref[i] = grad_rows[i]


def run_pairs(targets, payload, cotangent):
    number = targets.shape[0]
    age_count = targets.shape[-1]
    step = GROUP_PAIRS

    def spec(rows):
        return pl.BlockSpec((rows, step, age_count), lambda i: (0, i, 0))

    t_rows = jnp.transpose(targets, (1, 0, 2))
    s_rows = jnp.transpose(payload, (1, 0, 2))
    c_rows = jnp.transpose(cotangent, (1, 0, 2))
    velocity, grad_targets, grad_payload = pl.pallas_call(
        pair_kernel,
        grid=(number // step,),
        in_specs=[spec(3), spec(12), spec(3)],
        out_specs=[spec(3), spec(3), spec(11)],
        out_shape=[
            jax.ShapeDtypeStruct((3, number, age_count), jnp.float32),
            jax.ShapeDtypeStruct((3, number, age_count), jnp.float32),
            jax.ShapeDtypeStruct((11, number, age_count), jnp.float32),
        ],
    )(t_rows, s_rows, c_rows)
    return (
        jnp.transpose(velocity, (1, 0, 2)),
        jnp.transpose(grad_targets, (1, 0, 2)),
        jnp.transpose(grad_payload, (1, 0, 2)),
    )


def onehot_sum(indices, rows, values):
    selector = (jnp.arange(rows, dtype=jnp.int32)[:, None] == indices[None, :]).astype(jnp.float32)
    flat = values.reshape(values.shape[0], -1)
    summed = jnp.dot(
        selector, flat, precision=lax.Precision.HIGHEST, preferred_element_type=jnp.float32
    )
    return summed.reshape((rows,) + values.shape[1:])


def local(positions, strengths, core_radius, adjoint_seed, pair_target, pair_owner, pair_source):
    shape_here = positions.shape
    station_here = shape_here[3]
    age_here = shape_here[4]
    blocks_here = shape_here[1] * shape_here[2] * station_here
    group_size = lax.axis_size("turb") * lax.axis_size("age")
    pair_count = pair_target.shape[-1]
    capacity = 2 * pair_count // group_size
    target_ids = pair_target.reshape(pair_count)
    owner_ids = pair_owner.reshape(pair_count)
    source_ids = pair_source.reshape(pair_count)
    next_ages = shifted_2(positions[..., 0], "age", -1)
    next_stations = shifted_2(positions[:, :, :, 0, :], "span", -1)
    age_keep = (
        lax.axis_index("age") * age_here + jnp.arange(age_here, dtype=jnp.int32)
        < age_here * lax.axis_size("age") - 1
    ).astype(jnp.float32)
    station_keep = (
        lax.axis_index("span") * station_here + jnp.arange(station_here, dtype=jnp.int32)
        < station_here * lax.axis_size("span") - 1
    ).astype(jnp.float32)

    def build(nodes, after_age, after_station, circulation):
        trail_end = jnp.concatenate([nodes[..., 1:], after_age[..., None]], axis=-1)
        shed_end = jnp.concatenate([nodes[:, :, :, 1:, :], after_station[:, :, :, None, :]], axis=3)
        trail_gamma = circulation[0] * age_keep
        shed_gamma = circulation[1] * station_keep[:, None]
        stacked = jnp.concatenate(
            [nodes, trail_end, shed_end, trail_gamma[None], shed_gamma[None], core_radius[None]],
            axis=0,
        )
        return jnp.transpose(stacked.reshape(12, blocks_here, age_here), (1, 0, 2))

    payload, build_pullback = jax.vjp(build, positions, next_ages, next_stations, strengths)

    def to_rows(array):
        return jnp.transpose(array.reshape(array.shape[0], blocks_here, age_here), (1, 0, 2))

    def from_rows(array):
        return jnp.transpose(array, (1, 0, 2)).reshape(shape_here)

    target_blocks = to_rows(positions)
    seed_blocks = to_rows(adjoint_seed) * time_step
    owner_onehot = (owner_ids[:, None] == jnp.arange(group_size, dtype=jnp.int32)[None, :]).astype(
        jnp.int32
    )
    rank_within = jnp.sum((jnp.cumsum(owner_onehot, axis=0) - owner_onehot) * owner_onehot, axis=1)
    slot_index = owner_ids * capacity + rank_within
    request = (
        jnp.zeros((group_size * capacity,), jnp.int32)
        .at[slot_index]
        .set(source_ids)
        .reshape(group_size, capacity)
    )
    asked = lax.all_to_all(
        request, ("turb", "age"), split_axis=0, concat_axis=0, tiled=True
    ).reshape(group_size * capacity)
    pair_targets = target_blocks[target_ids]
    pair_seed = seed_blocks[target_ids]
    picked = payload[asked].reshape(group_size, capacity, 12, age_here)
    fetched = lax.all_to_all(
        picked, ("turb", "age"), split_axis=0, concat_axis=0, tiled=True
    ).reshape(group_size * capacity, 12, age_here)
    pair_velocity, pair_grad, payload_terms = run_pairs(
        pair_targets, fetched[slot_index], pair_seed
    )
    payload_terms = jnp.concatenate(
        [payload_terms, jnp.zeros_like(payload_terms[:, :1])], axis=1
    )
    outgoing = (
        jnp.zeros((group_size * capacity, 12, age_here), jnp.float32)
        .at[slot_index]
        .set(payload_terms)
    )
    returned = lax.all_to_all(
        outgoing.reshape(group_size, capacity, 12, age_here),
        ("turb", "age"),
        split_axis=0,
        concat_axis=0,
        tiled=True,
    )
    payload_grad = onehot_sum(
        asked, blocks_here, returned.reshape(group_size * capacity, 12, age_here)
    )
    velocity = onehot_sum(target_ids, blocks_here, pair_velocity)
    target_grad = onehot_sum(target_ids, blocks_here, pair_grad)
    advected = positions + time_step * from_rows(velocity)
    advected = advected.at[0].add(time_step)
    grad_nodes, grad_after_age, grad_after_station, grad_strengths = build_pullback(payload_grad)
    from_prior_age = shifted_2(grad_after_age, "age", 1)
    from_prior_station = shifted_2(grad_after_station, "span", 1)
    grad_positions = adjoint_seed + grad_nodes + from_rows(target_grad)
    grad_positions = grad_positions.at[..., 0].add(from_prior_age)
    grad_positions = grad_positions.at[:, :, :, 0, :].add(from_prior_station)
    return (advected, grad_positions, grad_strengths)


def solution(mesh):
    placed = (
        P(None, "turb", None, "span", "age"),
        P(None, "turb", None, "span", "age"),
        P("turb", None, "span", "age"),
        P(None, "turb", None, "span", "age"),
        P("turb", "age", "span", None),
        P("turb", "age", "span", None),
        P("turb", "age", "span", None),
    )
    return jax.shard_map(
        local,
        mesh=mesh,
        in_specs=placed,
        out_specs=(
            P(None, "turb", None, "span", "age"),
            P(None, "turb", None, "span", "age"),
            P(None, "turb", None, "span", "age"),
        ),
        check_vma=False,
    )
```

```python
import math

import jax
import jax.numpy as jnp
from jax import lax
from jax.sharding import PartitionSpec as P
from jax.experimental import pallas as pl
from jax.experimental.pallas import tpu as pltpu

REACH = 8


time_step = 0.5
four_pi = 4.0 * math.pi
batch_rows = 16


def shifted_2(value, axis, steps):
    count = lax.axis_size(axis)
    leading, last = (max(0, -steps), min(count, count - steps))
    return lax.ppermute(value, axis, [(source, source + steps) for source in range(leading, last)])


def windows(payload):
    age_count = payload.shape[-1]
    padded = jnp.pad(payload, ((0, 0), (0, 0), (REACH, REACH)))
    stacked = jnp.stack(
        [
            padded[:, :, REACH + offset : REACH + offset + age_count]
            for offset in range(-REACH, REACH)
        ]
    )
    shifted = (
        jnp.arange(-REACH, REACH, dtype=jnp.int32)[:, None]
        + jnp.arange(age_count, dtype=jnp.int32)[None, :]
    )
    inside = ((shifted >= 0) & (shifted < age_count)).astype(payload.dtype)
    return (stacked, inside)


def induced(targets, payload):
    stacked, inside = windows(payload)
    begins = stacked[:, :, 0:3]
    end_points = jnp.stack([stacked[:, :, 3:6], stacked[:, :, 6:9]])
    gammas = jnp.stack([stacked[:, :, 9], stacked[:, :, 10]]) * inside[None, :, None, :]
    core = jnp.where(inside[:, None, :] > 0, stacked[:, :, 11], 1.0)
    core_sq = core * core
    core_quad = core_sq * core_sq
    from_begin = targets[None] - begins
    from_end = targets[None, None] - end_points
    along = end_points - begins[None]
    near = from_begin[None]
    cross_x = near[..., 1, :] * from_end[..., 2, :] - near[..., 2, :] * from_end[..., 1, :]
    cross_y = near[..., 2, :] * from_end[..., 0, :] - near[..., 0, :] * from_end[..., 2, :]
    cross_z = near[..., 0, :] * from_end[..., 1, :] - near[..., 1, :] * from_end[..., 0, :]
    cross_sq = cross_x * cross_x + cross_y * cross_y + cross_z * cross_z
    length_sq = jnp.sum(along * along, axis=-2) + core_sq
    dist_begin = jnp.sqrt(jnp.sum(from_begin * from_begin, axis=-2) + core_sq)
    dist_end = jnp.sqrt(jnp.sum(from_end * from_end, axis=-2) + core_sq)
    projected = jnp.sum(
        along * (near / dist_begin[None, :, :, None, :] - from_end / dist_end[..., None, :]),
        axis=-2,
    )
    factor = (
        gammas
        * projected
        / (four_pi * jnp.sqrt(cross_sq * cross_sq + core_quad * length_sq * length_sq))
    )
    return jnp.stack(
        [
            jnp.sum(cross_x * factor, axis=(0, 1)),
            jnp.sum(cross_y * factor, axis=(0, 1)),
            jnp.sum(cross_z * factor, axis=(0, 1)),
        ],
        axis=1,
    )


GROUP_PAIRS = 8


def segment_pair(target, begin, trail_end, shed_end, trail_gamma, shed_gamma, core, inside):
    core_sq = core * core
    core_quad = core_sq * core_sq
    near = [target[i] - begin[i] for i in range(3)]
    begin_sq = near[0] * near[0] + near[1] * near[1] + near[2] * near[2]
    dist_begin = jnp.sqrt(begin_sq + core_sq)
    total = [0.0, 0.0, 0.0]
    for end_point, gamma in ((trail_end, trail_gamma), (shed_end, shed_gamma)):
        far = [target[i] - end_point[i] for i in range(3)]
        along = [end_point[i] - begin[i] for i in range(3)]
        cross_x = near[1] * far[2] - near[2] * far[1]
        cross_y = near[2] * far[0] - near[0] * far[2]
        cross_z = near[0] * far[1] - near[1] * far[0]
        cross_sq = cross_x * cross_x + cross_y * cross_y + cross_z * cross_z
        length_sq = along[0] * along[0] + along[1] * along[1] + along[2] * along[2] + core_sq
        dist_end = jnp.sqrt(far[0] * far[0] + far[1] * far[1] + far[2] * far[2] + core_sq)
        projected = (
            along[0] * (near[0] / dist_begin - far[0] / dist_end)
            + along[1] * (near[1] / dist_begin - far[1] / dist_end)
            + along[2] * (near[2] / dist_begin - far[2] / dist_end)
        )
        masked = jnp.where(inside, gamma, 0.0)
        factor = (
            masked
            * projected
            / (four_pi * jnp.sqrt(cross_sq * cross_sq + core_quad * length_sq * length_sq))
        )
        total = [total[0] + cross_x * factor, total[1] + cross_y * factor, total[2] + cross_z * factor]
    return tuple(total)


def pair_kernel(t_ref, s_ref, c_ref, v_ref, gt_ref, gs_ref):
    shape = t_ref.shape[1:]
    age_count = shape[-1]
    lane = lax.broadcasted_iota(jnp.int32, shape, 1)
    target = tuple(t_ref[i] for i in range(3))
    cotangent = tuple(c_ref[i] for i in range(3))
    rows = [s_ref[i] for i in range(12)]
    zero = jnp.zeros(shape, jnp.float32)
    velocity = [zero] * 3
    grad_target = [zero] * 3
    grad_rows = [zero] * 11
    for offset in range(-REACH, REACH):
        amount = (-offset) % age_count
        moved = [pltpu.roll(r, amount, 1) if amount else r for r in rows]
        inside = (lane + offset >= 0) & (lane + offset < age_count)
        core = moved[11]

        def field(t, b, te, se, tg, sg):
            return segment_pair(t, b, te, se, tg, sg, core, inside)

        u, pullback = jax.vjp(
            field,
            target,
            tuple(moved[0:3]),
            tuple(moved[3:6]),
            tuple(moved[6:9]),
            moved[9],
            moved[10],
        )
        d_t, d_b, d_te, d_se, d_tg, d_sg = pullback(cotangent)
        grads = list(d_b) + list(d_te) + list(d_se) + [d_tg, d_sg]
        back = (offset) % age_count
        for i in range(3):
            velocity[i] = velocity[i] + u[i]
            grad_target[i] = grad_target[i] + d_t[i]
        for i in range(11):
            g = pltpu.roll(grads[i], back, 1) if back else grads[i]
            grad_rows[i] = grad_rows[i] + g
    for i in range(3):
        v_ref[i] = velocity[i]
        gt_ref[i] = grad_target[i]
    for i in range(11):
        gs_ref[i] = grad_rows[i]


def run_pairs(targets, payload, cotangent):
    number = targets.shape[0]
    age_count = targets.shape[-1]
    step = GROUP_PAIRS

    def spec(rows):
        return pl.BlockSpec((rows, step, age_count), lambda i: (0, i, 0))

    t_rows = jnp.transpose(targets, (1, 0, 2))
    s_rows = jnp.transpose(payload, (1, 0, 2))
    c_rows = jnp.transpose(cotangent, (1, 0, 2))
    velocity, grad_targets, grad_payload = pl.pallas_call(
        pair_kernel,
        grid=(number // step,),
        in_specs=[spec(3), spec(12), spec(3)],
        out_specs=[spec(3), spec(3), spec(11)],
        out_shape=[
            jax.ShapeDtypeStruct((3, number, age_count), jnp.float32),
            jax.ShapeDtypeStruct((3, number, age_count), jnp.float32),
            jax.ShapeDtypeStruct((11, number, age_count), jnp.float32),
        ],
    )(t_rows, s_rows, c_rows)
    return (
        jnp.transpose(velocity, (1, 0, 2)),
        jnp.transpose(grad_targets, (1, 0, 2)),
        jnp.transpose(grad_payload, (1, 0, 2)),
    )


def onehot_sum(indices, rows, values):
    selector = (jnp.arange(rows, dtype=jnp.int32)[:, None] == indices[None, :]).astype(jnp.float32)
    flat = values.reshape(values.shape[0], -1)
    summed = jnp.dot(
        selector, flat, precision=lax.Precision.HIGHEST, preferred_element_type=jnp.float32
    )
    return summed.reshape((rows,) + values.shape[1:])


def local(positions, strengths, core_radius, adjoint_seed, pair_target, pair_owner, pair_source):
    shape_here = positions.shape
    station_here = shape_here[3]
    age_here = shape_here[4]
    blocks_here = shape_here[1] * shape_here[2] * station_here
    group_size = lax.axis_size("turb") * lax.axis_size("age")
    pair_count = pair_target.shape[-1]
    capacity = 2 * pair_count // group_size
    target_ids = pair_target.reshape(pair_count)
    owner_ids = pair_owner.reshape(pair_count)
    source_ids = pair_source.reshape(pair_count)
    next_ages = shifted_2(positions[..., 0], "age", -1)
    next_stations = shifted_2(positions[:, :, :, 0, :], "span", -1)
    age_keep = (
        lax.axis_index("age") * age_here + jnp.arange(age_here, dtype=jnp.int32)
        < age_here * lax.axis_size("age") - 1
    ).astype(jnp.float32)
    station_keep = (
        lax.axis_index("span") * station_here + jnp.arange(station_here, dtype=jnp.int32)
        < station_here * lax.axis_size("span") - 1
    ).astype(jnp.float32)

    def build(nodes, after_age, after_station, circulation):
        trail_end = jnp.concatenate([nodes[..., 1:], after_age[..., None]], axis=-1)
        shed_end = jnp.concatenate([nodes[:, :, :, 1:, :], after_station[:, :, :, None, :]], axis=3)
        trail_gamma = circulation[0] * age_keep
        shed_gamma = circulation[1] * station_keep[:, None]
        stacked = jnp.concatenate(
            [nodes, trail_end, shed_end, trail_gamma[None], shed_gamma[None], core_radius[None]],
            axis=0,
        )
        return jnp.transpose(stacked.reshape(12, blocks_here, age_here), (1, 0, 2))

    payload, build_pullback = jax.vjp(build, positions, next_ages, next_stations, strengths)

    def to_rows(array):
        return jnp.transpose(array.reshape(array.shape[0], blocks_here, age_here), (1, 0, 2))

    def from_rows(array):
        return jnp.transpose(array, (1, 0, 2)).reshape(shape_here)

    target_blocks = to_rows(positions)
    seed_blocks = to_rows(adjoint_seed) * time_step
    owner_onehot = (owner_ids[:, None] == jnp.arange(group_size, dtype=jnp.int32)[None, :]).astype(
        jnp.int32
    )
    rank_within = jnp.sum((jnp.cumsum(owner_onehot, axis=0) - owner_onehot) * owner_onehot, axis=1)
    slot_index = owner_ids * capacity + rank_within
    slot_count = group_size * capacity
    pair_targets = target_blocks[target_ids]
    pair_seed = seed_blocks[target_ids]
    ident = jnp.broadcast_to(
        source_ids.astype(jnp.float32)[:, None, None], (pair_count, 1, age_here)
    )
    sent = jnp.concatenate([pair_targets, pair_seed, ident], axis=1)
    outgoing = (
        jnp.zeros((slot_count, 7, age_here), jnp.float32)
        .at[:, 6]
        .set(-1.0)
        .at[slot_index]
        .set(sent)
    )
    received = lax.all_to_all(
        outgoing.reshape(group_size, capacity, 7, age_here),
        ("turb", "age"),
        split_axis=0,
        concat_axis=0,
        tiled=True,
    ).reshape(slot_count, 7, age_here)
    asked = received[:, 6, 0].astype(jnp.int32)
    slot_payload = payload[jnp.clip(asked, 0, blocks_here - 1)]
    slot_velocity, slot_grad, payload_terms = run_pairs(
        received[:, 0:3], slot_payload, received[:, 3:6]
    )
    payload_terms = jnp.concatenate(
        [payload_terms, jnp.zeros_like(payload_terms[:, :1])], axis=1
    )
    payload_grad = onehot_sum(asked, blocks_here, payload_terms)
    answered = lax.all_to_all(
        jnp.concatenate([slot_velocity, slot_grad], axis=1).reshape(
            group_size, capacity, 6, age_here
        ),
        ("turb", "age"),
        split_axis=0,
        concat_axis=0,
        tiled=True,
    ).reshape(slot_count, 6, age_here)[slot_index]
    velocity = onehot_sum(target_ids, blocks_here, answered[:, 0:3])
    target_grad = onehot_sum(target_ids, blocks_here, answered[:, 3:6])
    advected = positions + time_step * from_rows(velocity)
    advected = advected.at[0].add(time_step)
    grad_nodes, grad_after_age, grad_after_station, grad_strengths = build_pullback(payload_grad)
    from_prior_age = shifted_2(grad_after_age, "age", 1)
    from_prior_station = shifted_2(grad_after_station, "span", 1)
    grad_positions = adjoint_seed + grad_nodes + from_rows(target_grad)
    grad_positions = grad_positions.at[..., 0].add(from_prior_age)
    grad_positions = grad_positions.at[:, :, :, 0, :].add(from_prior_station)
    return (advected, grad_positions, grad_strengths)


def solution(mesh):
    placed = (
        P(None, "turb", None, "span", "age"),
        P(None, "turb", None, "span", "age"),
        P("turb", None, "span", "age"),
        P(None, "turb", None, "span", "age"),
        P("turb", "age", "span", None),
        P("turb", "age", "span", None),
        P("turb", "age", "span", None),
    )
    return jax.shard_map(
        local,
        mesh=mesh,
        in_specs=placed,
        out_specs=(
            P(None, "turb", None, "span", "age"),
            P(None, "turb", None, "span", "age"),
            P(None, "turb", None, "span", "age"),
        ),
        check_vma=False,
    )
```

```python
import math

import jax
import jax.numpy as jnp
from jax import lax
from jax.sharding import PartitionSpec as P
from jax.experimental import pallas as pl
from jax.experimental.pallas import tpu as pltpu

REACH = 8


time_step = 0.5
four_pi = 4.0 * math.pi
batch_rows = 16


def shifted_2(value, axis, steps):
    count = lax.axis_size(axis)
    leading, last = (max(0, -steps), min(count, count - steps))
    return lax.ppermute(value, axis, [(source, source + steps) for source in range(leading, last)])


def windows(payload):
    age_count = payload.shape[-1]
    padded = jnp.pad(payload, ((0, 0), (0, 0), (REACH, REACH)))
    stacked = jnp.stack(
        [
            padded[:, :, REACH + offset : REACH + offset + age_count]
            for offset in range(-REACH, REACH)
        ]
    )
    shifted = (
        jnp.arange(-REACH, REACH, dtype=jnp.int32)[:, None]
        + jnp.arange(age_count, dtype=jnp.int32)[None, :]
    )
    inside = ((shifted >= 0) & (shifted < age_count)).astype(payload.dtype)
    return (stacked, inside)


def induced(targets, payload):
    stacked, inside = windows(payload)
    begins = stacked[:, :, 0:3]
    end_points = jnp.stack([stacked[:, :, 3:6], stacked[:, :, 6:9]])
    gammas = jnp.stack([stacked[:, :, 9], stacked[:, :, 10]]) * inside[None, :, None, :]
    core = jnp.where(inside[:, None, :] > 0, stacked[:, :, 11], 1.0)
    core_sq = core * core
    core_quad = core_sq * core_sq
    from_begin = targets[None] - begins
    from_end = targets[None, None] - end_points
    along = end_points - begins[None]
    near = from_begin[None]
    cross_x = near[..., 1, :] * from_end[..., 2, :] - near[..., 2, :] * from_end[..., 1, :]
    cross_y = near[..., 2, :] * from_end[..., 0, :] - near[..., 0, :] * from_end[..., 2, :]
    cross_z = near[..., 0, :] * from_end[..., 1, :] - near[..., 1, :] * from_end[..., 0, :]
    cross_sq = cross_x * cross_x + cross_y * cross_y + cross_z * cross_z
    length_sq = jnp.sum(along * along, axis=-2) + core_sq
    dist_begin = jnp.sqrt(jnp.sum(from_begin * from_begin, axis=-2) + core_sq)
    dist_end = jnp.sqrt(jnp.sum(from_end * from_end, axis=-2) + core_sq)
    projected = jnp.sum(
        along * (near / dist_begin[None, :, :, None, :] - from_end / dist_end[..., None, :]),
        axis=-2,
    )
    factor = (
        gammas
        * projected
        / (four_pi * jnp.sqrt(cross_sq * cross_sq + core_quad * length_sq * length_sq))
    )
    return jnp.stack(
        [
            jnp.sum(cross_x * factor, axis=(0, 1)),
            jnp.sum(cross_y * factor, axis=(0, 1)),
            jnp.sum(cross_z * factor, axis=(0, 1)),
        ],
        axis=1,
    )


GROUP_PAIRS = 8


def dot3(a, b):
    return a[0] * b[0] + a[1] * b[1] + a[2] * b[2]


def cross3(a, b):
    return (
        a[1] * b[2] - a[2] * b[1],
        a[2] * b[0] - a[0] * b[2],
        a[0] * b[1] - a[1] * b[0],
    )


def segment_pair(target, begin, ends, gammas, core, inside, weight):
    core_sq = core * core
    core_quad = core_sq * core_sq
    near = [target[i] - begin[i] for i in range(3)]
    inv_begin = lax.rsqrt(dot3(near, near) + core_sq)
    velocity = [0.0, 0.0, 0.0]
    grad_target = [0.0, 0.0, 0.0]
    grad_begin = [0.0, 0.0, 0.0]
    grad_ends = []
    grad_gammas = []
    for end_point, raw_gamma in zip(ends, gammas):
        gamma = jnp.where(inside, raw_gamma, 0.0)
        far = [target[i] - end_point[i] for i in range(3)]
        along = [end_point[i] - begin[i] for i in range(3)]
        cross = cross3(near, far)
        cross_sq = dot3(cross, cross)
        length_sq = dot3(along, along) + core_sq
        inv_end = lax.rsqrt(dot3(far, far) + core_sq)
        along_near = dot3(along, near)
        along_far = dot3(along, far)
        projected = along_near * inv_begin - along_far * inv_end
        inv_den = lax.rsqrt(cross_sq * cross_sq + core_quad * length_sq * length_sq)
        base = projected * inv_den * (1.0 / four_pi)
        factor = gamma * base
        for i in range(3):
            velocity[i] = velocity[i] + cross[i] * factor
        ct_factor = dot3(cross, weight)
        grad_gammas.append(jnp.where(inside, ct_factor * base, 0.0))
        ct_proj = ct_factor * gamma * inv_den * (1.0 / four_pi)
        ct_q = -0.5 * ct_factor * factor * inv_den * inv_den
        cross_scale = 4.0 * cross_sq * ct_q
        along_scale = 4.0 * core_quad * length_sq * ct_q
        ct_cross = [factor * weight[i] + cross_scale * cross[i] for i in range(3)]
        near_scale = ct_proj * inv_begin
        far_scale = ct_proj * inv_end
        near_radial = near_scale * along_near * inv_begin * inv_begin
        far_radial = far_scale * along_far * inv_end * inv_end
        from_far = cross3(far, ct_cross)
        from_near = cross3(ct_cross, near)
        ct_along = [
            along_scale * along[i] + near_scale * near[i] - far_scale * far[i] for i in range(3)
        ]
        ct_near = [near_scale * along[i] - near_radial * near[i] + from_far[i] for i in range(3)]
        ct_far = [-far_scale * along[i] + far_radial * far[i] + from_near[i] for i in range(3)]
        for i in range(3):
            grad_target[i] = grad_target[i] + ct_near[i] + ct_far[i]
            grad_begin[i] = grad_begin[i] - ct_near[i] - ct_along[i]
        grad_ends.append([ct_along[i] - ct_far[i] for i in range(3)])
    return velocity, grad_target, grad_begin, grad_ends, grad_gammas


def pair_kernel(t_ref, s_ref, c_ref, v_ref, gt_ref, gs_ref):
    shape = t_ref.shape[1:]
    age_count = shape[-1]
    lane = lax.broadcasted_iota(jnp.int32, shape, 1)
    target = [t_ref[i] for i in range(3)]
    cotangent = [c_ref[i] for i in range(3)]
    rows = [s_ref[i] for i in range(12)]
    zero = jnp.zeros(shape, jnp.float32)
    velocity = [zero] * 3
    grad_target = [zero] * 3
    grad_rows = [zero] * 11
    for offset in range(-REACH, REACH):
        amount = (-offset) % age_count
        moved = [pltpu.roll(r, amount, 1) if amount else r for r in rows]
        inside = (lane + offset >= 0) & (lane + offset < age_count)
        u, d_t, d_b, d_ends, d_gammas = segment_pair(
            target,
            moved[0:3],
            (moved[3:6], moved[6:9]),
            (moved[9], moved[10]),
            moved[11],
            inside,
            cotangent,
        )
        grads = list(d_b) + list(d_ends[0]) + list(d_ends[1]) + list(d_gammas)
        back = offset % age_count
        for i in range(3):
            velocity[i] = velocity[i] + u[i]
            grad_target[i] = grad_target[i] + d_t[i]
        for i in range(11):
            g = pltpu.roll(grads[i], back, 1) if back else grads[i]
            grad_rows[i] = grad_rows[i] + g
    for i in range(3):
        v_ref[i] = velocity[i]
        gt_ref[i] = grad_target[i]
    for i in range(11):
        gs_ref[i] = grad_rows[i]


def run_pairs(targets, payload, cotangent):
    number = targets.shape[0]
    age_count = targets.shape[-1]
    step = GROUP_PAIRS

    def spec(rows):
        return pl.BlockSpec((rows, step, age_count), lambda i: (0, i, 0))

    t_rows = jnp.transpose(targets, (1, 0, 2))
    s_rows = jnp.transpose(payload, (1, 0, 2))
    c_rows = jnp.transpose(cotangent, (1, 0, 2))
    velocity, grad_targets, grad_payload = pl.pallas_call(
        pair_kernel,
        grid=(number // step,),
        in_specs=[spec(3), spec(12), spec(3)],
        out_specs=[spec(3), spec(3), spec(11)],
        out_shape=[
            jax.ShapeDtypeStruct((3, number, age_count), jnp.float32),
            jax.ShapeDtypeStruct((3, number, age_count), jnp.float32),
            jax.ShapeDtypeStruct((11, number, age_count), jnp.float32),
        ],
    )(t_rows, s_rows, c_rows)
    return (
        jnp.transpose(velocity, (1, 0, 2)),
        jnp.transpose(grad_targets, (1, 0, 2)),
        jnp.transpose(grad_payload, (1, 0, 2)),
    )


def onehot_sum(indices, rows, values):
    selector = (jnp.arange(rows, dtype=jnp.int32)[:, None] == indices[None, :]).astype(jnp.float32)
    flat = values.reshape(values.shape[0], -1)
    summed = jnp.dot(
        selector, flat, precision=lax.Precision.HIGHEST, preferred_element_type=jnp.float32
    )
    return summed.reshape((rows,) + values.shape[1:])


def local(positions, strengths, core_radius, adjoint_seed, pair_target, pair_owner, pair_source):
    shape_here = positions.shape
    station_here = shape_here[3]
    age_here = shape_here[4]
    blocks_here = shape_here[1] * shape_here[2] * station_here
    group_size = lax.axis_size("turb") * lax.axis_size("age")
    pair_count = pair_target.shape[-1]
    capacity = 2 * pair_count // group_size
    target_ids = pair_target.reshape(pair_count)
    owner_ids = pair_owner.reshape(pair_count)
    source_ids = pair_source.reshape(pair_count)
    next_ages = shifted_2(positions[..., 0], "age", -1)
    next_stations = shifted_2(positions[:, :, :, 0, :], "span", -1)
    age_keep = (
        lax.axis_index("age") * age_here + jnp.arange(age_here, dtype=jnp.int32)
        < age_here * lax.axis_size("age") - 1
    ).astype(jnp.float32)
    station_keep = (
        lax.axis_index("span") * station_here + jnp.arange(station_here, dtype=jnp.int32)
        < station_here * lax.axis_size("span") - 1
    ).astype(jnp.float32)

    def build(nodes, after_age, after_station, circulation):
        trail_end = jnp.concatenate([nodes[..., 1:], after_age[..., None]], axis=-1)
        shed_end = jnp.concatenate([nodes[:, :, :, 1:, :], after_station[:, :, :, None, :]], axis=3)
        trail_gamma = circulation[0] * age_keep
        shed_gamma = circulation[1] * station_keep[:, None]
        stacked = jnp.concatenate(
            [nodes, trail_end, shed_end, trail_gamma[None], shed_gamma[None], core_radius[None]],
            axis=0,
        )
        return jnp.transpose(stacked.reshape(12, blocks_here, age_here), (1, 0, 2))

    payload, build_pullback = jax.vjp(build, positions, next_ages, next_stations, strengths)

    def to_rows(array):
        return jnp.transpose(array.reshape(array.shape[0], blocks_here, age_here), (1, 0, 2))

    def from_rows(array):
        return jnp.transpose(array, (1, 0, 2)).reshape(shape_here)

    target_blocks = to_rows(positions)
    seed_blocks = to_rows(adjoint_seed) * time_step
    owner_onehot = (owner_ids[:, None] == jnp.arange(group_size, dtype=jnp.int32)[None, :]).astype(
        jnp.int32
    )
    rank_within = jnp.sum((jnp.cumsum(owner_onehot, axis=0) - owner_onehot) * owner_onehot, axis=1)
    slot_index = owner_ids * capacity + rank_within
    slot_count = group_size * capacity
    pair_targets = target_blocks[target_ids]
    pair_seed = seed_blocks[target_ids]
    ident = jnp.broadcast_to(
        source_ids.astype(jnp.float32)[:, None, None], (pair_count, 1, age_here)
    )
    sent = jnp.concatenate([pair_targets, pair_seed, ident], axis=1)
    outgoing = (
        jnp.zeros((slot_count, 7, age_here), jnp.float32)
        .at[:, 6]
        .set(-1.0)
        .at[slot_index]
        .set(sent)
    )
    received = lax.all_to_all(
        outgoing.reshape(group_size, capacity, 7, age_here),
        ("turb", "age"),
        split_axis=0,
        concat_axis=0,
        tiled=True,
    ).reshape(slot_count, 7, age_here)
    asked = received[:, 6, 0].astype(jnp.int32)
    slot_payload = payload[jnp.clip(asked, 0, blocks_here - 1)]
    slot_velocity, slot_grad, payload_terms = run_pairs(
        received[:, 0:3], slot_payload, received[:, 3:6]
    )
    payload_terms = jnp.concatenate(
        [payload_terms, jnp.zeros_like(payload_terms[:, :1])], axis=1
    )
    payload_grad = onehot_sum(asked, blocks_here, payload_terms)
    answered = lax.all_to_all(
        jnp.concatenate([slot_velocity, slot_grad], axis=1).reshape(
            group_size, capacity, 6, age_here
        ),
        ("turb", "age"),
        split_axis=0,
        concat_axis=0,
        tiled=True,
    ).reshape(slot_count, 6, age_here)[slot_index]
    velocity = onehot_sum(target_ids, blocks_here, answered[:, 0:3])
    target_grad = onehot_sum(target_ids, blocks_here, answered[:, 3:6])
    advected = positions + time_step * from_rows(velocity)
    advected = advected.at[0].add(time_step)
    grad_nodes, grad_after_age, grad_after_station, grad_strengths = build_pullback(payload_grad)
    from_prior_age = shifted_2(grad_after_age, "age", 1)
    from_prior_station = shifted_2(grad_after_station, "span", 1)
    grad_positions = adjoint_seed + grad_nodes + from_rows(target_grad)
    grad_positions = grad_positions.at[..., 0].add(from_prior_age)
    grad_positions = grad_positions.at[:, :, :, 0, :].add(from_prior_station)
    return (advected, grad_positions, grad_strengths)


def solution(mesh):
    placed = (
        P(None, "turb", None, "span", "age"),
        P(None, "turb", None, "span", "age"),
        P("turb", None, "span", "age"),
        P(None, "turb", None, "span", "age"),
        P("turb", "age", "span", None),
        P("turb", "age", "span", None),
        P("turb", "age", "span", None),
    )
    return jax.shard_map(
        local,
        mesh=mesh,
        in_specs=placed,
        out_specs=(
            P(None, "turb", None, "span", "age"),
            P(None, "turb", None, "span", "age"),
            P(None, "turb", None, "span", "age"),
        ),
        check_vma=False,
    )
```

```python
import math

import jax
import jax.numpy as jnp
from jax import lax
from jax.sharding import PartitionSpec as P
from jax.experimental import pallas as pl
from jax.experimental.pallas import tpu as pltpu

REACH = 8


time_step = 0.5
four_pi = 4.0 * math.pi
batch_rows = 16


def shifted_2(value, axis, steps):
    count = lax.axis_size(axis)
    leading, last = (max(0, -steps), min(count, count - steps))
    return lax.ppermute(value, axis, [(source, source + steps) for source in range(leading, last)])


def windows(payload):
    age_count = payload.shape[-1]
    padded = jnp.pad(payload, ((0, 0), (0, 0), (REACH, REACH)))
    stacked = jnp.stack(
        [
            padded[:, :, REACH + offset : REACH + offset + age_count]
            for offset in range(-REACH, REACH)
        ]
    )
    shifted = (
        jnp.arange(-REACH, REACH, dtype=jnp.int32)[:, None]
        + jnp.arange(age_count, dtype=jnp.int32)[None, :]
    )
    inside = ((shifted >= 0) & (shifted < age_count)).astype(payload.dtype)
    return (stacked, inside)


def induced(targets, payload):
    stacked, inside = windows(payload)
    begins = stacked[:, :, 0:3]
    end_points = jnp.stack([stacked[:, :, 3:6], stacked[:, :, 6:9]])
    gammas = jnp.stack([stacked[:, :, 9], stacked[:, :, 10]]) * inside[None, :, None, :]
    core = jnp.where(inside[:, None, :] > 0, stacked[:, :, 11], 1.0)
    core_sq = core * core
    core_quad = core_sq * core_sq
    from_begin = targets[None] - begins
    from_end = targets[None, None] - end_points
    along = end_points - begins[None]
    near = from_begin[None]
    cross_x = near[..., 1, :] * from_end[..., 2, :] - near[..., 2, :] * from_end[..., 1, :]
    cross_y = near[..., 2, :] * from_end[..., 0, :] - near[..., 0, :] * from_end[..., 2, :]
    cross_z = near[..., 0, :] * from_end[..., 1, :] - near[..., 1, :] * from_end[..., 0, :]
    cross_sq = cross_x * cross_x + cross_y * cross_y + cross_z * cross_z
    length_sq = jnp.sum(along * along, axis=-2) + core_sq
    dist_begin = jnp.sqrt(jnp.sum(from_begin * from_begin, axis=-2) + core_sq)
    dist_end = jnp.sqrt(jnp.sum(from_end * from_end, axis=-2) + core_sq)
    projected = jnp.sum(
        along * (near / dist_begin[None, :, :, None, :] - from_end / dist_end[..., None, :]),
        axis=-2,
    )
    factor = (
        gammas
        * projected
        / (four_pi * jnp.sqrt(cross_sq * cross_sq + core_quad * length_sq * length_sq))
    )
    return jnp.stack(
        [
            jnp.sum(cross_x * factor, axis=(0, 1)),
            jnp.sum(cross_y * factor, axis=(0, 1)),
            jnp.sum(cross_z * factor, axis=(0, 1)),
        ],
        axis=1,
    )


GROUP_PAIRS = 8
BLOCK_PAIRS = 64


def dot3(a, b):
    return a[0] * b[0] + a[1] * b[1] + a[2] * b[2]


def cross3(a, b):
    return (
        a[1] * b[2] - a[2] * b[1],
        a[2] * b[0] - a[0] * b[2],
        a[0] * b[1] - a[1] * b[0],
    )


def segment_pair(target, begin, ends, gammas, core, inside, weight):
    core_sq = core * core
    core_quad = core_sq * core_sq
    near = [target[i] - begin[i] for i in range(3)]
    inv_begin = lax.rsqrt(dot3(near, near) + core_sq)
    velocity = [0.0, 0.0, 0.0]
    grad_target = [0.0, 0.0, 0.0]
    grad_begin = [0.0, 0.0, 0.0]
    grad_ends = []
    grad_gammas = []
    for end_point, raw_gamma in zip(ends, gammas):
        gamma = jnp.where(inside, raw_gamma, 0.0)
        far = [target[i] - end_point[i] for i in range(3)]
        along = [end_point[i] - begin[i] for i in range(3)]
        cross = cross3(near, far)
        cross_sq = dot3(cross, cross)
        length_sq = dot3(along, along) + core_sq
        inv_end = lax.rsqrt(dot3(far, far) + core_sq)
        along_near = dot3(along, near)
        along_far = dot3(along, far)
        projected = along_near * inv_begin - along_far * inv_end
        inv_den = lax.rsqrt(cross_sq * cross_sq + core_quad * length_sq * length_sq)
        base = projected * inv_den * (1.0 / four_pi)
        factor = gamma * base
        for i in range(3):
            velocity[i] = velocity[i] + cross[i] * factor
        ct_factor = dot3(cross, weight)
        grad_gammas.append(jnp.where(inside, ct_factor * base, 0.0))
        ct_proj = ct_factor * gamma * inv_den * (1.0 / four_pi)
        ct_q = -0.5 * ct_factor * factor * inv_den * inv_den
        cross_scale = 4.0 * cross_sq * ct_q
        along_scale = 4.0 * core_quad * length_sq * ct_q
        ct_cross = [factor * weight[i] + cross_scale * cross[i] for i in range(3)]
        near_scale = ct_proj * inv_begin
        far_scale = ct_proj * inv_end
        near_radial = near_scale * along_near * inv_begin * inv_begin
        far_radial = far_scale * along_far * inv_end * inv_end
        from_far = cross3(far, ct_cross)
        from_near = cross3(ct_cross, near)
        ct_along = [
            along_scale * along[i] + near_scale * near[i] - far_scale * far[i] for i in range(3)
        ]
        ct_near = [near_scale * along[i] - near_radial * near[i] + from_far[i] for i in range(3)]
        ct_far = [-far_scale * along[i] + far_radial * far[i] + from_near[i] for i in range(3)]
        for i in range(3):
            grad_target[i] = grad_target[i] + ct_near[i] + ct_far[i]
            grad_begin[i] = grad_begin[i] - ct_near[i] - ct_along[i]
        grad_ends.append([ct_along[i] - ct_far[i] for i in range(3)])
    return velocity, grad_target, grad_begin, grad_ends, grad_gammas


def pair_group(target, cotangent, rows, lane):
    age_count = lane.shape[-1]
    velocity = [0.0] * 3
    grad_target = [0.0] * 3
    grad_rows = [0.0] * 11
    for offset in range(-REACH, REACH):
        amount = offset % age_count
        moved = [pltpu.roll(r, amount, 1) if amount else r for r in target]
        weight = [pltpu.roll(r, amount, 1) if amount else r for r in cotangent]
        inside = (lane - offset >= 0) & (lane - offset < age_count)
        u, d_t, d_b, d_ends, d_gammas = segment_pair(
            moved,
            rows[0:3],
            (rows[3:6], rows[6:9]),
            (rows[9], rows[10]),
            rows[11],
            inside,
            weight,
        )
        grads = list(d_b) + list(d_ends[0]) + list(d_ends[1]) + list(d_gammas)
        back = (-offset) % age_count
        for i in range(3):
            velocity[i] = velocity[i] + (pltpu.roll(u[i], back, 1) if back else u[i])
            grad_target[i] = grad_target[i] + (pltpu.roll(d_t[i], back, 1) if back else d_t[i])
        for i in range(11):
            grad_rows[i] = grad_rows[i] + grads[i]
    return velocity, grad_target, grad_rows


def pair_kernel(t_ref, s_ref, c_ref, v_ref, gt_ref, gs_ref):
    age_count = t_ref.shape[-1]
    lane = lax.broadcasted_iota(jnp.int32, (GROUP_PAIRS, age_count), 1)

    def body(group, carry):
        at = pl.ds(pl.multiple_of(group * GROUP_PAIRS, GROUP_PAIRS), GROUP_PAIRS)
        target = [t_ref[i, at, :] for i in range(3)]
        cotangent = [c_ref[i, at, :] for i in range(3)]
        rows = [s_ref[i, at, :] for i in range(12)]
        velocity, grad_target, grad_rows = pair_group(target, cotangent, rows, lane)
        for i in range(3):
            v_ref[i, at, :] = velocity[i]
            gt_ref[i, at, :] = grad_target[i]
        for i in range(11):
            gs_ref[i, at, :] = grad_rows[i]
        return carry

    lax.fori_loop(0, t_ref.shape[1] // GROUP_PAIRS, body, 0)


def run_pairs(targets, payload, cotangent):
    number = targets.shape[0]
    age_count = targets.shape[-1]
    step = min(number, BLOCK_PAIRS)

    def spec(rows):
        return pl.BlockSpec((rows, step, age_count), lambda i: (0, i, 0))

    t_rows = jnp.transpose(targets, (1, 0, 2))
    s_rows = jnp.transpose(payload, (1, 0, 2))
    c_rows = jnp.transpose(cotangent, (1, 0, 2))
    velocity, grad_targets, grad_payload = pl.pallas_call(
        pair_kernel,
        grid=(number // step,),
        in_specs=[spec(3), spec(12), spec(3)],
        out_specs=[spec(3), spec(3), spec(11)],
        out_shape=[
            jax.ShapeDtypeStruct((3, number, age_count), jnp.float32),
            jax.ShapeDtypeStruct((3, number, age_count), jnp.float32),
            jax.ShapeDtypeStruct((11, number, age_count), jnp.float32),
        ],
    )(t_rows, s_rows, c_rows)
    return (
        jnp.transpose(velocity, (1, 0, 2)),
        jnp.transpose(grad_targets, (1, 0, 2)),
        jnp.transpose(grad_payload, (1, 0, 2)),
    )


def onehot_sum(indices, rows, values):
    selector = (jnp.arange(rows, dtype=jnp.int32)[:, None] == indices[None, :]).astype(jnp.float32)
    flat = values.reshape(values.shape[0], -1)
    summed = jnp.dot(
        selector, flat, precision=lax.Precision.HIGHEST, preferred_element_type=jnp.float32
    )
    return summed.reshape((rows,) + values.shape[1:])


def local(positions, strengths, core_radius, adjoint_seed, pair_target, pair_owner, pair_source):
    shape_here = positions.shape
    station_here = shape_here[3]
    age_here = shape_here[4]
    blocks_here = shape_here[1] * shape_here[2] * station_here
    group_size = lax.axis_size("turb") * lax.axis_size("age")
    pair_count = pair_target.shape[-1]
    capacity = 2 * pair_count // group_size
    target_ids = pair_target.reshape(pair_count)
    owner_ids = pair_owner.reshape(pair_count)
    source_ids = pair_source.reshape(pair_count)
    next_ages = shifted_2(positions[..., 0], "age", -1)
    next_stations = shifted_2(positions[:, :, :, 0, :], "span", -1)
    age_keep = (
        lax.axis_index("age") * age_here + jnp.arange(age_here, dtype=jnp.int32)
        < age_here * lax.axis_size("age") - 1
    ).astype(jnp.float32)
    station_keep = (
        lax.axis_index("span") * station_here + jnp.arange(station_here, dtype=jnp.int32)
        < station_here * lax.axis_size("span") - 1
    ).astype(jnp.float32)

    def build(nodes, after_age, after_station, circulation):
        trail_end = jnp.concatenate([nodes[..., 1:], after_age[..., None]], axis=-1)
        shed_end = jnp.concatenate([nodes[:, :, :, 1:, :], after_station[:, :, :, None, :]], axis=3)
        trail_gamma = circulation[0] * age_keep
        shed_gamma = circulation[1] * station_keep[:, None]
        stacked = jnp.concatenate(
            [nodes, trail_end, shed_end, trail_gamma[None], shed_gamma[None], core_radius[None]],
            axis=0,
        )
        return jnp.transpose(stacked.reshape(12, blocks_here, age_here), (1, 0, 2))

    payload, build_pullback = jax.vjp(build, positions, next_ages, next_stations, strengths)

    def to_rows(array):
        return jnp.transpose(array.reshape(array.shape[0], blocks_here, age_here), (1, 0, 2))

    def from_rows(array):
        return jnp.transpose(array, (1, 0, 2)).reshape(shape_here)

    target_blocks = to_rows(positions)
    seed_blocks = to_rows(adjoint_seed) * time_step
    owner_onehot = (owner_ids[:, None] == jnp.arange(group_size, dtype=jnp.int32)[None, :]).astype(
        jnp.int32
    )
    rank_within = jnp.sum((jnp.cumsum(owner_onehot, axis=0) - owner_onehot) * owner_onehot, axis=1)
    slot_index = owner_ids * capacity + rank_within
    slot_count = group_size * capacity
    pair_targets = target_blocks[target_ids]
    pair_seed = seed_blocks[target_ids]
    ident = jnp.broadcast_to(
        source_ids.astype(jnp.float32)[:, None, None], (pair_count, 1, age_here)
    )
    sent = jnp.concatenate([pair_targets, pair_seed, ident], axis=1)
    outgoing = (
        jnp.zeros((slot_count, 7, age_here), jnp.float32)
        .at[:, 6]
        .set(-1.0)
        .at[slot_index]
        .set(sent)
    )
    received = lax.all_to_all(
        outgoing.reshape(group_size, capacity, 7, age_here),
        ("turb", "age"),
        split_axis=0,
        concat_axis=0,
        tiled=True,
    ).reshape(slot_count, 7, age_here)
    asked = received[:, 6, 0].astype(jnp.int32)
    slot_payload = payload[jnp.clip(asked, 0, blocks_here - 1)]
    slot_velocity, slot_grad, payload_terms = run_pairs(
        received[:, 0:3], slot_payload, received[:, 3:6]
    )
    payload_terms = jnp.concatenate(
        [payload_terms, jnp.zeros_like(payload_terms[:, :1])], axis=1
    )
    payload_grad = onehot_sum(asked, blocks_here, payload_terms)
    answered = lax.all_to_all(
        jnp.concatenate([slot_velocity, slot_grad], axis=1).reshape(
            group_size, capacity, 6, age_here
        ),
        ("turb", "age"),
        split_axis=0,
        concat_axis=0,
        tiled=True,
    ).reshape(slot_count, 6, age_here)[slot_index]
    velocity = onehot_sum(target_ids, blocks_here, answered[:, 0:3])
    target_grad = onehot_sum(target_ids, blocks_here, answered[:, 3:6])
    advected = positions + time_step * from_rows(velocity)
    advected = advected.at[0].add(time_step)
    grad_nodes, grad_after_age, grad_after_station, grad_strengths = build_pullback(payload_grad)
    from_prior_age = shifted_2(grad_after_age, "age", 1)
    from_prior_station = shifted_2(grad_after_station, "span", 1)
    grad_positions = adjoint_seed + grad_nodes + from_rows(target_grad)
    grad_positions = grad_positions.at[..., 0].add(from_prior_age)
    grad_positions = grad_positions.at[:, :, :, 0, :].add(from_prior_station)
    return (advected, grad_positions, grad_strengths)


def solution(mesh):
    placed = (
        P(None, "turb", None, "span", "age"),
        P(None, "turb", None, "span", "age"),
        P("turb", None, "span", "age"),
        P(None, "turb", None, "span", "age"),
        P("turb", "age", "span", None),
        P("turb", "age", "span", None),
        P("turb", "age", "span", None),
    )
    return jax.shard_map(
        local,
        mesh=mesh,
        in_specs=placed,
        out_specs=(
            P(None, "turb", None, "span", "age"),
            P(None, "turb", None, "span", "age"),
            P(None, "turb", None, "span", "age"),
        ),
        check_vma=False,
    )
```

```python
import math

import jax
import jax.numpy as jnp
from jax import lax
from jax.sharding import PartitionSpec as P
from jax.experimental import pallas as pl
from jax.experimental.pallas import tpu as pltpu

REACH = 8


time_step = 0.5
four_pi = 4.0 * math.pi
batch_rows = 16


def shifted_2(value, axis, steps):
    count = lax.axis_size(axis)
    leading, last = (max(0, -steps), min(count, count - steps))
    return lax.ppermute(value, axis, [(source, source + steps) for source in range(leading, last)])


def windows(payload):
    age_count = payload.shape[-1]
    padded = jnp.pad(payload, ((0, 0), (0, 0), (REACH, REACH)))
    stacked = jnp.stack(
        [
            padded[:, :, REACH + offset : REACH + offset + age_count]
            for offset in range(-REACH, REACH)
        ]
    )
    shifted = (
        jnp.arange(-REACH, REACH, dtype=jnp.int32)[:, None]
        + jnp.arange(age_count, dtype=jnp.int32)[None, :]
    )
    inside = ((shifted >= 0) & (shifted < age_count)).astype(payload.dtype)
    return (stacked, inside)


def induced(targets, payload):
    stacked, inside = windows(payload)
    begins = stacked[:, :, 0:3]
    end_points = jnp.stack([stacked[:, :, 3:6], stacked[:, :, 6:9]])
    gammas = jnp.stack([stacked[:, :, 9], stacked[:, :, 10]]) * inside[None, :, None, :]
    core = jnp.where(inside[:, None, :] > 0, stacked[:, :, 11], 1.0)
    core_sq = core * core
    core_quad = core_sq * core_sq
    from_begin = targets[None] - begins
    from_end = targets[None, None] - end_points
    along = end_points - begins[None]
    near = from_begin[None]
    cross_x = near[..., 1, :] * from_end[..., 2, :] - near[..., 2, :] * from_end[..., 1, :]
    cross_y = near[..., 2, :] * from_end[..., 0, :] - near[..., 0, :] * from_end[..., 2, :]
    cross_z = near[..., 0, :] * from_end[..., 1, :] - near[..., 1, :] * from_end[..., 0, :]
    cross_sq = cross_x * cross_x + cross_y * cross_y + cross_z * cross_z
    length_sq = jnp.sum(along * along, axis=-2) + core_sq
    dist_begin = jnp.sqrt(jnp.sum(from_begin * from_begin, axis=-2) + core_sq)
    dist_end = jnp.sqrt(jnp.sum(from_end * from_end, axis=-2) + core_sq)
    projected = jnp.sum(
        along * (near / dist_begin[None, :, :, None, :] - from_end / dist_end[..., None, :]),
        axis=-2,
    )
    factor = (
        gammas
        * projected
        / (four_pi * jnp.sqrt(cross_sq * cross_sq + core_quad * length_sq * length_sq))
    )
    return jnp.stack(
        [
            jnp.sum(cross_x * factor, axis=(0, 1)),
            jnp.sum(cross_y * factor, axis=(0, 1)),
            jnp.sum(cross_z * factor, axis=(0, 1)),
        ],
        axis=1,
    )


GROUP_PAIRS = 8
BLOCK_PAIRS = 64


def dot3(a, b):
    return a[0] * b[0] + a[1] * b[1] + a[2] * b[2]


def cross3(a, b):
    return (
        a[1] * b[2] - a[2] * b[1],
        a[2] * b[0] - a[0] * b[2],
        a[0] * b[1] - a[1] * b[0],
    )


def segment_pair(target, begin, ends, gammas, core, inside, weight):
    core_sq = core * core
    core_quad = core_sq * core_sq
    near = [target[i] - begin[i] for i in range(3)]
    inv_begin = lax.rsqrt(dot3(near, near) + core_sq)
    velocity = [0.0, 0.0, 0.0]
    grad_target = [0.0, 0.0, 0.0]
    grad_begin = [0.0, 0.0, 0.0]
    grad_ends = []
    grad_gammas = []
    for end_point, raw_gamma in zip(ends, gammas):
        gamma = jnp.where(inside, raw_gamma, 0.0)
        far = [target[i] - end_point[i] for i in range(3)]
        along = [end_point[i] - begin[i] for i in range(3)]
        cross = cross3(near, far)
        cross_sq = dot3(cross, cross)
        length_sq = dot3(along, along) + core_sq
        inv_end = lax.rsqrt(dot3(far, far) + core_sq)
        along_near = dot3(along, near)
        along_far = dot3(along, far)
        projected = along_near * inv_begin - along_far * inv_end
        inv_den = lax.rsqrt(cross_sq * cross_sq + core_quad * length_sq * length_sq)
        base = projected * inv_den * (1.0 / four_pi)
        factor = gamma * base
        for i in range(3):
            velocity[i] = velocity[i] + cross[i] * factor
        ct_factor = dot3(cross, weight)
        grad_gammas.append(jnp.where(inside, ct_factor * base, 0.0))
        ct_proj = ct_factor * gamma * inv_den * (1.0 / four_pi)
        ct_q = -0.5 * ct_factor * factor * inv_den * inv_den
        cross_scale = 4.0 * cross_sq * ct_q
        along_scale = 4.0 * core_quad * length_sq * ct_q
        ct_cross = [factor * weight[i] + cross_scale * cross[i] for i in range(3)]
        near_scale = ct_proj * inv_begin
        far_scale = ct_proj * inv_end
        near_radial = near_scale * along_near * inv_begin * inv_begin
        far_radial = far_scale * along_far * inv_end * inv_end
        from_far = cross3(far, ct_cross)
        from_near = cross3(ct_cross, near)
        ct_along = [
            along_scale * along[i] + near_scale * near[i] - far_scale * far[i] for i in range(3)
        ]
        ct_near = [near_scale * along[i] - near_radial * near[i] + from_far[i] for i in range(3)]
        ct_far = [-far_scale * along[i] + far_radial * far[i] + from_near[i] for i in range(3)]
        for i in range(3):
            grad_target[i] = grad_target[i] + ct_near[i] + ct_far[i]
            grad_begin[i] = grad_begin[i] - ct_near[i] - ct_along[i]
        grad_ends.append([ct_along[i] - ct_far[i] for i in range(3)])
    return velocity, grad_target, grad_begin, grad_ends, grad_gammas


def pair_group(target, cotangent, rows, lane):
    age_count = lane.shape[-1]
    velocity = [0.0] * 3
    grad_target = [0.0] * 3
    grad_rows = [0.0] * 11
    for offset in range(-REACH, REACH):
        amount = offset % age_count
        moved = [pltpu.roll(r, amount, 1) if amount else r for r in target]
        weight = [pltpu.roll(r, amount, 1) if amount else r for r in cotangent]
        inside = (lane - offset >= 0) & (lane - offset < age_count)
        u, d_t, d_b, d_ends, d_gammas = segment_pair(
            moved,
            rows[0:3],
            (rows[3:6], rows[6:9]),
            (rows[9], rows[10]),
            rows[11],
            inside,
            weight,
        )
        grads = list(d_b) + list(d_ends[0]) + list(d_ends[1]) + list(d_gammas)
        back = (-offset) % age_count
        for i in range(3):
            velocity[i] = velocity[i] + (pltpu.roll(u[i], back, 1) if back else u[i])
            grad_target[i] = grad_target[i] + (pltpu.roll(d_t[i], back, 1) if back else d_t[i])
        for i in range(11):
            grad_rows[i] = grad_rows[i] + grads[i]
    return velocity, grad_target, grad_rows


def pair_kernel(t_ref, s_ref, c_ref, v_ref, gt_ref, gs_ref):
    age_count = t_ref.shape[-1]
    lane = lax.broadcasted_iota(jnp.int32, (GROUP_PAIRS, age_count), 1)

    def body(group, carry):
        at = pl.ds(pl.multiple_of(group * GROUP_PAIRS, GROUP_PAIRS), GROUP_PAIRS)
        target = [t_ref[i, at, :] for i in range(3)]
        cotangent = [c_ref[i, at, :] for i in range(3)]
        rows = [s_ref[i, at, :] for i in range(12)]
        velocity, grad_target, grad_rows = pair_group(target, cotangent, rows, lane)
        for i in range(3):
            v_ref[i, at, :] = velocity[i]
            gt_ref[i, at, :] = grad_target[i]
        for i in range(11):
            gs_ref[i, at, :] = grad_rows[i]
        return carry

    lax.fori_loop(0, t_ref.shape[1] // GROUP_PAIRS, body, 0)


def run_pairs(targets, payload, cotangent):
    number = targets.shape[0]
    age_count = targets.shape[-1]
    step = min(number, BLOCK_PAIRS)

    def spec(rows):
        return pl.BlockSpec((rows, step, age_count), lambda i: (0, i, 0))

    t_rows = jnp.transpose(targets, (1, 0, 2))
    s_rows = jnp.transpose(payload, (1, 0, 2))
    c_rows = jnp.transpose(cotangent, (1, 0, 2))
    velocity, grad_targets, grad_payload = pl.pallas_call(
        pair_kernel,
        grid=(number // step,),
        in_specs=[spec(3), spec(12), spec(3)],
        out_specs=[spec(3), spec(3), spec(11)],
        out_shape=[
            jax.ShapeDtypeStruct((3, number, age_count), jnp.float32),
            jax.ShapeDtypeStruct((3, number, age_count), jnp.float32),
            jax.ShapeDtypeStruct((11, number, age_count), jnp.float32),
        ],
    )(t_rows, s_rows, c_rows)
    return (
        jnp.transpose(velocity, (1, 0, 2)),
        jnp.transpose(grad_targets, (1, 0, 2)),
        jnp.transpose(grad_payload, (1, 0, 2)),
    )


def onehot_sum(indices, rows, values):
    selector = (jnp.arange(rows, dtype=jnp.int32)[:, None] == indices[None, :]).astype(jnp.float32)
    flat = values.reshape(values.shape[0], -1)
    summed = jnp.dot(
        selector, flat, precision=lax.Precision.HIGHEST, preferred_element_type=jnp.float32
    )
    return summed.reshape((rows,) + values.shape[1:])


def local(positions, strengths, core_radius, adjoint_seed, pair_target, pair_owner, pair_source):
    shape_here = positions.shape
    station_here = shape_here[3]
    age_here = shape_here[4]
    blocks_here = shape_here[1] * shape_here[2] * station_here
    group_size = lax.axis_size("turb") * lax.axis_size("age")
    pair_count = pair_target.shape[-1]
    capacity = 2 * pair_count // group_size
    target_ids = pair_target.reshape(pair_count)
    owner_ids = pair_owner.reshape(pair_count)
    source_ids = pair_source.reshape(pair_count)
    next_ages = shifted_2(positions[..., 0], "age", -1)
    next_stations = shifted_2(positions[:, :, :, 0, :], "span", -1)
    age_keep = (
        lax.axis_index("age") * age_here + jnp.arange(age_here, dtype=jnp.int32)
        < age_here * lax.axis_size("age") - 1
    ).astype(jnp.float32)
    station_keep = (
        lax.axis_index("span") * station_here + jnp.arange(station_here, dtype=jnp.int32)
        < station_here * lax.axis_size("span") - 1
    ).astype(jnp.float32)

    def build(nodes, after_age, after_station, circulation):
        trail_end = jnp.concatenate([nodes[..., 1:], after_age[..., None]], axis=-1)
        shed_end = jnp.concatenate([nodes[:, :, :, 1:, :], after_station[:, :, :, None, :]], axis=3)
        trail_gamma = circulation[0] * age_keep
        shed_gamma = circulation[1] * station_keep[:, None]
        stacked = jnp.concatenate(
            [nodes, trail_end, shed_end, trail_gamma[None], shed_gamma[None], core_radius[None]],
            axis=0,
        )
        return jnp.transpose(stacked.reshape(12, blocks_here, age_here), (1, 0, 2))

    payload, build_pullback = jax.vjp(build, positions, next_ages, next_stations, strengths)

    def to_rows(array):
        return jnp.transpose(array.reshape(array.shape[0], blocks_here, age_here), (1, 0, 2))

    def from_rows(array):
        return jnp.transpose(array, (1, 0, 2)).reshape(shape_here)

    target_blocks = to_rows(positions)
    seed_blocks = to_rows(adjoint_seed) * time_step
    owner_onehot = (owner_ids[:, None] == jnp.arange(group_size, dtype=jnp.int32)[None, :]).astype(
        jnp.int32
    )
    rank_within = jnp.sum((jnp.cumsum(owner_onehot, axis=0) - owner_onehot) * owner_onehot, axis=1)
    slot_index = owner_ids * capacity + rank_within
    slot_count = group_size * capacity
    pair_of_slot = (
        jnp.full((slot_count,), pair_count, jnp.int32)
        .at[slot_index]
        .set(jnp.arange(pair_count, dtype=jnp.int32))
    )
    block_of_slot = jnp.concatenate([target_ids, jnp.zeros((1,), jnp.int32)])[pair_of_slot]
    id_of_slot = jnp.concatenate(
        [source_ids.astype(jnp.float32), jnp.full((1,), -1.0, jnp.float32)]
    )[pair_of_slot]
    outgoing = jnp.concatenate(
        [
            target_blocks[block_of_slot],
            seed_blocks[block_of_slot],
            jnp.broadcast_to(id_of_slot[:, None, None], (slot_count, 1, age_here)),
        ],
        axis=1,
    )
    received = lax.all_to_all(
        outgoing.reshape(group_size, capacity, 7, age_here),
        ("turb", "age"),
        split_axis=0,
        concat_axis=0,
        tiled=True,
    ).reshape(slot_count, 7, age_here)
    asked = received[:, 6, 0].astype(jnp.int32)
    slot_payload = payload[jnp.clip(asked, 0, blocks_here - 1)]
    slot_velocity, slot_grad, payload_terms = run_pairs(
        received[:, 0:3], slot_payload, received[:, 3:6]
    )
    payload_terms = jnp.concatenate(
        [payload_terms, jnp.zeros_like(payload_terms[:, :1])], axis=1
    )
    payload_grad = onehot_sum(asked, blocks_here, payload_terms)
    answered = lax.all_to_all(
        jnp.concatenate([slot_velocity, slot_grad], axis=1).reshape(
            group_size, capacity, 6, age_here
        ),
        ("turb", "age"),
        split_axis=0,
        concat_axis=0,
        tiled=True,
    ).reshape(slot_count, 6, age_here)[slot_index]
    velocity = onehot_sum(target_ids, blocks_here, answered[:, 0:3])
    target_grad = onehot_sum(target_ids, blocks_here, answered[:, 3:6])
    advected = positions + time_step * from_rows(velocity)
    advected = advected.at[0].add(time_step)
    grad_nodes, grad_after_age, grad_after_station, grad_strengths = build_pullback(payload_grad)
    from_prior_age = shifted_2(grad_after_age, "age", 1)
    from_prior_station = shifted_2(grad_after_station, "span", 1)
    grad_positions = adjoint_seed + grad_nodes + from_rows(target_grad)
    grad_positions = grad_positions.at[..., 0].add(from_prior_age)
    grad_positions = grad_positions.at[:, :, :, 0, :].add(from_prior_station)
    return (advected, grad_positions, grad_strengths)


def solution(mesh):
    placed = (
        P(None, "turb", None, "span", "age"),
        P(None, "turb", None, "span", "age"),
        P("turb", None, "span", "age"),
        P(None, "turb", None, "span", "age"),
        P("turb", "age", "span", None),
        P("turb", "age", "span", None),
        P("turb", "age", "span", None),
    )
    return jax.shard_map(
        local,
        mesh=mesh,
        in_specs=placed,
        out_specs=(
            P(None, "turb", None, "span", "age"),
            P(None, "turb", None, "span", "age"),
            P(None, "turb", None, "span", "age"),
        ),
        check_vma=False,
    )
```

```python
import math

import jax
import jax.numpy as jnp
from jax import lax
from jax.sharding import PartitionSpec as P
from jax.experimental import pallas as pl
from jax.experimental.pallas import tpu as pltpu

REACH = 8


time_step = 0.5
four_pi = 4.0 * math.pi
batch_rows = 16


def shifted_2(value, axis, steps):
    count = lax.axis_size(axis)
    leading, last = (max(0, -steps), min(count, count - steps))
    return lax.ppermute(value, axis, [(source, source + steps) for source in range(leading, last)])


def windows(payload):
    age_count = payload.shape[-1]
    padded = jnp.pad(payload, ((0, 0), (0, 0), (REACH, REACH)))
    stacked = jnp.stack(
        [
            padded[:, :, REACH + offset : REACH + offset + age_count]
            for offset in range(-REACH, REACH)
        ]
    )
    shifted = (
        jnp.arange(-REACH, REACH, dtype=jnp.int32)[:, None]
        + jnp.arange(age_count, dtype=jnp.int32)[None, :]
    )
    inside = ((shifted >= 0) & (shifted < age_count)).astype(payload.dtype)
    return (stacked, inside)


def induced(targets, payload):
    stacked, inside = windows(payload)
    begins = stacked[:, :, 0:3]
    end_points = jnp.stack([stacked[:, :, 3:6], stacked[:, :, 6:9]])
    gammas = jnp.stack([stacked[:, :, 9], stacked[:, :, 10]]) * inside[None, :, None, :]
    core = jnp.where(inside[:, None, :] > 0, stacked[:, :, 11], 1.0)
    core_sq = core * core
    core_quad = core_sq * core_sq
    from_begin = targets[None] - begins
    from_end = targets[None, None] - end_points
    along = end_points - begins[None]
    near = from_begin[None]
    cross_x = near[..., 1, :] * from_end[..., 2, :] - near[..., 2, :] * from_end[..., 1, :]
    cross_y = near[..., 2, :] * from_end[..., 0, :] - near[..., 0, :] * from_end[..., 2, :]
    cross_z = near[..., 0, :] * from_end[..., 1, :] - near[..., 1, :] * from_end[..., 0, :]
    cross_sq = cross_x * cross_x + cross_y * cross_y + cross_z * cross_z
    length_sq = jnp.sum(along * along, axis=-2) + core_sq
    dist_begin = jnp.sqrt(jnp.sum(from_begin * from_begin, axis=-2) + core_sq)
    dist_end = jnp.sqrt(jnp.sum(from_end * from_end, axis=-2) + core_sq)
    projected = jnp.sum(
        along * (near / dist_begin[None, :, :, None, :] - from_end / dist_end[..., None, :]),
        axis=-2,
    )
    factor = (
        gammas
        * projected
        / (four_pi * jnp.sqrt(cross_sq * cross_sq + core_quad * length_sq * length_sq))
    )
    return jnp.stack(
        [
            jnp.sum(cross_x * factor, axis=(0, 1)),
            jnp.sum(cross_y * factor, axis=(0, 1)),
            jnp.sum(cross_z * factor, axis=(0, 1)),
        ],
        axis=1,
    )


GROUP_PAIRS = 8
BLOCK_PAIRS = 64


def dot3(a, b):
    return a[0] * b[0] + a[1] * b[1] + a[2] * b[2]


def cross3(a, b):
    return (
        a[1] * b[2] - a[2] * b[1],
        a[2] * b[0] - a[0] * b[2],
        a[0] * b[1] - a[1] * b[0],
    )


def segment_pair(target, begin, ends, gammas, core, inside, weight):
    core_sq = core * core
    core_quad = core_sq * core_sq
    near = [target[i] - begin[i] for i in range(3)]
    inv_begin = lax.rsqrt(dot3(near, near) + core_sq)
    velocity = [0.0, 0.0, 0.0]
    grad_target = [0.0, 0.0, 0.0]
    grad_begin = [0.0, 0.0, 0.0]
    grad_ends = []
    grad_gammas = []
    for end_point, raw_gamma in zip(ends, gammas):
        gamma = jnp.where(inside, raw_gamma, 0.0)
        far = [target[i] - end_point[i] for i in range(3)]
        along = [end_point[i] - begin[i] for i in range(3)]
        cross = cross3(near, far)
        cross_sq = dot3(cross, cross)
        length_sq = dot3(along, along) + core_sq
        inv_end = lax.rsqrt(dot3(far, far) + core_sq)
        along_near = dot3(along, near)
        along_far = dot3(along, far)
        projected = along_near * inv_begin - along_far * inv_end
        inv_den = lax.rsqrt(cross_sq * cross_sq + core_quad * length_sq * length_sq)
        base = projected * inv_den * (1.0 / four_pi)
        factor = gamma * base
        for i in range(3):
            velocity[i] = velocity[i] + cross[i] * factor
        ct_factor = dot3(cross, weight)
        grad_gammas.append(jnp.where(inside, ct_factor * base, 0.0))
        ct_proj = ct_factor * gamma * inv_den * (1.0 / four_pi)
        ct_q = -0.5 * ct_factor * factor * inv_den * inv_den
        cross_scale = 4.0 * cross_sq * ct_q
        along_scale = 4.0 * core_quad * length_sq * ct_q
        ct_cross = [factor * weight[i] + cross_scale * cross[i] for i in range(3)]
        near_scale = ct_proj * inv_begin
        far_scale = ct_proj * inv_end
        near_radial = near_scale * along_near * inv_begin * inv_begin
        far_radial = far_scale * along_far * inv_end * inv_end
        from_far = cross3(far, ct_cross)
        from_near = cross3(ct_cross, near)
        ct_along = [
            along_scale * along[i] + near_scale * near[i] - far_scale * far[i] for i in range(3)
        ]
        ct_near = [near_scale * along[i] - near_radial * near[i] + from_far[i] for i in range(3)]
        ct_far = [-far_scale * along[i] + far_radial * far[i] + from_near[i] for i in range(3)]
        for i in range(3):
            grad_target[i] = grad_target[i] + ct_near[i] + ct_far[i]
            grad_begin[i] = grad_begin[i] - ct_near[i] - ct_along[i]
        grad_ends.append([ct_along[i] - ct_far[i] for i in range(3)])
    return velocity, grad_target, grad_begin, grad_ends, grad_gammas


def pair_group(target, cotangent, rows, lane):
    age_count = lane.shape[-1]
    velocity = [0.0] * 3
    grad_target = [0.0] * 3
    grad_rows = [0.0] * 11
    for offset in range(-REACH, REACH):
        amount = offset % age_count
        moved = [pltpu.roll(r, amount, 1) if amount else r for r in target]
        weight = [pltpu.roll(r, amount, 1) if amount else r for r in cotangent]
        inside = (lane - offset >= 0) & (lane - offset < age_count)
        u, d_t, d_b, d_ends, d_gammas = segment_pair(
            moved,
            rows[0:3],
            (rows[3:6], rows[6:9]),
            (rows[9], rows[10]),
            rows[11],
            inside,
            weight,
        )
        grads = list(d_b) + list(d_ends[0]) + list(d_ends[1]) + list(d_gammas)
        back = (-offset) % age_count
        for i in range(3):
            velocity[i] = velocity[i] + (pltpu.roll(u[i], back, 1) if back else u[i])
            grad_target[i] = grad_target[i] + (pltpu.roll(d_t[i], back, 1) if back else d_t[i])
        for i in range(11):
            grad_rows[i] = grad_rows[i] + grads[i]
    return velocity, grad_target, grad_rows


def pair_kernel(t_ref, s_ref, c_ref, v_ref, gt_ref, gs_ref):
    age_count = t_ref.shape[-1]
    lane = lax.broadcasted_iota(jnp.int32, (GROUP_PAIRS, age_count), 1)

    def body(group, carry):
        at = pl.ds(pl.multiple_of(group * GROUP_PAIRS, GROUP_PAIRS), GROUP_PAIRS)
        target = [t_ref[i, at, :] for i in range(3)]
        cotangent = [c_ref[i, at, :] for i in range(3)]
        rows = [s_ref[i, at, :] for i in range(12)]
        velocity, grad_target, grad_rows = pair_group(target, cotangent, rows, lane)
        for i in range(3):
            v_ref[i, at, :] = velocity[i]
            gt_ref[i, at, :] = grad_target[i]
        for i in range(11):
            gs_ref[i, at, :] = grad_rows[i]
        return carry

    lax.fori_loop(0, t_ref.shape[1] // GROUP_PAIRS, body, 0)


def run_pairs(targets, payload, cotangent):
    number = targets.shape[0]
    age_count = targets.shape[-1]
    step = min(number, BLOCK_PAIRS)

    def spec(rows):
        return pl.BlockSpec((rows, step, age_count), lambda i: (0, i, 0))

    t_rows = jnp.transpose(targets, (1, 0, 2))
    s_rows = jnp.transpose(payload, (1, 0, 2))
    c_rows = jnp.transpose(cotangent, (1, 0, 2))
    velocity, grad_targets, grad_payload = pl.pallas_call(
        pair_kernel,
        grid=(number // step,),
        in_specs=[spec(3), spec(12), spec(3)],
        out_specs=[spec(3), spec(3), spec(11)],
        out_shape=[
            jax.ShapeDtypeStruct((3, number, age_count), jnp.float32),
            jax.ShapeDtypeStruct((3, number, age_count), jnp.float32),
            jax.ShapeDtypeStruct((11, number, age_count), jnp.float32),
        ],
    )(t_rows, s_rows, c_rows)
    return (
        jnp.transpose(velocity, (1, 0, 2)),
        jnp.transpose(grad_targets, (1, 0, 2)),
        jnp.transpose(grad_payload, (1, 0, 2)),
    )


def onehot_sum(indices, rows, values):
    selector = (jnp.arange(rows, dtype=jnp.int32)[:, None] == indices[None, :]).astype(jnp.float32)
    flat = values.reshape(values.shape[0], -1)
    summed = jnp.dot(
        selector, flat, precision=lax.Precision.HIGHEST, preferred_element_type=jnp.float32
    )
    return summed.reshape((rows,) + values.shape[1:])


def staged_all_to_all(slots):
    turb_count = lax.axis_size("turb")
    age_count = lax.axis_size("age")
    split = slots.reshape((turb_count, age_count, -1) + slots.shape[1:])
    split = lax.all_to_all(split, "age", split_axis=1, concat_axis=1, tiled=True)
    return lax.all_to_all(split, "turb", split_axis=0, concat_axis=0, tiled=True)


def local(positions, strengths, core_radius, adjoint_seed, pair_target, pair_owner, pair_source):
    shape_here = positions.shape
    station_here = shape_here[3]
    age_here = shape_here[4]
    blocks_here = shape_here[1] * shape_here[2] * station_here
    group_size = lax.axis_size("turb") * lax.axis_size("age")
    pair_count = pair_target.shape[-1]
    capacity = 2 * pair_count // group_size
    target_ids = pair_target.reshape(pair_count)
    owner_ids = pair_owner.reshape(pair_count)
    source_ids = pair_source.reshape(pair_count)
    next_ages = shifted_2(positions[..., 0], "age", -1)
    next_stations = shifted_2(positions[:, :, :, 0, :], "span", -1)
    age_keep = (
        lax.axis_index("age") * age_here + jnp.arange(age_here, dtype=jnp.int32)
        < age_here * lax.axis_size("age") - 1
    ).astype(jnp.float32)
    station_keep = (
        lax.axis_index("span") * station_here + jnp.arange(station_here, dtype=jnp.int32)
        < station_here * lax.axis_size("span") - 1
    ).astype(jnp.float32)

    def build(nodes, after_age, after_station, circulation):
        trail_end = jnp.concatenate([nodes[..., 1:], after_age[..., None]], axis=-1)
        shed_end = jnp.concatenate([nodes[:, :, :, 1:, :], after_station[:, :, :, None, :]], axis=3)
        trail_gamma = circulation[0] * age_keep
        shed_gamma = circulation[1] * station_keep[:, None]
        stacked = jnp.concatenate(
            [nodes, trail_end, shed_end, trail_gamma[None], shed_gamma[None], core_radius[None]],
            axis=0,
        )
        return jnp.transpose(stacked.reshape(12, blocks_here, age_here), (1, 0, 2))

    payload, build_pullback = jax.vjp(build, positions, next_ages, next_stations, strengths)

    def to_rows(array):
        return jnp.transpose(array.reshape(array.shape[0], blocks_here, age_here), (1, 0, 2))

    def from_rows(array):
        return jnp.transpose(array, (1, 0, 2)).reshape(shape_here)

    target_blocks = to_rows(positions)
    seed_blocks = to_rows(adjoint_seed) * time_step
    owner_onehot = (owner_ids[:, None] == jnp.arange(group_size, dtype=jnp.int32)[None, :]).astype(
        jnp.int32
    )
    rank_within = jnp.sum((jnp.cumsum(owner_onehot, axis=0) - owner_onehot) * owner_onehot, axis=1)
    slot_index = owner_ids * capacity + rank_within
    slot_count = group_size * capacity
    pair_targets = target_blocks[target_ids]
    pair_seed = seed_blocks[target_ids]
    ident = jnp.broadcast_to(
        source_ids.astype(jnp.float32)[:, None, None], (pair_count, 1, age_here)
    )
    sent = jnp.concatenate([pair_targets, pair_seed, ident], axis=1)
    outgoing = (
        jnp.zeros((slot_count, 7, age_here), jnp.float32)
        .at[:, 6]
        .set(-1.0)
        .at[slot_index]
        .set(sent)
    )
    received = staged_all_to_all(outgoing).reshape(slot_count, 7, age_here)
    asked = received[:, 6, 0].astype(jnp.int32)
    slot_payload = payload[jnp.clip(asked, 0, blocks_here - 1)]
    slot_velocity, slot_grad, payload_terms = run_pairs(
        received[:, 0:3], slot_payload, received[:, 3:6]
    )
    payload_terms = jnp.concatenate(
        [payload_terms, jnp.zeros_like(payload_terms[:, :1])], axis=1
    )
    payload_grad = onehot_sum(asked, blocks_here, payload_terms)
    answered = staged_all_to_all(
        jnp.concatenate([slot_velocity, slot_grad], axis=1)
    ).reshape(slot_count, 6, age_here)[slot_index]
    velocity = onehot_sum(target_ids, blocks_here, answered[:, 0:3])
    target_grad = onehot_sum(target_ids, blocks_here, answered[:, 3:6])
    advected = positions + time_step * from_rows(velocity)
    advected = advected.at[0].add(time_step)
    grad_nodes, grad_after_age, grad_after_station, grad_strengths = build_pullback(payload_grad)
    from_prior_age = shifted_2(grad_after_age, "age", 1)
    from_prior_station = shifted_2(grad_after_station, "span", 1)
    grad_positions = adjoint_seed + grad_nodes + from_rows(target_grad)
    grad_positions = grad_positions.at[..., 0].add(from_prior_age)
    grad_positions = grad_positions.at[:, :, :, 0, :].add(from_prior_station)
    return (advected, grad_positions, grad_strengths)


def solution(mesh):
    placed = (
        P(None, "turb", None, "span", "age"),
        P(None, "turb", None, "span", "age"),
        P("turb", None, "span", "age"),
        P(None, "turb", None, "span", "age"),
        P("turb", "age", "span", None),
        P("turb", "age", "span", None),
        P("turb", "age", "span", None),
    )
    return jax.shard_map(
        local,
        mesh=mesh,
        in_specs=placed,
        out_specs=(
            P(None, "turb", None, "span", "age"),
            P(None, "turb", None, "span", "age"),
            P(None, "turb", None, "span", "age"),
        ),
        check_vma=False,
    )
```

```python
import math

import jax
import jax.numpy as jnp
from jax import lax
from jax.sharding import PartitionSpec as P
from jax.experimental import pallas as pl
from jax.experimental.pallas import tpu as pltpu

REACH = 8


time_step = 0.5
four_pi = 4.0 * math.pi
batch_rows = 16


def shifted_2(value, axis, steps):
    count = lax.axis_size(axis)
    leading, last = (max(0, -steps), min(count, count - steps))
    return lax.ppermute(value, axis, [(source, source + steps) for source in range(leading, last)])


def windows(payload):
    age_count = payload.shape[-1]
    padded = jnp.pad(payload, ((0, 0), (0, 0), (REACH, REACH)))
    stacked = jnp.stack(
        [
            padded[:, :, REACH + offset : REACH + offset + age_count]
            for offset in range(-REACH, REACH)
        ]
    )
    shifted = (
        jnp.arange(-REACH, REACH, dtype=jnp.int32)[:, None]
        + jnp.arange(age_count, dtype=jnp.int32)[None, :]
    )
    inside = ((shifted >= 0) & (shifted < age_count)).astype(payload.dtype)
    return (stacked, inside)


def induced(targets, payload):
    stacked, inside = windows(payload)
    begins = stacked[:, :, 0:3]
    end_points = jnp.stack([stacked[:, :, 3:6], stacked[:, :, 6:9]])
    gammas = jnp.stack([stacked[:, :, 9], stacked[:, :, 10]]) * inside[None, :, None, :]
    core = jnp.where(inside[:, None, :] > 0, stacked[:, :, 11], 1.0)
    core_sq = core * core
    core_quad = core_sq * core_sq
    from_begin = targets[None] - begins
    from_end = targets[None, None] - end_points
    along = end_points - begins[None]
    near = from_begin[None]
    cross_x = near[..., 1, :] * from_end[..., 2, :] - near[..., 2, :] * from_end[..., 1, :]
    cross_y = near[..., 2, :] * from_end[..., 0, :] - near[..., 0, :] * from_end[..., 2, :]
    cross_z = near[..., 0, :] * from_end[..., 1, :] - near[..., 1, :] * from_end[..., 0, :]
    cross_sq = cross_x * cross_x + cross_y * cross_y + cross_z * cross_z
    length_sq = jnp.sum(along * along, axis=-2) + core_sq
    dist_begin = jnp.sqrt(jnp.sum(from_begin * from_begin, axis=-2) + core_sq)
    dist_end = jnp.sqrt(jnp.sum(from_end * from_end, axis=-2) + core_sq)
    projected = jnp.sum(
        along * (near / dist_begin[None, :, :, None, :] - from_end / dist_end[..., None, :]),
        axis=-2,
    )
    factor = (
        gammas
        * projected
        / (four_pi * jnp.sqrt(cross_sq * cross_sq + core_quad * length_sq * length_sq))
    )
    return jnp.stack(
        [
            jnp.sum(cross_x * factor, axis=(0, 1)),
            jnp.sum(cross_y * factor, axis=(0, 1)),
            jnp.sum(cross_z * factor, axis=(0, 1)),
        ],
        axis=1,
    )


GROUP_PAIRS = 8
BLOCK_PAIRS = 64


def dot3(a, b):
    return a[0] * b[0] + a[1] * b[1] + a[2] * b[2]


def cross3(a, b):
    return (
        a[1] * b[2] - a[2] * b[1],
        a[2] * b[0] - a[0] * b[2],
        a[0] * b[1] - a[1] * b[0],
    )


def segment_pair(target, begin, ends, gammas, core, inside, weight):
    core_sq = core * core
    core_quad = core_sq * core_sq
    near = [target[i] - begin[i] for i in range(3)]
    inv_begin = lax.rsqrt(dot3(near, near) + core_sq)
    velocity = [0.0, 0.0, 0.0]
    grad_target = [0.0, 0.0, 0.0]
    grad_begin = [0.0, 0.0, 0.0]
    grad_ends = []
    grad_gammas = []
    for end_point, raw_gamma in zip(ends, gammas):
        gamma = jnp.where(inside, raw_gamma, 0.0)
        far = [target[i] - end_point[i] for i in range(3)]
        along = [end_point[i] - begin[i] for i in range(3)]
        cross = cross3(near, far)
        cross_sq = dot3(cross, cross)
        length_sq = dot3(along, along) + core_sq
        inv_end = lax.rsqrt(dot3(far, far) + core_sq)
        along_near = dot3(along, near)
        along_far = dot3(along, far)
        projected = along_near * inv_begin - along_far * inv_end
        inv_den = lax.rsqrt(cross_sq * cross_sq + core_quad * length_sq * length_sq)
        base = projected * inv_den * (1.0 / four_pi)
        factor = gamma * base
        for i in range(3):
            velocity[i] = velocity[i] + cross[i] * factor
        ct_factor = dot3(cross, weight)
        grad_gammas.append(jnp.where(inside, ct_factor * base, 0.0))
        ct_proj = ct_factor * gamma * inv_den * (1.0 / four_pi)
        ct_q = -0.5 * ct_factor * factor * inv_den * inv_den
        cross_scale = 4.0 * cross_sq * ct_q
        along_scale = 4.0 * core_quad * length_sq * ct_q
        ct_cross = [factor * weight[i] + cross_scale * cross[i] for i in range(3)]
        near_scale = ct_proj * inv_begin
        far_scale = ct_proj * inv_end
        near_radial = near_scale * along_near * inv_begin * inv_begin
        far_radial = far_scale * along_far * inv_end * inv_end
        from_far = cross3(far, ct_cross)
        from_near = cross3(ct_cross, near)
        ct_along = [
            along_scale * along[i] + near_scale * near[i] - far_scale * far[i] for i in range(3)
        ]
        ct_near = [near_scale * along[i] - near_radial * near[i] + from_far[i] for i in range(3)]
        ct_far = [-far_scale * along[i] + far_radial * far[i] + from_near[i] for i in range(3)]
        for i in range(3):
            grad_target[i] = grad_target[i] + ct_near[i] + ct_far[i]
            grad_begin[i] = grad_begin[i] - ct_near[i] - ct_along[i]
        grad_ends.append([ct_along[i] - ct_far[i] for i in range(3)])
    return velocity, grad_target, grad_begin, grad_ends, grad_gammas


def pair_group(target, cotangent, rows, lane):
    age_count = lane.shape[-1]
    velocity = [0.0] * 3
    grad_target = [0.0] * 3
    grad_rows = [0.0] * 11
    for offset in range(-REACH, REACH):
        amount = offset % age_count
        moved = [pltpu.roll(r, amount, 1) if amount else r for r in target]
        weight = [pltpu.roll(r, amount, 1) if amount else r for r in cotangent]
        inside = (lane - offset >= 0) & (lane - offset < age_count)
        u, d_t, d_b, d_ends, d_gammas = segment_pair(
            moved,
            rows[0:3],
            (rows[3:6], rows[6:9]),
            (rows[9], rows[10]),
            rows[11],
            inside,
            weight,
        )
        grads = list(d_b) + list(d_ends[0]) + list(d_ends[1]) + list(d_gammas)
        back = (-offset) % age_count
        for i in range(3):
            velocity[i] = velocity[i] + (pltpu.roll(u[i], back, 1) if back else u[i])
            grad_target[i] = grad_target[i] + (pltpu.roll(d_t[i], back, 1) if back else d_t[i])
        for i in range(11):
            grad_rows[i] = grad_rows[i] + grads[i]
    return velocity, grad_target, grad_rows


def pair_kernel(t_ref, s_ref, v_ref, gs_ref):
    age_count = t_ref.shape[-1]
    lane = lax.broadcasted_iota(jnp.int32, (GROUP_PAIRS, age_count), 1)

    def body(group, carry):
        at = pl.ds(pl.multiple_of(group * GROUP_PAIRS, GROUP_PAIRS), GROUP_PAIRS)
        target = [t_ref[at, i, :] for i in range(3)]
        cotangent = [t_ref[at, 3 + i, :] for i in range(3)]
        rows = [s_ref[at, i, :] for i in range(12)]
        velocity, grad_target, grad_rows = pair_group(target, cotangent, rows, lane)
        for i in range(3):
            v_ref[at, i, :] = velocity[i]
            v_ref[at, 3 + i, :] = grad_target[i]
        for i in range(11):
            gs_ref[at, i, :] = grad_rows[i]
        return carry

    lax.fori_loop(0, t_ref.shape[0] // GROUP_PAIRS, body, 0)


def run_pairs(received, payload):
    number = received.shape[0]
    age_count = received.shape[-1]
    step = min(number, BLOCK_PAIRS)

    def spec(rows):
        return pl.BlockSpec((step, rows, age_count), lambda i: (i, 0, 0))

    return pl.pallas_call(
        pair_kernel,
        grid=(number // step,),
        in_specs=[spec(received.shape[1]), spec(12)],
        out_specs=[spec(6), spec(11)],
        out_shape=[
            jax.ShapeDtypeStruct((number, 6, age_count), jnp.float32),
            jax.ShapeDtypeStruct((number, 11, age_count), jnp.float32),
        ],
    )(received, payload)


def onehot_sum(indices, rows, values):
    selector = (jnp.arange(rows, dtype=jnp.int32)[:, None] == indices[None, :]).astype(jnp.float32)
    flat = values.reshape(values.shape[0], -1)
    summed = jnp.dot(
        selector, flat, precision=lax.Precision.HIGHEST, preferred_element_type=jnp.float32
    )
    return summed.reshape((rows,) + values.shape[1:])


def local(positions, strengths, core_radius, adjoint_seed, pair_target, pair_owner, pair_source):
    shape_here = positions.shape
    station_here = shape_here[3]
    age_here = shape_here[4]
    blocks_here = shape_here[1] * shape_here[2] * station_here
    group_size = lax.axis_size("turb") * lax.axis_size("age")
    pair_count = pair_target.shape[-1]
    capacity = 2 * pair_count // group_size
    target_ids = pair_target.reshape(pair_count)
    owner_ids = pair_owner.reshape(pair_count)
    source_ids = pair_source.reshape(pair_count)
    next_ages = shifted_2(positions[..., 0], "age", -1)
    next_stations = shifted_2(positions[:, :, :, 0, :], "span", -1)
    age_keep = (
        lax.axis_index("age") * age_here + jnp.arange(age_here, dtype=jnp.int32)
        < age_here * lax.axis_size("age") - 1
    ).astype(jnp.float32)
    station_keep = (
        lax.axis_index("span") * station_here + jnp.arange(station_here, dtype=jnp.int32)
        < station_here * lax.axis_size("span") - 1
    ).astype(jnp.float32)

    def build(nodes, after_age, after_station, circulation):
        trail_end = jnp.concatenate([nodes[..., 1:], after_age[..., None]], axis=-1)
        shed_end = jnp.concatenate([nodes[:, :, :, 1:, :], after_station[:, :, :, None, :]], axis=3)
        trail_gamma = circulation[0] * age_keep
        shed_gamma = circulation[1] * station_keep[:, None]
        stacked = jnp.concatenate(
            [nodes, trail_end, shed_end, trail_gamma[None], shed_gamma[None], core_radius[None]],
            axis=0,
        )
        return jnp.transpose(stacked.reshape(12, blocks_here, age_here), (1, 0, 2))

    payload, build_pullback = jax.vjp(build, positions, next_ages, next_stations, strengths)

    def to_rows(array):
        return jnp.transpose(array.reshape(array.shape[0], blocks_here, age_here), (1, 0, 2))

    def from_rows(array):
        return jnp.transpose(array, (1, 0, 2)).reshape(shape_here)

    target_blocks = to_rows(positions)
    seed_blocks = to_rows(adjoint_seed) * time_step
    owner_onehot = (owner_ids[:, None] == jnp.arange(group_size, dtype=jnp.int32)[None, :]).astype(
        jnp.int32
    )
    rank_within = jnp.sum((jnp.cumsum(owner_onehot, axis=0) - owner_onehot) * owner_onehot, axis=1)
    slot_index = owner_ids * capacity + rank_within
    slot_count = group_size * capacity
    pair_targets = target_blocks[target_ids]
    pair_seed = seed_blocks[target_ids]
    ident = jnp.broadcast_to(
        source_ids.astype(jnp.float32)[:, None, None], (pair_count, 1, age_here)
    )
    sent = jnp.concatenate([pair_targets, pair_seed, ident], axis=1)
    outgoing = (
        jnp.zeros((slot_count, 7, age_here), jnp.float32)
        .at[:, 6]
        .set(-1.0)
        .at[slot_index]
        .set(sent)
    )
    received = lax.all_to_all(
        outgoing.reshape(group_size, capacity, 7, age_here),
        ("turb", "age"),
        split_axis=0,
        concat_axis=0,
        tiled=True,
    ).reshape(slot_count, 7, age_here)
    asked = received[:, 6, 0].astype(jnp.int32)
    slot_payload = payload[jnp.clip(asked, 0, blocks_here - 1)]
    slot_answer, payload_terms = run_pairs(received, slot_payload)
    payload_terms = jnp.concatenate(
        [payload_terms, jnp.zeros_like(payload_terms[:, :1])], axis=1
    )
    payload_grad = onehot_sum(asked, blocks_here, payload_terms)
    answered = lax.all_to_all(
        slot_answer.reshape(
            group_size, capacity, 6, age_here
        ),
        ("turb", "age"),
        split_axis=0,
        concat_axis=0,
        tiled=True,
    ).reshape(slot_count, 6, age_here)[slot_index]
    velocity = onehot_sum(target_ids, blocks_here, answered[:, 0:3])
    target_grad = onehot_sum(target_ids, blocks_here, answered[:, 3:6])
    advected = positions + time_step * from_rows(velocity)
    advected = advected.at[0].add(time_step)
    grad_nodes, grad_after_age, grad_after_station, grad_strengths = build_pullback(payload_grad)
    from_prior_age = shifted_2(grad_after_age, "age", 1)
    from_prior_station = shifted_2(grad_after_station, "span", 1)
    grad_positions = adjoint_seed + grad_nodes + from_rows(target_grad)
    grad_positions = grad_positions.at[..., 0].add(from_prior_age)
    grad_positions = grad_positions.at[:, :, :, 0, :].add(from_prior_station)
    return (advected, grad_positions, grad_strengths)


def solution(mesh):
    placed = (
        P(None, "turb", None, "span", "age"),
        P(None, "turb", None, "span", "age"),
        P("turb", None, "span", "age"),
        P(None, "turb", None, "span", "age"),
        P("turb", "age", "span", None),
        P("turb", "age", "span", None),
        P("turb", "age", "span", None),
    )
    return jax.shard_map(
        local,
        mesh=mesh,
        in_specs=placed,
        out_specs=(
            P(None, "turb", None, "span", "age"),
            P(None, "turb", None, "span", "age"),
            P(None, "turb", None, "span", "age"),
        ),
        check_vma=False,
    )
```

```python
import math

import jax
import jax.numpy as jnp
from jax import lax
from jax.sharding import PartitionSpec as P
from jax.experimental import pallas as pl
from jax.experimental.pallas import tpu as pltpu

REACH = 8


time_step = 0.5
four_pi = 4.0 * math.pi
batch_rows = 16


def shifted_2(value, axis, steps):
    count = lax.axis_size(axis)
    leading, last = (max(0, -steps), min(count, count - steps))
    return lax.ppermute(value, axis, [(source, source + steps) for source in range(leading, last)])


def windows(payload):
    age_count = payload.shape[-1]
    padded = jnp.pad(payload, ((0, 0), (0, 0), (REACH, REACH)))
    stacked = jnp.stack(
        [
            padded[:, :, REACH + offset : REACH + offset + age_count]
            for offset in range(-REACH, REACH)
        ]
    )
    shifted = (
        jnp.arange(-REACH, REACH, dtype=jnp.int32)[:, None]
        + jnp.arange(age_count, dtype=jnp.int32)[None, :]
    )
    inside = ((shifted >= 0) & (shifted < age_count)).astype(payload.dtype)
    return (stacked, inside)


def induced(targets, payload):
    stacked, inside = windows(payload)
    begins = stacked[:, :, 0:3]
    end_points = jnp.stack([stacked[:, :, 3:6], stacked[:, :, 6:9]])
    gammas = jnp.stack([stacked[:, :, 9], stacked[:, :, 10]]) * inside[None, :, None, :]
    core = jnp.where(inside[:, None, :] > 0, stacked[:, :, 11], 1.0)
    core_sq = core * core
    core_quad = core_sq * core_sq
    from_begin = targets[None] - begins
    from_end = targets[None, None] - end_points
    along = end_points - begins[None]
    near = from_begin[None]
    cross_x = near[..., 1, :] * from_end[..., 2, :] - near[..., 2, :] * from_end[..., 1, :]
    cross_y = near[..., 2, :] * from_end[..., 0, :] - near[..., 0, :] * from_end[..., 2, :]
    cross_z = near[..., 0, :] * from_end[..., 1, :] - near[..., 1, :] * from_end[..., 0, :]
    cross_sq = cross_x * cross_x + cross_y * cross_y + cross_z * cross_z
    length_sq = jnp.sum(along * along, axis=-2) + core_sq
    dist_begin = jnp.sqrt(jnp.sum(from_begin * from_begin, axis=-2) + core_sq)
    dist_end = jnp.sqrt(jnp.sum(from_end * from_end, axis=-2) + core_sq)
    projected = jnp.sum(
        along * (near / dist_begin[None, :, :, None, :] - from_end / dist_end[..., None, :]),
        axis=-2,
    )
    factor = (
        gammas
        * projected
        / (four_pi * jnp.sqrt(cross_sq * cross_sq + core_quad * length_sq * length_sq))
    )
    return jnp.stack(
        [
            jnp.sum(cross_x * factor, axis=(0, 1)),
            jnp.sum(cross_y * factor, axis=(0, 1)),
            jnp.sum(cross_z * factor, axis=(0, 1)),
        ],
        axis=1,
    )


GROUP_PAIRS = 8
BLOCK_PAIRS = 64


def dot3(a, b):
    return a[0] * b[0] + a[1] * b[1] + a[2] * b[2]


def cross3(a, b):
    return (
        a[1] * b[2] - a[2] * b[1],
        a[2] * b[0] - a[0] * b[2],
        a[0] * b[1] - a[1] * b[0],
    )


def segment_pair(target, begin, ends, gammas, core, inside, weight):
    core_sq = core * core
    core_quad = core_sq * core_sq
    near = [target[i] - begin[i] for i in range(3)]
    inv_begin = lax.rsqrt(dot3(near, near) + core_sq)
    velocity = [0.0, 0.0, 0.0]
    grad_target = [0.0, 0.0, 0.0]
    grad_begin = [0.0, 0.0, 0.0]
    grad_ends = []
    grad_gammas = []
    for end_point, raw_gamma in zip(ends, gammas):
        gamma = jnp.where(inside, raw_gamma, 0.0)
        far = [target[i] - end_point[i] for i in range(3)]
        along = [end_point[i] - begin[i] for i in range(3)]
        cross = cross3(near, far)
        cross_sq = dot3(cross, cross)
        length_sq = dot3(along, along) + core_sq
        inv_end = lax.rsqrt(dot3(far, far) + core_sq)
        along_near = dot3(along, near)
        along_far = dot3(along, far)
        projected = along_near * inv_begin - along_far * inv_end
        inv_den = lax.rsqrt(cross_sq * cross_sq + core_quad * length_sq * length_sq)
        base = projected * inv_den * (1.0 / four_pi)
        factor = gamma * base
        for i in range(3):
            velocity[i] = velocity[i] + cross[i] * factor
        ct_factor = dot3(cross, weight)
        grad_gammas.append(jnp.where(inside, ct_factor * base, 0.0))
        ct_proj = ct_factor * gamma * inv_den * (1.0 / four_pi)
        ct_q = -0.5 * ct_factor * factor * inv_den * inv_den
        cross_scale = 4.0 * cross_sq * ct_q
        along_scale = 4.0 * core_quad * length_sq * ct_q
        ct_cross = [factor * weight[i] + cross_scale * cross[i] for i in range(3)]
        near_scale = ct_proj * inv_begin
        far_scale = ct_proj * inv_end
        near_radial = near_scale * along_near * inv_begin * inv_begin
        far_radial = far_scale * along_far * inv_end * inv_end
        from_far = cross3(far, ct_cross)
        from_near = cross3(ct_cross, near)
        ct_along = [
            along_scale * along[i] + near_scale * near[i] - far_scale * far[i] for i in range(3)
        ]
        ct_near = [near_scale * along[i] - near_radial * near[i] + from_far[i] for i in range(3)]
        ct_far = [-far_scale * along[i] + far_radial * far[i] + from_near[i] for i in range(3)]
        for i in range(3):
            grad_target[i] = grad_target[i] + ct_near[i] + ct_far[i]
            grad_begin[i] = grad_begin[i] - ct_near[i] - ct_along[i]
        grad_ends.append([ct_along[i] - ct_far[i] for i in range(3)])
    return velocity, grad_target, grad_begin, grad_ends, grad_gammas


def pair_group(target, cotangent, rows, lane):
    age_count = lane.shape[-1]
    velocity = [0.0] * 3
    grad_target = [0.0] * 3
    grad_rows = [0.0] * 11
    for offset in range(-REACH, REACH):
        amount = offset % age_count
        moved = [pltpu.roll(r, amount, 1) if amount else r for r in target]
        weight = [pltpu.roll(r, amount, 1) if amount else r for r in cotangent]
        inside = (lane - offset >= 0) & (lane - offset < age_count)
        u, d_t, d_b, d_ends, d_gammas = segment_pair(
            moved,
            rows[0:3],
            (rows[3:6], rows[6:9]),
            (rows[9], rows[10]),
            rows[11],
            inside,
            weight,
        )
        grads = list(d_b) + list(d_ends[0]) + list(d_ends[1]) + list(d_gammas)
        back = (-offset) % age_count
        for i in range(3):
            velocity[i] = velocity[i] + (pltpu.roll(u[i], back, 1) if back else u[i])
            grad_target[i] = grad_target[i] + (pltpu.roll(d_t[i], back, 1) if back else d_t[i])
        for i in range(11):
            grad_rows[i] = grad_rows[i] + grads[i]
    return velocity, grad_target, grad_rows


def pair_kernel(t_ref, s_ref, c_ref, v_ref, gt_ref, gs_ref):
    age_count = t_ref.shape[-1]
    lane = lax.broadcasted_iota(jnp.int32, (GROUP_PAIRS, age_count), 1)

    def body(group, carry):
        at = pl.ds(pl.multiple_of(group * GROUP_PAIRS, GROUP_PAIRS), GROUP_PAIRS)
        target = [t_ref[i, at, :] for i in range(3)]
        cotangent = [c_ref[i, at, :] for i in range(3)]
        rows = [s_ref[i, at, :] for i in range(12)]
        velocity, grad_target, grad_rows = pair_group(target, cotangent, rows, lane)
        for i in range(3):
            v_ref[i, at, :] = velocity[i]
            gt_ref[i, at, :] = grad_target[i]
        for i in range(11):
            gs_ref[i, at, :] = grad_rows[i]
        return carry

    lax.fori_loop(0, t_ref.shape[1] // GROUP_PAIRS, body, 0)


def run_pairs(targets, payload, cotangent):
    number = targets.shape[0]
    age_count = targets.shape[-1]
    step = min(number, BLOCK_PAIRS)

    def spec(rows):
        return pl.BlockSpec((rows, step, age_count), lambda i: (0, i, 0))

    t_rows = jnp.transpose(targets, (1, 0, 2))
    s_rows = jnp.transpose(payload, (1, 0, 2))
    c_rows = jnp.transpose(cotangent, (1, 0, 2))
    velocity, grad_targets, grad_payload = pl.pallas_call(
        pair_kernel,
        grid=(number // step,),
        in_specs=[spec(3), spec(12), spec(3)],
        out_specs=[spec(3), spec(3), spec(11)],
        out_shape=[
            jax.ShapeDtypeStruct((3, number, age_count), jnp.float32),
            jax.ShapeDtypeStruct((3, number, age_count), jnp.float32),
            jax.ShapeDtypeStruct((11, number, age_count), jnp.float32),
        ],
    )(t_rows, s_rows, c_rows)
    return (
        jnp.transpose(velocity, (1, 0, 2)),
        jnp.transpose(grad_targets, (1, 0, 2)),
        jnp.transpose(grad_payload, (1, 0, 2)),
    )


def onehot_sum(indices, rows, values):
    selector = (jnp.arange(rows, dtype=jnp.int32)[:, None] == indices[None, :]).astype(jnp.float32)
    flat = values.reshape(values.shape[0], -1)
    summed = jnp.dot(
        selector, flat, precision=lax.Precision.HIGHEST, preferred_element_type=jnp.float32
    )
    return summed.reshape((rows,) + values.shape[1:])


def local(positions, strengths, core_radius, adjoint_seed, pair_target, pair_owner, pair_source):
    shape_here = positions.shape
    station_here = shape_here[3]
    age_here = shape_here[4]
    blocks_here = shape_here[1] * shape_here[2] * station_here
    group_size = lax.axis_size("turb") * lax.axis_size("age")
    pair_count = pair_target.shape[-1]
    capacity = 2 * pair_count // group_size
    target_ids = pair_target.reshape(pair_count)
    owner_ids = pair_owner.reshape(pair_count)
    source_ids = pair_source.reshape(pair_count)
    next_ages = shifted_2(positions[..., 0], "age", -1)
    next_stations = shifted_2(positions[:, :, :, 0, :], "span", -1)
    age_keep = (
        lax.axis_index("age") * age_here + jnp.arange(age_here, dtype=jnp.int32)
        < age_here * lax.axis_size("age") - 1
    ).astype(jnp.float32)
    station_keep = (
        lax.axis_index("span") * station_here + jnp.arange(station_here, dtype=jnp.int32)
        < station_here * lax.axis_size("span") - 1
    ).astype(jnp.float32)

    def build(nodes, after_age, after_station, circulation):
        trail_end = jnp.concatenate([nodes[..., 1:], after_age[..., None]], axis=-1)
        shed_end = jnp.concatenate([nodes[:, :, :, 1:, :], after_station[:, :, :, None, :]], axis=3)
        trail_gamma = circulation[0] * age_keep
        shed_gamma = circulation[1] * station_keep[:, None]
        stacked = jnp.concatenate(
            [nodes, trail_end, shed_end, trail_gamma[None], shed_gamma[None], core_radius[None]],
            axis=0,
        )
        return jnp.transpose(stacked.reshape(12, blocks_here, age_here), (1, 0, 2))

    payload, build_pullback = jax.vjp(build, positions, next_ages, next_stations, strengths)

    def to_rows(array):
        return jnp.transpose(array.reshape(array.shape[0], blocks_here, age_here), (1, 0, 2))

    def from_rows(array):
        return jnp.transpose(array, (1, 0, 2)).reshape(shape_here)

    target_blocks = to_rows(positions)
    seed_blocks = to_rows(adjoint_seed) * time_step
    owner_onehot = (owner_ids[:, None] == jnp.arange(group_size, dtype=jnp.int32)[None, :]).astype(
        jnp.int32
    )
    rank_within = jnp.sum((jnp.cumsum(owner_onehot, axis=0) - owner_onehot) * owner_onehot, axis=1)
    slot_index = owner_ids * capacity + rank_within
    slot_count = group_size * capacity
    slot_pick = (
        jnp.arange(slot_count, dtype=jnp.int32)[:, None] == slot_index[None, :]
    ).astype(jnp.float32)
    block_pick = (
        target_ids[:, None] == jnp.arange(blocks_here, dtype=jnp.int32)[None, :]
    ).astype(jnp.float32)
    slot_block = jnp.dot(slot_pick, block_pick, preferred_element_type=jnp.float32)
    blocks_sent = jnp.concatenate([target_blocks, seed_blocks], axis=1)
    rows_sent = jnp.dot(
        slot_block,
        blocks_sent.reshape(blocks_here, -1),
        precision=lax.Precision.HIGHEST,
        preferred_element_type=jnp.float32,
    ).reshape(slot_count, 6, age_here)
    ident = jnp.dot(
        slot_pick,
        (source_ids + 1).astype(jnp.float32),
        precision=lax.Precision.HIGHEST,
        preferred_element_type=jnp.float32,
    )
    outgoing = jnp.concatenate(
        [rows_sent, jnp.broadcast_to(ident[:, None, None], (slot_count, 1, age_here))],
        axis=1,
    )
    received = lax.all_to_all(
        outgoing.reshape(group_size, capacity, 7, age_here),
        ("turb", "age"),
        split_axis=0,
        concat_axis=0,
        tiled=True,
    ).reshape(slot_count, 7, age_here)
    asked = received[:, 6, 0].astype(jnp.int32) - 1
    slot_payload = payload[jnp.clip(asked, 0, blocks_here - 1)]
    slot_velocity, slot_grad, payload_terms = run_pairs(
        received[:, 0:3], slot_payload, received[:, 3:6]
    )
    payload_terms = jnp.concatenate(
        [payload_terms, jnp.zeros_like(payload_terms[:, :1])], axis=1
    )
    payload_grad = onehot_sum(asked, blocks_here, payload_terms)
    answered = lax.all_to_all(
        jnp.concatenate([slot_velocity, slot_grad], axis=1).reshape(
            group_size, capacity, 6, age_here
        ),
        ("turb", "age"),
        split_axis=0,
        concat_axis=0,
        tiled=True,
    ).reshape(slot_count, 6, age_here)[slot_index]
    velocity = onehot_sum(target_ids, blocks_here, answered[:, 0:3])
    target_grad = onehot_sum(target_ids, blocks_here, answered[:, 3:6])
    advected = positions + time_step * from_rows(velocity)
    advected = advected.at[0].add(time_step)
    grad_nodes, grad_after_age, grad_after_station, grad_strengths = build_pullback(payload_grad)
    from_prior_age = shifted_2(grad_after_age, "age", 1)
    from_prior_station = shifted_2(grad_after_station, "span", 1)
    grad_positions = adjoint_seed + grad_nodes + from_rows(target_grad)
    grad_positions = grad_positions.at[..., 0].add(from_prior_age)
    grad_positions = grad_positions.at[:, :, :, 0, :].add(from_prior_station)
    return (advected, grad_positions, grad_strengths)


def solution(mesh):
    placed = (
        P(None, "turb", None, "span", "age"),
        P(None, "turb", None, "span", "age"),
        P("turb", None, "span", "age"),
        P(None, "turb", None, "span", "age"),
        P("turb", "age", "span", None),
        P("turb", "age", "span", None),
        P("turb", "age", "span", None),
    )
    return jax.shard_map(
        local,
        mesh=mesh,
        in_specs=placed,
        out_specs=(
            P(None, "turb", None, "span", "age"),
            P(None, "turb", None, "span", "age"),
            P(None, "turb", None, "span", "age"),
        ),
        check_vma=False,
    )
```

```python
import math

import jax
import jax.numpy as jnp
from jax import lax
from jax.sharding import PartitionSpec as P
from jax.experimental import pallas as pl
from jax.experimental.pallas import tpu as pltpu

REACH = 8


time_step = 0.5
four_pi = 4.0 * math.pi
batch_rows = 16


def shifted_2(value, axis, steps):
    count = lax.axis_size(axis)
    leading, last = (max(0, -steps), min(count, count - steps))
    return lax.ppermute(value, axis, [(source, source + steps) for source in range(leading, last)])


def windows(payload):
    age_count = payload.shape[-1]
    padded = jnp.pad(payload, ((0, 0), (0, 0), (REACH, REACH)))
    stacked = jnp.stack(
        [
            padded[:, :, REACH + offset : REACH + offset + age_count]
            for offset in range(-REACH, REACH)
        ]
    )
    shifted = (
        jnp.arange(-REACH, REACH, dtype=jnp.int32)[:, None]
        + jnp.arange(age_count, dtype=jnp.int32)[None, :]
    )
    inside = ((shifted >= 0) & (shifted < age_count)).astype(payload.dtype)
    return (stacked, inside)


def induced(targets, payload):
    stacked, inside = windows(payload)
    begins = stacked[:, :, 0:3]
    end_points = jnp.stack([stacked[:, :, 3:6], stacked[:, :, 6:9]])
    gammas = jnp.stack([stacked[:, :, 9], stacked[:, :, 10]]) * inside[None, :, None, :]
    core = jnp.where(inside[:, None, :] > 0, stacked[:, :, 11], 1.0)
    core_sq = core * core
    core_quad = core_sq * core_sq
    from_begin = targets[None] - begins
    from_end = targets[None, None] - end_points
    along = end_points - begins[None]
    near = from_begin[None]
    cross_x = near[..., 1, :] * from_end[..., 2, :] - near[..., 2, :] * from_end[..., 1, :]
    cross_y = near[..., 2, :] * from_end[..., 0, :] - near[..., 0, :] * from_end[..., 2, :]
    cross_z = near[..., 0, :] * from_end[..., 1, :] - near[..., 1, :] * from_end[..., 0, :]
    cross_sq = cross_x * cross_x + cross_y * cross_y + cross_z * cross_z
    length_sq = jnp.sum(along * along, axis=-2) + core_sq
    dist_begin = jnp.sqrt(jnp.sum(from_begin * from_begin, axis=-2) + core_sq)
    dist_end = jnp.sqrt(jnp.sum(from_end * from_end, axis=-2) + core_sq)
    projected = jnp.sum(
        along * (near / dist_begin[None, :, :, None, :] - from_end / dist_end[..., None, :]),
        axis=-2,
    )
    factor = (
        gammas
        * projected
        / (four_pi * jnp.sqrt(cross_sq * cross_sq + core_quad * length_sq * length_sq))
    )
    return jnp.stack(
        [
            jnp.sum(cross_x * factor, axis=(0, 1)),
            jnp.sum(cross_y * factor, axis=(0, 1)),
            jnp.sum(cross_z * factor, axis=(0, 1)),
        ],
        axis=1,
    )


GROUP_PAIRS = 8
BLOCK_PAIRS = 64


def dot3(a, b):
    return a[0] * b[0] + a[1] * b[1] + a[2] * b[2]


def cross3(a, b):
    return (
        a[1] * b[2] - a[2] * b[1],
        a[2] * b[0] - a[0] * b[2],
        a[0] * b[1] - a[1] * b[0],
    )


def segment_pair(target, begin, ends, gammas, core, inside, weight):
    core_sq = core * core
    core_quad = core_sq * core_sq
    near = [target[i] - begin[i] for i in range(3)]
    inv_begin = lax.rsqrt(dot3(near, near) + core_sq)
    velocity = [0.0, 0.0, 0.0]
    grad_target = [0.0, 0.0, 0.0]
    grad_begin = [0.0, 0.0, 0.0]
    grad_ends = []
    grad_gammas = []
    for end_point, raw_gamma in zip(ends, gammas):
        gamma = jnp.where(inside, raw_gamma, 0.0)
        far = [target[i] - end_point[i] for i in range(3)]
        along = [end_point[i] - begin[i] for i in range(3)]
        cross = cross3(near, far)
        cross_sq = dot3(cross, cross)
        length_sq = dot3(along, along) + core_sq
        inv_end = lax.rsqrt(dot3(far, far) + core_sq)
        along_near = dot3(along, near)
        along_far = dot3(along, far)
        projected = along_near * inv_begin - along_far * inv_end
        inv_den = lax.rsqrt(cross_sq * cross_sq + core_quad * length_sq * length_sq)
        base = projected * inv_den * (1.0 / four_pi)
        factor = gamma * base
        for i in range(3):
            velocity[i] = velocity[i] + cross[i] * factor
        ct_factor = dot3(cross, weight)
        grad_gammas.append(jnp.where(inside, ct_factor * base, 0.0))
        ct_proj = ct_factor * gamma * inv_den * (1.0 / four_pi)
        ct_q = -0.5 * ct_factor * factor * inv_den * inv_den
        cross_scale = 4.0 * cross_sq * ct_q
        along_scale = 4.0 * core_quad * length_sq * ct_q
        ct_cross = [factor * weight[i] + cross_scale * cross[i] for i in range(3)]
        near_scale = ct_proj * inv_begin
        far_scale = ct_proj * inv_end
        near_radial = near_scale * along_near * inv_begin * inv_begin
        far_radial = far_scale * along_far * inv_end * inv_end
        from_far = cross3(far, ct_cross)
        from_near = cross3(ct_cross, near)
        ct_along = [
            along_scale * along[i] + near_scale * near[i] - far_scale * far[i] for i in range(3)
        ]
        ct_near = [near_scale * along[i] - near_radial * near[i] + from_far[i] for i in range(3)]
        ct_far = [-far_scale * along[i] + far_radial * far[i] + from_near[i] for i in range(3)]
        for i in range(3):
            grad_target[i] = grad_target[i] + ct_near[i] + ct_far[i]
            grad_begin[i] = grad_begin[i] - ct_near[i] - ct_along[i]
        grad_ends.append([ct_along[i] - ct_far[i] for i in range(3)])
    return velocity, grad_target, grad_begin, grad_ends, grad_gammas


def pair_group(target, cotangent, rows, lane):
    age_count = lane.shape[-1]
    velocity = [0.0] * 3
    grad_target = [0.0] * 3
    grad_rows = [0.0] * 11
    for offset in range(-REACH, REACH):
        amount = offset % age_count
        moved = [pltpu.roll(r, amount, 1) if amount else r for r in target]
        weight = [pltpu.roll(r, amount, 1) if amount else r for r in cotangent]
        inside = (lane - offset >= 0) & (lane - offset < age_count)
        u, d_t, d_b, d_ends, d_gammas = segment_pair(
            moved,
            rows[0:3],
            (rows[3:6], rows[6:9]),
            (rows[9], rows[10]),
            rows[11],
            inside,
            weight,
        )
        grads = list(d_b) + list(d_ends[0]) + list(d_ends[1]) + list(d_gammas)
        back = (-offset) % age_count
        for i in range(3):
            velocity[i] = velocity[i] + (pltpu.roll(u[i], back, 1) if back else u[i])
            grad_target[i] = grad_target[i] + (pltpu.roll(d_t[i], back, 1) if back else d_t[i])
        for i in range(11):
            grad_rows[i] = grad_rows[i] + grads[i]
    return velocity, grad_target, grad_rows


def pair_kernel(t_ref, s_ref, c_ref, v_ref, gt_ref, gs_ref):
    age_count = t_ref.shape[-1]
    lane = lax.broadcasted_iota(jnp.int32, (GROUP_PAIRS, age_count), 1)

    def body(group, carry):
        at = pl.ds(pl.multiple_of(group * GROUP_PAIRS, GROUP_PAIRS), GROUP_PAIRS)
        target = [t_ref[i, at, :] for i in range(3)]
        cotangent = [c_ref[i, at, :] for i in range(3)]
        rows = [s_ref[i, at, :] for i in range(12)]
        velocity, grad_target, grad_rows = pair_group(target, cotangent, rows, lane)
        for i in range(3):
            v_ref[i, at, :] = velocity[i]
            gt_ref[i, at, :] = grad_target[i]
        for i in range(11):
            gs_ref[i, at, :] = grad_rows[i]
        return carry

    lax.fori_loop(0, t_ref.shape[1] // GROUP_PAIRS, body, 0)


def run_pairs(targets, payload, cotangent):
    number = targets.shape[0]
    age_count = targets.shape[-1]
    step = min(number, BLOCK_PAIRS)

    def spec(rows):
        return pl.BlockSpec((rows, step, age_count), lambda i: (0, i, 0))

    t_rows = jnp.transpose(targets, (1, 0, 2))
    s_rows = jnp.transpose(payload, (1, 0, 2))
    c_rows = jnp.transpose(cotangent, (1, 0, 2))
    velocity, grad_targets, grad_payload = pl.pallas_call(
        pair_kernel,
        grid=(number // step,),
        in_specs=[spec(3), spec(12), spec(3)],
        out_specs=[spec(3), spec(3), spec(11)],
        out_shape=[
            jax.ShapeDtypeStruct((3, number, age_count), jnp.float32),
            jax.ShapeDtypeStruct((3, number, age_count), jnp.float32),
            jax.ShapeDtypeStruct((11, number, age_count), jnp.float32),
        ],
    )(t_rows, s_rows, c_rows)
    return (
        jnp.transpose(velocity, (1, 0, 2)),
        jnp.transpose(grad_targets, (1, 0, 2)),
        jnp.transpose(grad_payload, (1, 0, 2)),
    )


def onehot_sum(indices, rows, values):
    selector = (jnp.arange(rows, dtype=jnp.int32)[:, None] == indices[None, :]).astype(jnp.float32)
    flat = values.reshape(values.shape[0], -1)
    summed = jnp.dot(
        selector, flat, precision=lax.Precision.HIGHEST, preferred_element_type=jnp.float32
    )
    return summed.reshape((rows,) + values.shape[1:])


def local(positions, strengths, core_radius, adjoint_seed, pair_target, pair_owner, pair_source):
    shape_here = positions.shape
    station_here = shape_here[3]
    age_here = shape_here[4]
    blocks_here = shape_here[1] * shape_here[2] * station_here
    group_size = lax.axis_size("turb") * lax.axis_size("age")
    pair_count = pair_target.shape[-1]
    capacity = 2 * pair_count // group_size
    target_ids = pair_target.reshape(pair_count)
    owner_ids = pair_owner.reshape(pair_count)
    source_ids = pair_source.reshape(pair_count)
    next_ages = shifted_2(positions[..., 0], "age", -1)
    next_stations = shifted_2(positions[:, :, :, 0, :], "span", -1)
    age_keep = (
        lax.axis_index("age") * age_here + jnp.arange(age_here, dtype=jnp.int32)
        < age_here * lax.axis_size("age") - 1
    ).astype(jnp.float32)
    station_keep = (
        lax.axis_index("span") * station_here + jnp.arange(station_here, dtype=jnp.int32)
        < station_here * lax.axis_size("span") - 1
    ).astype(jnp.float32)

    def build(nodes, after_age, after_station, circulation):
        trail_end = jnp.concatenate([nodes[..., 1:], after_age[..., None]], axis=-1)
        shed_end = jnp.concatenate([nodes[:, :, :, 1:, :], after_station[:, :, :, None, :]], axis=3)
        trail_gamma = circulation[0] * age_keep
        shed_gamma = circulation[1] * station_keep[:, None]
        stacked = jnp.concatenate(
            [nodes, trail_end, shed_end, trail_gamma[None], shed_gamma[None], core_radius[None]],
            axis=0,
        )
        return jnp.transpose(stacked.reshape(12, blocks_here, age_here), (1, 0, 2))

    payload, build_pullback = jax.vjp(build, positions, next_ages, next_stations, strengths)

    def to_rows(array):
        return jnp.transpose(array.reshape(array.shape[0], blocks_here, age_here), (1, 0, 2))

    def from_rows(array):
        return jnp.transpose(array, (1, 0, 2)).reshape(shape_here)

    target_blocks = to_rows(positions)
    seed_blocks = to_rows(adjoint_seed)
    earlier = (
        jnp.arange(pair_count, dtype=jnp.int32)[:, None]
        > jnp.arange(pair_count, dtype=jnp.int32)[None, :]
    )
    rank_within = jnp.sum(
        ((owner_ids[:, None] == owner_ids[None, :]) & earlier).astype(jnp.int32), axis=1
    )
    slot_index = owner_ids * capacity + rank_within
    slot_count = group_size * capacity
    slot_pick = (
        jnp.arange(slot_count, dtype=jnp.int32)[:, None] == slot_index[None, :]
    ).astype(jnp.float32)
    block_pick = (
        target_ids[:, None] == jnp.arange(blocks_here, dtype=jnp.int32)[None, :]
    ).astype(jnp.float32)
    slot_block = jnp.dot(slot_pick, block_pick, preferred_element_type=jnp.float32)
    blocks_sent = jnp.concatenate([target_blocks, seed_blocks], axis=1)
    rows_sent = jnp.dot(
        slot_block,
        blocks_sent.reshape(blocks_here, -1),
        precision=lax.Precision.HIGHEST,
        preferred_element_type=jnp.float32,
    ).reshape(slot_count, 6, age_here)
    ident = jnp.dot(
        slot_pick,
        (source_ids + 1).astype(jnp.float32),
        precision=lax.Precision.HIGHEST,
        preferred_element_type=jnp.float32,
    )
    outgoing = jnp.concatenate(
        [rows_sent, jnp.broadcast_to(ident[:, None, None], (slot_count, 1, age_here))],
        axis=1,
    )
    received = lax.all_to_all(
        outgoing.reshape(group_size, capacity, 7, age_here),
        ("turb", "age"),
        split_axis=0,
        concat_axis=0,
        tiled=True,
    ).reshape(slot_count, 7, age_here)
    asked = received[:, 6, 0].astype(jnp.int32) - 1
    slot_payload = payload[jnp.clip(asked, 0, blocks_here - 1)]
    slot_velocity, slot_grad, payload_terms = run_pairs(
        received[:, 0:3], slot_payload, received[:, 3:6] * time_step
    )
    payload_terms = jnp.concatenate(
        [payload_terms, jnp.zeros_like(payload_terms[:, :1])], axis=1
    )
    payload_grad = onehot_sum(asked, blocks_here, payload_terms)
    answered = lax.all_to_all(
        jnp.concatenate([slot_velocity, slot_grad], axis=1).reshape(
            group_size, capacity, 6, age_here
        ),
        ("turb", "age"),
        split_axis=0,
        concat_axis=0,
        tiled=True,
    ).reshape(slot_count, 6, age_here)[slot_index]
    velocity = onehot_sum(target_ids, blocks_here, answered[:, 0:3])
    target_grad = onehot_sum(target_ids, blocks_here, answered[:, 3:6])
    advected = positions + time_step * from_rows(velocity)
    advected = advected.at[0].add(time_step)
    grad_nodes, grad_after_age, grad_after_station, grad_strengths = build_pullback(payload_grad)
    from_prior_age = shifted_2(grad_after_age, "age", 1)
    from_prior_station = shifted_2(grad_after_station, "span", 1)
    grad_positions = adjoint_seed + grad_nodes + from_rows(target_grad)
    grad_positions = grad_positions.at[..., 0].add(from_prior_age)
    grad_positions = grad_positions.at[:, :, :, 0, :].add(from_prior_station)
    return (advected, grad_positions, grad_strengths)


def solution(mesh):
    placed = (
        P(None, "turb", None, "span", "age"),
        P(None, "turb", None, "span", "age"),
        P("turb", None, "span", "age"),
        P(None, "turb", None, "span", "age"),
        P("turb", "age", "span", None),
        P("turb", "age", "span", None),
        P("turb", "age", "span", None),
    )
    return jax.shard_map(
        local,
        mesh=mesh,
        in_specs=placed,
        out_specs=(
            P(None, "turb", None, "span", "age"),
            P(None, "turb", None, "span", "age"),
            P(None, "turb", None, "span", "age"),
        ),
        check_vma=False,
    )
```

```python
import math

import jax
import jax.numpy as jnp
from jax import lax
from jax.sharding import PartitionSpec as P
from jax.experimental import pallas as pl
from jax.experimental.pallas import tpu as pltpu

REACH = 8


time_step = 0.5
four_pi = 4.0 * math.pi
batch_rows = 16


def shifted_2(value, axis, steps):
    count = lax.axis_size(axis)
    leading, last = (max(0, -steps), min(count, count - steps))
    return lax.ppermute(value, axis, [(source, source + steps) for source in range(leading, last)])


def windows(payload):
    age_count = payload.shape[-1]
    padded = jnp.pad(payload, ((0, 0), (0, 0), (REACH, REACH)))
    stacked = jnp.stack(
        [
            padded[:, :, REACH + offset : REACH + offset + age_count]
            for offset in range(-REACH, REACH)
        ]
    )
    shifted = (
        jnp.arange(-REACH, REACH, dtype=jnp.int32)[:, None]
        + jnp.arange(age_count, dtype=jnp.int32)[None, :]
    )
    inside = ((shifted >= 0) & (shifted < age_count)).astype(payload.dtype)
    return (stacked, inside)


def induced(targets, payload):
    stacked, inside = windows(payload)
    begins = stacked[:, :, 0:3]
    end_points = jnp.stack([stacked[:, :, 3:6], stacked[:, :, 6:9]])
    gammas = jnp.stack([stacked[:, :, 9], stacked[:, :, 10]]) * inside[None, :, None, :]
    core = jnp.where(inside[:, None, :] > 0, stacked[:, :, 11], 1.0)
    core_sq = core * core
    core_quad = core_sq * core_sq
    from_begin = targets[None] - begins
    from_end = targets[None, None] - end_points
    along = end_points - begins[None]
    near = from_begin[None]
    cross_x = near[..., 1, :] * from_end[..., 2, :] - near[..., 2, :] * from_end[..., 1, :]
    cross_y = near[..., 2, :] * from_end[..., 0, :] - near[..., 0, :] * from_end[..., 2, :]
    cross_z = near[..., 0, :] * from_end[..., 1, :] - near[..., 1, :] * from_end[..., 0, :]
    cross_sq = cross_x * cross_x + cross_y * cross_y + cross_z * cross_z
    length_sq = jnp.sum(along * along, axis=-2) + core_sq
    dist_begin = jnp.sqrt(jnp.sum(from_begin * from_begin, axis=-2) + core_sq)
    dist_end = jnp.sqrt(jnp.sum(from_end * from_end, axis=-2) + core_sq)
    projected = jnp.sum(
        along * (near / dist_begin[None, :, :, None, :] - from_end / dist_end[..., None, :]),
        axis=-2,
    )
    factor = (
        gammas
        * projected
        / (four_pi * jnp.sqrt(cross_sq * cross_sq + core_quad * length_sq * length_sq))
    )
    return jnp.stack(
        [
            jnp.sum(cross_x * factor, axis=(0, 1)),
            jnp.sum(cross_y * factor, axis=(0, 1)),
            jnp.sum(cross_z * factor, axis=(0, 1)),
        ],
        axis=1,
    )


GROUP_PAIRS = 8
BLOCK_PAIRS = 64


def dot3(a, b):
    return a[0] * b[0] + a[1] * b[1] + a[2] * b[2]


def cross3(a, b):
    return (
        a[1] * b[2] - a[2] * b[1],
        a[2] * b[0] - a[0] * b[2],
        a[0] * b[1] - a[1] * b[0],
    )


def segment_pair(target, begin, ends, gammas, core, inside, weight):
    core_sq = core * core
    core_quad = core_sq * core_sq
    near = [target[i] - begin[i] for i in range(3)]
    inv_begin = lax.rsqrt(dot3(near, near) + core_sq)
    velocity = [0.0, 0.0, 0.0]
    grad_target = [0.0, 0.0, 0.0]
    grad_begin = [0.0, 0.0, 0.0]
    grad_ends = []
    grad_gammas = []
    for end_point, raw_gamma in zip(ends, gammas):
        gamma = jnp.where(inside, raw_gamma, 0.0)
        far = [target[i] - end_point[i] for i in range(3)]
        along = [end_point[i] - begin[i] for i in range(3)]
        cross = cross3(near, far)
        cross_sq = dot3(cross, cross)
        length_sq = dot3(along, along) + core_sq
        inv_end = lax.rsqrt(dot3(far, far) + core_sq)
        along_near = dot3(along, near)
        along_far = dot3(along, far)
        projected = along_near * inv_begin - along_far * inv_end
        inv_den = lax.rsqrt(cross_sq * cross_sq + core_quad * length_sq * length_sq)
        base = projected * inv_den * (1.0 / four_pi)
        factor = gamma * base
        for i in range(3):
            velocity[i] = velocity[i] + cross[i] * factor
        ct_factor = dot3(cross, weight)
        grad_gammas.append(jnp.where(inside, ct_factor * base, 0.0))
        ct_proj = ct_factor * gamma * inv_den * (1.0 / four_pi)
        ct_q = -0.5 * ct_factor * factor * inv_den * inv_den
        cross_scale = 4.0 * cross_sq * ct_q
        along_scale = 4.0 * core_quad * length_sq * ct_q
        ct_cross = [factor * weight[i] + cross_scale * cross[i] for i in range(3)]
        near_scale = ct_proj * inv_begin
        far_scale = ct_proj * inv_end
        near_radial = near_scale * along_near * inv_begin * inv_begin
        far_radial = far_scale * along_far * inv_end * inv_end
        from_far = cross3(far, ct_cross)
        from_near = cross3(ct_cross, near)
        ct_along = [
            along_scale * along[i] + near_scale * near[i] - far_scale * far[i] for i in range(3)
        ]
        ct_near = [near_scale * along[i] - near_radial * near[i] + from_far[i] for i in range(3)]
        ct_far = [-far_scale * along[i] + far_radial * far[i] + from_near[i] for i in range(3)]
        for i in range(3):
            grad_target[i] = grad_target[i] + ct_near[i] + ct_far[i]
            grad_begin[i] = grad_begin[i] - ct_near[i] - ct_along[i]
        grad_ends.append([ct_along[i] - ct_far[i] for i in range(3)])
    return velocity, grad_target, grad_begin, grad_ends, grad_gammas


def pair_group(target, cotangent, rows, lane):
    age_count = lane.shape[-1]
    velocity = [0.0] * 3
    grad_target = [0.0] * 3
    grad_rows = [0.0] * 11
    for offset in range(-REACH, REACH):
        amount = offset % age_count
        moved = [pltpu.roll(r, amount, 1) if amount else r for r in target]
        weight = [pltpu.roll(r, amount, 1) if amount else r for r in cotangent]
        inside = (lane - offset >= 0) & (lane - offset < age_count)
        u, d_t, d_b, d_ends, d_gammas = segment_pair(
            moved,
            rows[0:3],
            (rows[3:6], rows[6:9]),
            (rows[9], rows[10]),
            rows[11],
            inside,
            weight,
        )
        grads = list(d_b) + list(d_ends[0]) + list(d_ends[1]) + list(d_gammas)
        back = (-offset) % age_count
        for i in range(3):
            velocity[i] = velocity[i] + (pltpu.roll(u[i], back, 1) if back else u[i])
            grad_target[i] = grad_target[i] + (pltpu.roll(d_t[i], back, 1) if back else d_t[i])
        for i in range(11):
            grad_rows[i] = grad_rows[i] + grads[i]
    return velocity, grad_target, grad_rows


def pair_kernel(t_ref, s_ref, c_ref, v_ref, gt_ref, gs_ref):
    age_count = t_ref.shape[-1]
    lane = lax.broadcasted_iota(jnp.int32, (GROUP_PAIRS, age_count), 1)

    def body(group, carry):
        at = pl.ds(pl.multiple_of(group * GROUP_PAIRS, GROUP_PAIRS), GROUP_PAIRS)
        target = [t_ref[i, at, :] for i in range(3)]
        cotangent = [c_ref[i, at, :] for i in range(3)]
        rows = [s_ref[i, at, :] for i in range(12)]
        velocity, grad_target, grad_rows = pair_group(target, cotangent, rows, lane)
        for i in range(3):
            v_ref[i, at, :] = velocity[i]
            gt_ref[i, at, :] = grad_target[i]
        for i in range(11):
            gs_ref[i, at, :] = grad_rows[i]
        return carry

    lax.fori_loop(0, t_ref.shape[1] // GROUP_PAIRS, body, 0)


def run_pairs(targets, payload, cotangent):
    number = targets.shape[0]
    age_count = targets.shape[-1]
    step = min(number, BLOCK_PAIRS)

    def spec(rows):
        return pl.BlockSpec((rows, step, age_count), lambda i: (0, i, 0))

    t_rows = jnp.transpose(targets, (1, 0, 2))
    s_rows = jnp.transpose(payload, (1, 0, 2))
    c_rows = jnp.transpose(cotangent, (1, 0, 2))
    velocity, grad_targets, grad_payload = pl.pallas_call(
        pair_kernel,
        grid=(number // step,),
        in_specs=[spec(3), spec(12), spec(3)],
        out_specs=[spec(3), spec(3), spec(11)],
        out_shape=[
            jax.ShapeDtypeStruct((3, number, age_count), jnp.float32),
            jax.ShapeDtypeStruct((3, number, age_count), jnp.float32),
            jax.ShapeDtypeStruct((11, number, age_count), jnp.float32),
        ],
    )(t_rows, s_rows, c_rows)
    return (
        jnp.transpose(velocity, (1, 0, 2)),
        jnp.transpose(grad_targets, (1, 0, 2)),
        jnp.transpose(grad_payload, (1, 0, 2)),
    )


def onehot_sum(indices, rows, values):
    selector = (jnp.arange(rows, dtype=jnp.int32)[:, None] == indices[None, :]).astype(jnp.float32)
    flat = values.reshape(values.shape[0], -1)
    summed = jnp.dot(
        selector, flat, precision=lax.Precision.HIGHEST, preferred_element_type=jnp.float32
    )
    return summed.reshape((rows,) + values.shape[1:])


def local(positions, strengths, core_radius, adjoint_seed, pair_target, pair_owner, pair_source):
    shape_here = positions.shape
    station_here = shape_here[3]
    age_here = shape_here[4]
    blocks_here = shape_here[1] * shape_here[2] * station_here
    group_size = lax.axis_size("turb") * lax.axis_size("age")
    pair_count = pair_target.shape[-1]
    capacity = 2 * pair_count // group_size
    target_ids = pair_target.reshape(pair_count)
    owner_ids = pair_owner.reshape(pair_count)
    source_ids = pair_source.reshape(pair_count)
    next_ages = shifted_2(positions[..., 0], "age", -1)
    next_stations = shifted_2(positions[:, :, :, 0, :], "span", -1)
    age_keep = (
        lax.axis_index("age") * age_here + jnp.arange(age_here, dtype=jnp.int32)
        < age_here * lax.axis_size("age") - 1
    ).astype(jnp.float32)
    station_keep = (
        lax.axis_index("span") * station_here + jnp.arange(station_here, dtype=jnp.int32)
        < station_here * lax.axis_size("span") - 1
    ).astype(jnp.float32)

    def build(nodes, after_age, after_station, circulation):
        trail_end = jnp.concatenate([nodes[..., 1:], after_age[..., None]], axis=-1)
        shed_end = jnp.concatenate([nodes[:, :, :, 1:, :], after_station[:, :, :, None, :]], axis=3)
        trail_gamma = circulation[0] * age_keep
        shed_gamma = circulation[1] * station_keep[:, None]
        stacked = jnp.concatenate(
            [nodes, trail_end, shed_end, trail_gamma[None], shed_gamma[None], core_radius[None]],
            axis=0,
        )
        return jnp.transpose(stacked.reshape(12, blocks_here, age_here), (1, 0, 2))

    payload, build_pullback = jax.vjp(build, positions, next_ages, next_stations, strengths)

    def to_rows(array):
        return jnp.transpose(array.reshape(array.shape[0], blocks_here, age_here), (1, 0, 2))

    def from_rows(array):
        return jnp.transpose(array, (1, 0, 2)).reshape(shape_here)

    target_blocks = to_rows(positions)
    seed_blocks = to_rows(adjoint_seed)
    earlier = (
        jnp.arange(pair_count, dtype=jnp.int32)[:, None]
        > jnp.arange(pair_count, dtype=jnp.int32)[None, :]
    )
    rank_within = jnp.sum(
        ((owner_ids[:, None] == owner_ids[None, :]) & earlier).astype(jnp.int32), axis=1
    )
    slot_index = owner_ids * capacity + rank_within
    slot_count = group_size * capacity
    slot_pick = (
        jnp.arange(slot_count, dtype=jnp.int32)[:, None] == slot_index[None, :]
    ).astype(jnp.float32)
    block_pick = (
        target_ids[:, None] == jnp.arange(blocks_here, dtype=jnp.int32)[None, :]
    ).astype(jnp.float32)
    slot_block = jnp.dot(slot_pick, block_pick, preferred_element_type=jnp.float32)
    blocks_sent = jnp.concatenate([target_blocks, seed_blocks], axis=1)
    rows_sent = jnp.dot(
        slot_block,
        blocks_sent.reshape(blocks_here, -1),
        precision=lax.Precision.HIGHEST,
        preferred_element_type=jnp.float32,
    ).reshape(slot_count, 6, age_here)
    ident = jnp.dot(
        slot_pick,
        (source_ids + 1).astype(jnp.float32),
        precision=lax.Precision.HIGHEST,
        preferred_element_type=jnp.float32,
    )
    outgoing = jnp.concatenate(
        [rows_sent, jnp.broadcast_to(ident[:, None, None], (slot_count, 1, age_here))],
        axis=1,
    )
    received = lax.all_to_all(
        outgoing.reshape(group_size, capacity, 7, age_here),
        ("turb", "age"),
        split_axis=0,
        concat_axis=0,
        tiled=True,
    ).reshape(slot_count, 7, age_here)
    asked = received[:, 6, 0].astype(jnp.int32) - 1
    slot_payload = payload[jnp.clip(asked, 0, blocks_here - 1)]
    slot_velocity, slot_grad, payload_terms = run_pairs(
        received[:, 0:3], slot_payload, received[:, 3:6] * time_step
    )
    payload_terms = jnp.concatenate(
        [payload_terms, jnp.zeros_like(payload_terms[:, :1])], axis=1
    )
    payload_grad = onehot_sum(asked, blocks_here, payload_terms)
    answered = lax.all_to_all(
        jnp.concatenate([slot_velocity, slot_grad], axis=1).reshape(
            group_size, capacity, 6, age_here
        ),
        ("turb", "age"),
        split_axis=0,
        concat_axis=0,
        tiled=True,
    ).reshape(slot_count, 6, age_here)
    summed = jnp.dot(
        slot_block.T,
        answered.reshape(slot_count, -1),
        precision=lax.Precision.HIGHEST,
        preferred_element_type=jnp.float32,
    ).reshape(blocks_here, 6, age_here)
    velocity = summed[:, 0:3]
    target_grad = summed[:, 3:6]
    advected = positions + time_step * from_rows(velocity)
    advected = advected.at[0].add(time_step)
    grad_nodes, grad_after_age, grad_after_station, grad_strengths = build_pullback(payload_grad)
    from_prior_age = shifted_2(grad_after_age, "age", 1)
    from_prior_station = shifted_2(grad_after_station, "span", 1)
    grad_positions = adjoint_seed + grad_nodes + from_rows(target_grad)
    grad_positions = grad_positions.at[..., 0].add(from_prior_age)
    grad_positions = grad_positions.at[:, :, :, 0, :].add(from_prior_station)
    return (advected, grad_positions, grad_strengths)


def solution(mesh):
    placed = (
        P(None, "turb", None, "span", "age"),
        P(None, "turb", None, "span", "age"),
        P("turb", None, "span", "age"),
        P(None, "turb", None, "span", "age"),
        P("turb", "age", "span", None),
        P("turb", "age", "span", None),
        P("turb", "age", "span", None),
    )
    return jax.shard_map(
        local,
        mesh=mesh,
        in_specs=placed,
        out_specs=(
            P(None, "turb", None, "span", "age"),
            P(None, "turb", None, "span", "age"),
            P(None, "turb", None, "span", "age"),
        ),
        check_vma=False,
    )
```

```python
import math

import jax
import jax.numpy as jnp
from jax import lax
from jax.sharding import PartitionSpec as P
from jax.experimental import pallas as pl
from jax.experimental.pallas import tpu as pltpu

REACH = 8


time_step = 0.5
four_pi = 4.0 * math.pi
batch_rows = 16


def shifted_2(value, axis, steps):
    count = lax.axis_size(axis)
    leading, last = (max(0, -steps), min(count, count - steps))
    return lax.ppermute(value, axis, [(source, source + steps) for source in range(leading, last)])


def windows(payload):
    age_count = payload.shape[-1]
    padded = jnp.pad(payload, ((0, 0), (0, 0), (REACH, REACH)))
    stacked = jnp.stack(
        [
            padded[:, :, REACH + offset : REACH + offset + age_count]
            for offset in range(-REACH, REACH)
        ]
    )
    shifted = (
        jnp.arange(-REACH, REACH, dtype=jnp.int32)[:, None]
        + jnp.arange(age_count, dtype=jnp.int32)[None, :]
    )
    inside = ((shifted >= 0) & (shifted < age_count)).astype(payload.dtype)
    return (stacked, inside)


def induced(targets, payload):
    stacked, inside = windows(payload)
    begins = stacked[:, :, 0:3]
    end_points = jnp.stack([stacked[:, :, 3:6], stacked[:, :, 6:9]])
    gammas = jnp.stack([stacked[:, :, 9], stacked[:, :, 10]]) * inside[None, :, None, :]
    core = jnp.where(inside[:, None, :] > 0, stacked[:, :, 11], 1.0)
    core_sq = core * core
    core_quad = core_sq * core_sq
    from_begin = targets[None] - begins
    from_end = targets[None, None] - end_points
    along = end_points - begins[None]
    near = from_begin[None]
    cross_x = near[..., 1, :] * from_end[..., 2, :] - near[..., 2, :] * from_end[..., 1, :]
    cross_y = near[..., 2, :] * from_end[..., 0, :] - near[..., 0, :] * from_end[..., 2, :]
    cross_z = near[..., 0, :] * from_end[..., 1, :] - near[..., 1, :] * from_end[..., 0, :]
    cross_sq = cross_x * cross_x + cross_y * cross_y + cross_z * cross_z
    length_sq = jnp.sum(along * along, axis=-2) + core_sq
    dist_begin = jnp.sqrt(jnp.sum(from_begin * from_begin, axis=-2) + core_sq)
    dist_end = jnp.sqrt(jnp.sum(from_end * from_end, axis=-2) + core_sq)
    projected = jnp.sum(
        along * (near / dist_begin[None, :, :, None, :] - from_end / dist_end[..., None, :]),
        axis=-2,
    )
    factor = (
        gammas
        * projected
        / (four_pi * jnp.sqrt(cross_sq * cross_sq + core_quad * length_sq * length_sq))
    )
    return jnp.stack(
        [
            jnp.sum(cross_x * factor, axis=(0, 1)),
            jnp.sum(cross_y * factor, axis=(0, 1)),
            jnp.sum(cross_z * factor, axis=(0, 1)),
        ],
        axis=1,
    )


GROUP_PAIRS = 8
BLOCK_PAIRS = 64


def dot3(a, b):
    return a[0] * b[0] + a[1] * b[1] + a[2] * b[2]


def cross3(a, b):
    return (
        a[1] * b[2] - a[2] * b[1],
        a[2] * b[0] - a[0] * b[2],
        a[0] * b[1] - a[1] * b[0],
    )


def segment_pair(target, begin, ends, gammas, core, inside, weight):
    core_sq = core * core
    core_quad = core_sq * core_sq
    near = [target[i] - begin[i] for i in range(3)]
    inv_begin = lax.rsqrt(dot3(near, near) + core_sq)
    velocity = [0.0, 0.0, 0.0]
    grad_target = [0.0, 0.0, 0.0]
    grad_begin = [0.0, 0.0, 0.0]
    grad_ends = []
    grad_gammas = []
    for end_point, raw_gamma in zip(ends, gammas):
        gamma = jnp.where(inside, raw_gamma, 0.0)
        far = [target[i] - end_point[i] for i in range(3)]
        along = [end_point[i] - begin[i] for i in range(3)]
        cross = cross3(near, far)
        cross_sq = dot3(cross, cross)
        length_sq = dot3(along, along) + core_sq
        inv_end = lax.rsqrt(dot3(far, far) + core_sq)
        along_near = dot3(along, near)
        along_far = dot3(along, far)
        projected = along_near * inv_begin - along_far * inv_end
        inv_den = lax.rsqrt(cross_sq * cross_sq + core_quad * length_sq * length_sq)
        base = projected * inv_den * (1.0 / four_pi)
        factor = gamma * base
        for i in range(3):
            velocity[i] = velocity[i] + cross[i] * factor
        ct_factor = dot3(cross, weight)
        grad_gammas.append(jnp.where(inside, ct_factor * base, 0.0))
        ct_proj = ct_factor * gamma * inv_den * (1.0 / four_pi)
        ct_q = -0.5 * ct_factor * factor * inv_den * inv_den
        cross_scale = 4.0 * cross_sq * ct_q
        along_scale = 4.0 * core_quad * length_sq * ct_q
        ct_cross = [factor * weight[i] + cross_scale * cross[i] for i in range(3)]
        near_scale = ct_proj * inv_begin
        far_scale = ct_proj * inv_end
        near_radial = near_scale * along_near * inv_begin * inv_begin
        far_radial = far_scale * along_far * inv_end * inv_end
        from_far = cross3(far, ct_cross)
        from_near = cross3(ct_cross, near)
        ct_along = [
            along_scale * along[i] + near_scale * near[i] - far_scale * far[i] for i in range(3)
        ]
        ct_near = [near_scale * along[i] - near_radial * near[i] + from_far[i] for i in range(3)]
        ct_far = [-far_scale * along[i] + far_radial * far[i] + from_near[i] for i in range(3)]
        for i in range(3):
            grad_target[i] = grad_target[i] + ct_near[i] + ct_far[i]
            grad_begin[i] = grad_begin[i] - ct_near[i] - ct_along[i]
        grad_ends.append([ct_along[i] - ct_far[i] for i in range(3)])
    return velocity, grad_target, grad_begin, grad_ends, grad_gammas


def pair_group(target, cotangent, rows, lane):
    age_count = lane.shape[-1]
    velocity = [0.0] * 3
    grad_target = [0.0] * 3
    grad_rows = [0.0] * 11
    for offset in range(-REACH, REACH):
        amount = offset % age_count
        moved = [pltpu.roll(r, amount, 1) if amount else r for r in target]
        weight = [pltpu.roll(r, amount, 1) if amount else r for r in cotangent]
        inside = (lane - offset >= 0) & (lane - offset < age_count)
        u, d_t, d_b, d_ends, d_gammas = segment_pair(
            moved,
            rows[0:3],
            (rows[3:6], rows[6:9]),
            (rows[9], rows[10]),
            rows[11],
            inside,
            weight,
        )
        grads = list(d_b) + list(d_ends[0]) + list(d_ends[1]) + list(d_gammas)
        back = (-offset) % age_count
        for i in range(3):
            velocity[i] = velocity[i] + (pltpu.roll(u[i], back, 1) if back else u[i])
            grad_target[i] = grad_target[i] + (pltpu.roll(d_t[i], back, 1) if back else d_t[i])
        for i in range(11):
            grad_rows[i] = grad_rows[i] + grads[i]
    return velocity, grad_target, grad_rows


def pair_kernel(t_ref, s_ref, c_ref, v_ref, gt_ref, gs_ref):
    age_count = t_ref.shape[-1]
    lane = lax.broadcasted_iota(jnp.int32, (GROUP_PAIRS, age_count), 1)

    def body(group, carry):
        at = pl.ds(pl.multiple_of(group * GROUP_PAIRS, GROUP_PAIRS), GROUP_PAIRS)
        target = [t_ref[i, at, :] for i in range(3)]
        cotangent = [c_ref[i, at, :] for i in range(3)]
        rows = [s_ref[i, at, :] for i in range(12)]
        velocity, grad_target, grad_rows = pair_group(target, cotangent, rows, lane)
        for i in range(3):
            v_ref[i, at, :] = velocity[i]
            gt_ref[i, at, :] = grad_target[i]
        for i in range(11):
            gs_ref[i, at, :] = grad_rows[i]
        return carry

    lax.fori_loop(0, t_ref.shape[1] // GROUP_PAIRS, body, 0)


def run_pairs(targets, payload, cotangent):
    number = targets.shape[1]
    age_count = targets.shape[-1]
    step = min(number, BLOCK_PAIRS)

    def spec(rows):
        return pl.BlockSpec((rows, step, age_count), lambda i: (0, i, 0))

    return pl.pallas_call(
        pair_kernel,
        grid=(number // step,),
        in_specs=[spec(3), spec(12), spec(3)],
        out_specs=[spec(3), spec(3), spec(11)],
        out_shape=[
            jax.ShapeDtypeStruct((3, number, age_count), jnp.float32),
            jax.ShapeDtypeStruct((3, number, age_count), jnp.float32),
            jax.ShapeDtypeStruct((11, number, age_count), jnp.float32),
        ],
    )(targets, payload, cotangent)


def onehot_sum(indices, rows, values):
    selector = (jnp.arange(rows, dtype=jnp.int32)[:, None] == indices[None, :]).astype(jnp.float32)
    flat = values.reshape(values.shape[0], -1)
    summed = jnp.dot(
        selector, flat, precision=lax.Precision.HIGHEST, preferred_element_type=jnp.float32
    )
    return summed.reshape((rows,) + values.shape[1:])


def local(positions, strengths, core_radius, adjoint_seed, pair_target, pair_owner, pair_source):
    shape_here = positions.shape
    station_here = shape_here[3]
    age_here = shape_here[4]
    blocks_here = shape_here[1] * shape_here[2] * station_here
    group_size = lax.axis_size("turb") * lax.axis_size("age")
    pair_count = pair_target.shape[-1]
    capacity = 2 * pair_count // group_size
    target_ids = pair_target.reshape(pair_count)
    owner_ids = pair_owner.reshape(pair_count)
    source_ids = pair_source.reshape(pair_count)
    next_ages = shifted_2(positions[..., 0], "age", -1)
    next_stations = shifted_2(positions[:, :, :, 0, :], "span", -1)
    age_keep = (
        lax.axis_index("age") * age_here + jnp.arange(age_here, dtype=jnp.int32)
        < age_here * lax.axis_size("age") - 1
    ).astype(jnp.float32)
    station_keep = (
        lax.axis_index("span") * station_here + jnp.arange(station_here, dtype=jnp.int32)
        < station_here * lax.axis_size("span") - 1
    ).astype(jnp.float32)

    def build(nodes, after_age, after_station, circulation):
        trail_end = jnp.concatenate([nodes[..., 1:], after_age[..., None]], axis=-1)
        shed_end = jnp.concatenate([nodes[:, :, :, 1:, :], after_station[:, :, :, None, :]], axis=3)
        trail_gamma = circulation[0] * age_keep
        shed_gamma = circulation[1] * station_keep[:, None]
        stacked = jnp.concatenate(
            [nodes, trail_end, shed_end, trail_gamma[None], shed_gamma[None], core_radius[None]],
            axis=0,
        )
        return stacked.reshape(12, blocks_here, age_here)

    payload, build_pullback = jax.vjp(build, positions, next_ages, next_stations, strengths)

    def to_rows(array):
        return array.reshape(array.shape[0], blocks_here, age_here)

    def from_rows(array):
        return array.reshape(shape_here)

    def pick_rows(selector, values):
        return jnp.einsum(
            "sb,rba->rsa",
            selector,
            values,
            precision=lax.Precision.HIGHEST,
            preferred_element_type=jnp.float32,
        )

    def sum_rows(selector, values):
        return jnp.einsum(
            "sb,rsa->rba",
            selector,
            values,
            precision=lax.Precision.HIGHEST,
            preferred_element_type=jnp.float32,
        )

    target_blocks = to_rows(positions)
    seed_blocks = to_rows(adjoint_seed)
    earlier = (
        jnp.arange(pair_count, dtype=jnp.int32)[:, None]
        > jnp.arange(pair_count, dtype=jnp.int32)[None, :]
    )
    rank_within = jnp.sum(
        ((owner_ids[:, None] == owner_ids[None, :]) & earlier).astype(jnp.int32), axis=1
    )
    slot_index = owner_ids * capacity + rank_within
    slot_count = group_size * capacity
    slot_pick = (
        jnp.arange(slot_count, dtype=jnp.int32)[:, None] == slot_index[None, :]
    ).astype(jnp.float32)
    block_pick = (
        target_ids[:, None] == jnp.arange(blocks_here, dtype=jnp.int32)[None, :]
    ).astype(jnp.float32)
    slot_block = jnp.dot(slot_pick, block_pick, preferred_element_type=jnp.float32)
    rows_sent = pick_rows(slot_block, jnp.concatenate([target_blocks, seed_blocks], axis=0))
    ident = jnp.dot(
        slot_pick,
        (source_ids + 1).astype(jnp.float32),
        precision=lax.Precision.HIGHEST,
        preferred_element_type=jnp.float32,
    )
    outgoing = jnp.concatenate(
        [rows_sent, jnp.broadcast_to(ident[None, :, None], (1, slot_count, age_here))],
        axis=0,
    )
    received = lax.all_to_all(
        outgoing.reshape(7, group_size, capacity, age_here),
        ("turb", "age"),
        split_axis=1,
        concat_axis=1,
        tiled=True,
    ).reshape(7, slot_count, age_here)
    asked = received[6, :, 0].astype(jnp.int32) - 1
    slot_payload = payload[:, jnp.clip(asked, 0, blocks_here - 1)]
    slot_velocity, slot_grad, payload_terms = run_pairs(
        received[0:3], slot_payload, received[3:6] * time_step
    )
    payload_terms = jnp.concatenate(
        [payload_terms, jnp.zeros_like(payload_terms[:1])], axis=0
    )
    asked_pick = (
        asked[:, None] == jnp.arange(blocks_here, dtype=jnp.int32)[None, :]
    ).astype(jnp.float32)
    payload_grad = sum_rows(asked_pick, payload_terms)
    answered = lax.all_to_all(
        jnp.concatenate([slot_velocity, slot_grad], axis=0).reshape(
            6, group_size, capacity, age_here
        ),
        ("turb", "age"),
        split_axis=1,
        concat_axis=1,
        tiled=True,
    ).reshape(6, slot_count, age_here)
    summed = sum_rows(slot_block, answered)
    velocity = summed[0:3]
    target_grad = summed[3:6]
    advected = positions + time_step * from_rows(velocity)
    advected = advected.at[0].add(time_step)
    grad_nodes, grad_after_age, grad_after_station, grad_strengths = build_pullback(payload_grad)
    from_prior_age = shifted_2(grad_after_age, "age", 1)
    from_prior_station = shifted_2(grad_after_station, "span", 1)
    grad_positions = adjoint_seed + grad_nodes + from_rows(target_grad)
    grad_positions = grad_positions.at[..., 0].add(from_prior_age)
    grad_positions = grad_positions.at[:, :, :, 0, :].add(from_prior_station)
    return (advected, grad_positions, grad_strengths)


def solution(mesh):
    placed = (
        P(None, "turb", None, "span", "age"),
        P(None, "turb", None, "span", "age"),
        P("turb", None, "span", "age"),
        P(None, "turb", None, "span", "age"),
        P("turb", "age", "span", None),
        P("turb", "age", "span", None),
        P("turb", "age", "span", None),
    )
    return jax.shard_map(
        local,
        mesh=mesh,
        in_specs=placed,
        out_specs=(
            P(None, "turb", None, "span", "age"),
            P(None, "turb", None, "span", "age"),
            P(None, "turb", None, "span", "age"),
        ),
        check_vma=False,
    )
```

```python
import math

import jax
import jax.numpy as jnp
from jax import lax
from jax.sharding import PartitionSpec as P
from jax.experimental import pallas as pl
from jax.experimental.pallas import tpu as pltpu

REACH = 8


time_step = 0.5
four_pi = 4.0 * math.pi
batch_rows = 16


def shifted_2(value, axis, steps):
    count = lax.axis_size(axis)
    leading, last = (max(0, -steps), min(count, count - steps))
    return lax.ppermute(value, axis, [(source, source + steps) for source in range(leading, last)])


def windows(payload):
    age_count = payload.shape[-1]
    padded = jnp.pad(payload, ((0, 0), (0, 0), (REACH, REACH)))
    stacked = jnp.stack(
        [
            padded[:, :, REACH + offset : REACH + offset + age_count]
            for offset in range(-REACH, REACH)
        ]
    )
    shifted = (
        jnp.arange(-REACH, REACH, dtype=jnp.int32)[:, None]
        + jnp.arange(age_count, dtype=jnp.int32)[None, :]
    )
    inside = ((shifted >= 0) & (shifted < age_count)).astype(payload.dtype)
    return (stacked, inside)


def induced(targets, payload):
    stacked, inside = windows(payload)
    begins = stacked[:, :, 0:3]
    end_points = jnp.stack([stacked[:, :, 3:6], stacked[:, :, 6:9]])
    gammas = jnp.stack([stacked[:, :, 9], stacked[:, :, 10]]) * inside[None, :, None, :]
    core = jnp.where(inside[:, None, :] > 0, stacked[:, :, 11], 1.0)
    core_sq = core * core
    core_quad = core_sq * core_sq
    from_begin = targets[None] - begins
    from_end = targets[None, None] - end_points
    along = end_points - begins[None]
    near = from_begin[None]
    cross_x = near[..., 1, :] * from_end[..., 2, :] - near[..., 2, :] * from_end[..., 1, :]
    cross_y = near[..., 2, :] * from_end[..., 0, :] - near[..., 0, :] * from_end[..., 2, :]
    cross_z = near[..., 0, :] * from_end[..., 1, :] - near[..., 1, :] * from_end[..., 0, :]
    cross_sq = cross_x * cross_x + cross_y * cross_y + cross_z * cross_z
    length_sq = jnp.sum(along * along, axis=-2) + core_sq
    dist_begin = jnp.sqrt(jnp.sum(from_begin * from_begin, axis=-2) + core_sq)
    dist_end = jnp.sqrt(jnp.sum(from_end * from_end, axis=-2) + core_sq)
    projected = jnp.sum(
        along * (near / dist_begin[None, :, :, None, :] - from_end / dist_end[..., None, :]),
        axis=-2,
    )
    factor = (
        gammas
        * projected
        / (four_pi * jnp.sqrt(cross_sq * cross_sq + core_quad * length_sq * length_sq))
    )
    return jnp.stack(
        [
            jnp.sum(cross_x * factor, axis=(0, 1)),
            jnp.sum(cross_y * factor, axis=(0, 1)),
            jnp.sum(cross_z * factor, axis=(0, 1)),
        ],
        axis=1,
    )


GROUP_PAIRS = 8
BLOCK_PAIRS = 64


def dot3(a, b):
    return a[0] * b[0] + a[1] * b[1] + a[2] * b[2]


def cross3(a, b):
    return (
        a[1] * b[2] - a[2] * b[1],
        a[2] * b[0] - a[0] * b[2],
        a[0] * b[1] - a[1] * b[0],
    )


def segment_pair(target, begin, ends, gammas, core, inside, weight):
    core_sq = core * core
    core_quad = core_sq * core_sq
    near = [target[i] - begin[i] for i in range(3)]
    inv_begin = lax.rsqrt(dot3(near, near) + core_sq)
    velocity = [0.0, 0.0, 0.0]
    grad_target = [0.0, 0.0, 0.0]
    grad_begin = [0.0, 0.0, 0.0]
    grad_ends = []
    grad_gammas = []
    for end_point, raw_gamma in zip(ends, gammas):
        gamma = jnp.where(inside, raw_gamma, 0.0)
        far = [target[i] - end_point[i] for i in range(3)]
        along = [end_point[i] - begin[i] for i in range(3)]
        cross = cross3(near, far)
        cross_sq = dot3(cross, cross)
        length_sq = dot3(along, along) + core_sq
        inv_end = lax.rsqrt(dot3(far, far) + core_sq)
        along_near = dot3(along, near)
        along_far = dot3(along, far)
        projected = along_near * inv_begin - along_far * inv_end
        inv_den = lax.rsqrt(cross_sq * cross_sq + core_quad * length_sq * length_sq)
        base = projected * inv_den * (1.0 / four_pi)
        factor = gamma * base
        for i in range(3):
            velocity[i] = velocity[i] + cross[i] * factor
        ct_factor = dot3(cross, weight)
        grad_gammas.append(jnp.where(inside, ct_factor * base, 0.0))
        ct_proj = ct_factor * gamma * inv_den * (1.0 / four_pi)
        ct_q = -0.5 * ct_factor * factor * inv_den * inv_den
        cross_scale = 4.0 * cross_sq * ct_q
        along_scale = 4.0 * core_quad * length_sq * ct_q
        ct_cross = [factor * weight[i] + cross_scale * cross[i] for i in range(3)]
        near_scale = ct_proj * inv_begin
        far_scale = ct_proj * inv_end
        near_radial = near_scale * along_near * inv_begin * inv_begin
        far_radial = far_scale * along_far * inv_end * inv_end
        from_far = cross3(far, ct_cross)
        from_near = cross3(ct_cross, near)
        ct_along = [
            along_scale * along[i] + near_scale * near[i] - far_scale * far[i] for i in range(3)
        ]
        ct_near = [near_scale * along[i] - near_radial * near[i] + from_far[i] for i in range(3)]
        ct_far = [-far_scale * along[i] + far_radial * far[i] + from_near[i] for i in range(3)]
        for i in range(3):
            grad_target[i] = grad_target[i] + ct_near[i] + ct_far[i]
            grad_begin[i] = grad_begin[i] - ct_near[i] - ct_along[i]
        grad_ends.append([ct_along[i] - ct_far[i] for i in range(3)])
    return velocity, grad_target, grad_begin, grad_ends, grad_gammas


def pair_group(target, cotangent, rows, lane):
    age_count = lane.shape[-1]
    velocity = [0.0] * 3
    grad_target = [0.0] * 3
    grad_rows = [0.0] * 11
    for offset in range(-REACH, REACH):
        amount = offset % age_count
        moved = [pltpu.roll(r, amount, 1) if amount else r for r in target]
        weight = [pltpu.roll(r, amount, 1) if amount else r for r in cotangent]
        inside = (lane - offset >= 0) & (lane - offset < age_count)
        u, d_t, d_b, d_ends, d_gammas = segment_pair(
            moved,
            rows[0:3],
            (rows[3:6], rows[6:9]),
            (rows[9], rows[10]),
            rows[11],
            inside,
            weight,
        )
        grads = list(d_b) + list(d_ends[0]) + list(d_ends[1]) + list(d_gammas)
        back = (-offset) % age_count
        for i in range(3):
            velocity[i] = velocity[i] + (pltpu.roll(u[i], back, 1) if back else u[i])
            grad_target[i] = grad_target[i] + (pltpu.roll(d_t[i], back, 1) if back else d_t[i])
        for i in range(11):
            grad_rows[i] = grad_rows[i] + grads[i]
    return velocity, grad_target, grad_rows


def pair_kernel(t_ref, s_ref, c_ref, v_ref, gt_ref, gs_ref):
    age_count = t_ref.shape[-1]
    lane = lax.broadcasted_iota(jnp.int32, (GROUP_PAIRS, age_count), 1)

    def body(group, carry):
        at = pl.ds(pl.multiple_of(group * GROUP_PAIRS, GROUP_PAIRS), GROUP_PAIRS)
        target = [t_ref[i, at, :] for i in range(3)]
        cotangent = [c_ref[i, at, :] for i in range(3)]
        rows = [s_ref[i, at, :] for i in range(12)]
        velocity, grad_target, grad_rows = pair_group(target, cotangent, rows, lane)
        for i in range(3):
            v_ref[i, at, :] = velocity[i]
            gt_ref[i, at, :] = grad_target[i]
        for i in range(11):
            gs_ref[i, at, :] = grad_rows[i]
        return carry

    lax.fori_loop(0, t_ref.shape[1] // GROUP_PAIRS, body, 0)


def run_pairs(targets, payload, cotangent):
    number = targets.shape[1]
    age_count = targets.shape[-1]
    step = min(number, BLOCK_PAIRS)

    def spec(rows):
        return pl.BlockSpec((rows, step, age_count), lambda i: (0, i, 0))

    return pl.pallas_call(
        pair_kernel,
        grid=(number // step,),
        in_specs=[spec(3), spec(12), spec(3)],
        out_specs=[spec(3), spec(3), spec(11)],
        out_shape=[
            jax.ShapeDtypeStruct((3, number, age_count), jnp.float32),
            jax.ShapeDtypeStruct((3, number, age_count), jnp.float32),
            jax.ShapeDtypeStruct((11, number, age_count), jnp.float32),
        ],
    )(targets, payload, cotangent)


def onehot_sum(indices, rows, values):
    selector = (jnp.arange(rows, dtype=jnp.int32)[:, None] == indices[None, :]).astype(jnp.float32)
    flat = values.reshape(values.shape[0], -1)
    summed = jnp.dot(
        selector, flat, precision=lax.Precision.HIGHEST, preferred_element_type=jnp.float32
    )
    return summed.reshape((rows,) + values.shape[1:])


def local(positions, strengths, core_radius, adjoint_seed, pair_target, pair_owner, pair_source):
    shape_here = positions.shape
    station_here = shape_here[3]
    age_here = shape_here[4]
    blocks_here = shape_here[1] * shape_here[2] * station_here
    group_size = lax.axis_size("turb") * lax.axis_size("age")
    pair_count = pair_target.shape[-1]
    capacity = 2 * pair_count // group_size
    target_ids = pair_target.reshape(pair_count)
    owner_ids = pair_owner.reshape(pair_count)
    source_ids = pair_source.reshape(pair_count)
    next_ages = shifted_2(positions[..., 0], "age", -1)
    next_stations = shifted_2(positions[:, :, :, 0, :], "span", -1)
    age_keep = (
        lax.axis_index("age") * age_here + jnp.arange(age_here, dtype=jnp.int32)
        < age_here * lax.axis_size("age") - 1
    ).astype(jnp.float32)
    station_keep = (
        lax.axis_index("span") * station_here + jnp.arange(station_here, dtype=jnp.int32)
        < station_here * lax.axis_size("span") - 1
    ).astype(jnp.float32)

    def build(nodes, after_age, after_station, circulation):
        trail_end = jnp.concatenate([nodes[..., 1:], after_age[..., None]], axis=-1)
        shed_end = jnp.concatenate([nodes[:, :, :, 1:, :], after_station[:, :, :, None, :]], axis=3)
        trail_gamma = circulation[0] * age_keep
        shed_gamma = circulation[1] * station_keep[:, None]
        stacked = jnp.concatenate(
            [nodes, trail_end, shed_end, trail_gamma[None], shed_gamma[None], core_radius[None]],
            axis=0,
        )
        return stacked.reshape(12, blocks_here, age_here)

    payload, build_pullback = jax.vjp(build, positions, next_ages, next_stations, strengths)

    def to_rows(array):
        return array.reshape(array.shape[0], blocks_here, age_here)

    def from_rows(array):
        return array.reshape(shape_here)

    def pick_rows(selector, values):
        return jnp.einsum(
            "sb,rba->rsa",
            selector,
            values,
            precision=lax.Precision.HIGHEST,
            preferred_element_type=jnp.float32,
        )

    def sum_rows(selector, values):
        return jnp.einsum(
            "sb,rsa->rba",
            selector,
            values,
            precision=lax.Precision.HIGHEST,
            preferred_element_type=jnp.float32,
        )

    target_blocks = to_rows(positions)
    seed_blocks = to_rows(adjoint_seed)
    earlier = (
        jnp.arange(pair_count, dtype=jnp.int32)[:, None]
        > jnp.arange(pair_count, dtype=jnp.int32)[None, :]
    )
    rank_within = jnp.sum(
        ((owner_ids[:, None] == owner_ids[None, :]) & earlier).astype(jnp.int32), axis=1
    )
    slot_index = owner_ids * capacity + rank_within
    slot_count = group_size * capacity
    slot_pick = (
        jnp.arange(slot_count, dtype=jnp.int32)[:, None] == slot_index[None, :]
    ).astype(jnp.float32)
    block_pick = (
        target_ids[:, None] == jnp.arange(blocks_here, dtype=jnp.int32)[None, :]
    ).astype(jnp.float32)
    slot_block = jnp.dot(slot_pick, block_pick, preferred_element_type=jnp.float32)
    rows_sent = pick_rows(slot_block, jnp.concatenate([target_blocks, seed_blocks], axis=0))
    ident = jnp.dot(
        slot_pick,
        (source_ids + 1).astype(jnp.float32),
        precision=lax.Precision.HIGHEST,
        preferred_element_type=jnp.float32,
    )
    outgoing = jnp.concatenate(
        [rows_sent, jnp.broadcast_to(ident[None, :, None], (1, slot_count, age_here))],
        axis=0,
    )
    received = lax.all_to_all(
        outgoing.reshape(7, group_size, capacity, age_here),
        ("turb", "age"),
        split_axis=1,
        concat_axis=1,
        tiled=True,
    ).reshape(7, slot_count, age_here)
    asked = received[6, :, 0].astype(jnp.int32) - 1
    safe_pick = (
        jnp.clip(asked, 0, blocks_here - 1)[:, None]
        == jnp.arange(blocks_here, dtype=jnp.int32)[None, :]
    ).astype(jnp.float32)
    slot_payload = pick_rows(safe_pick, payload)
    slot_velocity, slot_grad, payload_terms = run_pairs(
        received[0:3], slot_payload, received[3:6] * time_step
    )
    payload_terms = jnp.concatenate(
        [payload_terms, jnp.zeros_like(payload_terms[:1])], axis=0
    )
    asked_pick = (
        asked[:, None] == jnp.arange(blocks_here, dtype=jnp.int32)[None, :]
    ).astype(jnp.float32)
    payload_grad = sum_rows(asked_pick, payload_terms)
    answered = lax.all_to_all(
        jnp.concatenate([slot_velocity, slot_grad], axis=0).reshape(
            6, group_size, capacity, age_here
        ),
        ("turb", "age"),
        split_axis=1,
        concat_axis=1,
        tiled=True,
    ).reshape(6, slot_count, age_here)
    summed = sum_rows(slot_block, answered)
    velocity = summed[0:3]
    target_grad = summed[3:6]
    advected = positions + time_step * from_rows(velocity)
    advected = advected.at[0].add(time_step)
    grad_nodes, grad_after_age, grad_after_station, grad_strengths = build_pullback(payload_grad)
    from_prior_age = shifted_2(grad_after_age, "age", 1)
    from_prior_station = shifted_2(grad_after_station, "span", 1)
    grad_positions = adjoint_seed + grad_nodes + from_rows(target_grad)
    grad_positions = grad_positions.at[..., 0].add(from_prior_age)
    grad_positions = grad_positions.at[:, :, :, 0, :].add(from_prior_station)
    return (advected, grad_positions, grad_strengths)


def solution(mesh):
    placed = (
        P(None, "turb", None, "span", "age"),
        P(None, "turb", None, "span", "age"),
        P("turb", None, "span", "age"),
        P(None, "turb", None, "span", "age"),
        P("turb", "age", "span", None),
        P("turb", "age", "span", None),
        P("turb", "age", "span", None),
    )
    return jax.shard_map(
        local,
        mesh=mesh,
        in_specs=placed,
        out_specs=(
            P(None, "turb", None, "span", "age"),
            P(None, "turb", None, "span", "age"),
            P(None, "turb", None, "span", "age"),
        ),
        check_vma=False,
    )
```

```python
import math

import jax
import jax.numpy as jnp
from jax import lax
from jax.sharding import PartitionSpec as P
from jax.experimental import pallas as pl
from jax.experimental.pallas import tpu as pltpu

REACH = 8


time_step = 0.5
four_pi = 4.0 * math.pi
batch_rows = 16


def shifted_2(value, axis, steps):
    count = lax.axis_size(axis)
    leading, last = (max(0, -steps), min(count, count - steps))
    return lax.ppermute(value, axis, [(source, source + steps) for source in range(leading, last)])


def windows(payload):
    age_count = payload.shape[-1]
    padded = jnp.pad(payload, ((0, 0), (0, 0), (REACH, REACH)))
    stacked = jnp.stack(
        [
            padded[:, :, REACH + offset : REACH + offset + age_count]
            for offset in range(-REACH, REACH)
        ]
    )
    shifted = (
        jnp.arange(-REACH, REACH, dtype=jnp.int32)[:, None]
        + jnp.arange(age_count, dtype=jnp.int32)[None, :]
    )
    inside = ((shifted >= 0) & (shifted < age_count)).astype(payload.dtype)
    return (stacked, inside)


def induced(targets, payload):
    stacked, inside = windows(payload)
    begins = stacked[:, :, 0:3]
    end_points = jnp.stack([stacked[:, :, 3:6], stacked[:, :, 6:9]])
    gammas = jnp.stack([stacked[:, :, 9], stacked[:, :, 10]]) * inside[None, :, None, :]
    core = jnp.where(inside[:, None, :] > 0, stacked[:, :, 11], 1.0)
    core_sq = core * core
    core_quad = core_sq * core_sq
    from_begin = targets[None] - begins
    from_end = targets[None, None] - end_points
    along = end_points - begins[None]
    near = from_begin[None]
    cross_x = near[..., 1, :] * from_end[..., 2, :] - near[..., 2, :] * from_end[..., 1, :]
    cross_y = near[..., 2, :] * from_end[..., 0, :] - near[..., 0, :] * from_end[..., 2, :]
    cross_z = near[..., 0, :] * from_end[..., 1, :] - near[..., 1, :] * from_end[..., 0, :]
    cross_sq = cross_x * cross_x + cross_y * cross_y + cross_z * cross_z
    length_sq = jnp.sum(along * along, axis=-2) + core_sq
    dist_begin = jnp.sqrt(jnp.sum(from_begin * from_begin, axis=-2) + core_sq)
    dist_end = jnp.sqrt(jnp.sum(from_end * from_end, axis=-2) + core_sq)
    projected = jnp.sum(
        along * (near / dist_begin[None, :, :, None, :] - from_end / dist_end[..., None, :]),
        axis=-2,
    )
    factor = (
        gammas
        * projected
        / (four_pi * jnp.sqrt(cross_sq * cross_sq + core_quad * length_sq * length_sq))
    )
    return jnp.stack(
        [
            jnp.sum(cross_x * factor, axis=(0, 1)),
            jnp.sum(cross_y * factor, axis=(0, 1)),
            jnp.sum(cross_z * factor, axis=(0, 1)),
        ],
        axis=1,
    )


GROUP_PAIRS = 8
BLOCK_PAIRS = 64


def dot3(a, b):
    return a[0] * b[0] + a[1] * b[1] + a[2] * b[2]


def cross3(a, b):
    return (
        a[1] * b[2] - a[2] * b[1],
        a[2] * b[0] - a[0] * b[2],
        a[0] * b[1] - a[1] * b[0],
    )


def segment_pair(target, begin, ends, gammas, core, inside, weight):
    core_sq = core * core
    core_quad = core_sq * core_sq
    near = [target[i] - begin[i] for i in range(3)]
    inv_begin = lax.rsqrt(dot3(near, near) + core_sq)
    velocity = [0.0, 0.0, 0.0]
    grad_target = [0.0, 0.0, 0.0]
    grad_begin = [0.0, 0.0, 0.0]
    grad_ends = []
    grad_gammas = []
    for end_point, raw_gamma in zip(ends, gammas):
        gamma = jnp.where(inside, raw_gamma, 0.0)
        far = [target[i] - end_point[i] for i in range(3)]
        along = [end_point[i] - begin[i] for i in range(3)]
        cross = cross3(near, far)
        cross_sq = dot3(cross, cross)
        length_sq = dot3(along, along) + core_sq
        inv_end = lax.rsqrt(dot3(far, far) + core_sq)
        along_near = dot3(along, near)
        along_far = dot3(along, far)
        projected = along_near * inv_begin - along_far * inv_end
        inv_den = lax.rsqrt(cross_sq * cross_sq + core_quad * length_sq * length_sq)
        base = projected * inv_den * (1.0 / four_pi)
        factor = gamma * base
        for i in range(3):
            velocity[i] = velocity[i] + cross[i] * factor
        ct_factor = dot3(cross, weight)
        grad_gammas.append(jnp.where(inside, ct_factor * base, 0.0))
        ct_proj = ct_factor * gamma * inv_den * (1.0 / four_pi)
        ct_q = -0.5 * ct_factor * factor * inv_den * inv_den
        cross_scale = 4.0 * cross_sq * ct_q
        along_scale = 4.0 * core_quad * length_sq * ct_q
        ct_cross = [factor * weight[i] + cross_scale * cross[i] for i in range(3)]
        near_scale = ct_proj * inv_begin
        far_scale = ct_proj * inv_end
        near_radial = near_scale * along_near * inv_begin * inv_begin
        far_radial = far_scale * along_far * inv_end * inv_end
        from_far = cross3(far, ct_cross)
        from_near = cross3(ct_cross, near)
        ct_along = [
            along_scale * along[i] + near_scale * near[i] - far_scale * far[i] for i in range(3)
        ]
        ct_near = [near_scale * along[i] - near_radial * near[i] + from_far[i] for i in range(3)]
        ct_far = [-far_scale * along[i] + far_radial * far[i] + from_near[i] for i in range(3)]
        for i in range(3):
            grad_target[i] = grad_target[i] + ct_near[i] + ct_far[i]
            grad_begin[i] = grad_begin[i] - ct_near[i] - ct_along[i]
        grad_ends.append([ct_along[i] - ct_far[i] for i in range(3)])
    return velocity, grad_target, grad_begin, grad_ends, grad_gammas


def pair_group(target, cotangent, rows, lane):
    age_count = lane.shape[-1]
    velocity = [0.0] * 3
    grad_target = [0.0] * 3
    grad_rows = [0.0] * 11
    for offset in range(-REACH, REACH):
        amount = offset % age_count
        moved = [pltpu.roll(r, amount, 1) if amount else r for r in target]
        weight = [pltpu.roll(r, amount, 1) if amount else r for r in cotangent]
        inside = (lane - offset >= 0) & (lane - offset < age_count)
        u, d_t, d_b, d_ends, d_gammas = segment_pair(
            moved,
            rows[0:3],
            (rows[3:6], rows[6:9]),
            (rows[9], rows[10]),
            rows[11],
            inside,
            weight,
        )
        grads = list(d_b) + list(d_ends[0]) + list(d_ends[1]) + list(d_gammas)
        back = (-offset) % age_count
        for i in range(3):
            velocity[i] = velocity[i] + (pltpu.roll(u[i], back, 1) if back else u[i])
            grad_target[i] = grad_target[i] + (pltpu.roll(d_t[i], back, 1) if back else d_t[i])
        for i in range(11):
            grad_rows[i] = grad_rows[i] + grads[i]
    return velocity, grad_target, grad_rows


def pair_kernel(t_ref, s_ref, c_ref, v_ref, gs_ref):
    age_count = t_ref.shape[-1]
    lane = lax.broadcasted_iota(jnp.int32, (GROUP_PAIRS, age_count), 1)

    def body(group, carry):
        at = pl.ds(pl.multiple_of(group * GROUP_PAIRS, GROUP_PAIRS), GROUP_PAIRS)
        target = [t_ref[i, at, :] for i in range(3)]
        cotangent = [c_ref[i, at, :] for i in range(3)]
        rows = [s_ref[i, at, :] for i in range(12)]
        velocity, grad_target, grad_rows = pair_group(target, cotangent, rows, lane)
        for i in range(3):
            v_ref[i, at, :] = velocity[i]
            v_ref[3 + i, at, :] = grad_target[i]
        for i in range(11):
            gs_ref[i, at, :] = grad_rows[i]
        return carry

    lax.fori_loop(0, t_ref.shape[1] // GROUP_PAIRS, body, 0)


def run_pairs(targets, payload, cotangent):
    number = targets.shape[1]
    age_count = targets.shape[-1]
    step = min(number, BLOCK_PAIRS)

    def spec(rows):
        return pl.BlockSpec((rows, step, age_count), lambda i: (0, i, 0))

    return pl.pallas_call(
        pair_kernel,
        grid=(number // step,),
        in_specs=[spec(3), spec(12), spec(3)],
        out_specs=[spec(6), spec(11)],
        out_shape=[
            jax.ShapeDtypeStruct((6, number, age_count), jnp.float32),
            jax.ShapeDtypeStruct((11, number, age_count), jnp.float32),
        ],
    )(targets, payload, cotangent)


def onehot_sum(indices, rows, values):
    selector = (jnp.arange(rows, dtype=jnp.int32)[:, None] == indices[None, :]).astype(jnp.float32)
    flat = values.reshape(values.shape[0], -1)
    summed = jnp.dot(
        selector, flat, precision=lax.Precision.HIGHEST, preferred_element_type=jnp.float32
    )
    return summed.reshape((rows,) + values.shape[1:])


def local(positions, strengths, core_radius, adjoint_seed, pair_target, pair_owner, pair_source):
    shape_here = positions.shape
    station_here = shape_here[3]
    age_here = shape_here[4]
    blocks_here = shape_here[1] * shape_here[2] * station_here
    group_size = lax.axis_size("turb") * lax.axis_size("age")
    pair_count = pair_target.shape[-1]
    capacity = 2 * pair_count // group_size
    target_ids = pair_target.reshape(pair_count)
    owner_ids = pair_owner.reshape(pair_count)
    source_ids = pair_source.reshape(pair_count)
    next_ages = shifted_2(positions[..., 0], "age", -1)
    next_stations = shifted_2(positions[:, :, :, 0, :], "span", -1)
    age_keep = (
        lax.axis_index("age") * age_here + jnp.arange(age_here, dtype=jnp.int32)
        < age_here * lax.axis_size("age") - 1
    ).astype(jnp.float32)
    station_keep = (
        lax.axis_index("span") * station_here + jnp.arange(station_here, dtype=jnp.int32)
        < station_here * lax.axis_size("span") - 1
    ).astype(jnp.float32)

    def build(nodes, after_age, after_station, circulation):
        trail_end = jnp.concatenate([nodes[..., 1:], after_age[..., None]], axis=-1)
        shed_end = jnp.concatenate([nodes[:, :, :, 1:, :], after_station[:, :, :, None, :]], axis=3)
        trail_gamma = circulation[0] * age_keep
        shed_gamma = circulation[1] * station_keep[:, None]
        stacked = jnp.concatenate(
            [nodes, trail_end, shed_end, trail_gamma[None], shed_gamma[None], core_radius[None]],
            axis=0,
        )
        return stacked.reshape(12, blocks_here, age_here)

    payload, build_pullback = jax.vjp(build, positions, next_ages, next_stations, strengths)

    def to_rows(array):
        return array.reshape(array.shape[0], blocks_here, age_here)

    def from_rows(array):
        return array.reshape(shape_here)

    def pick_rows(selector, values):
        return jnp.einsum(
            "sb,rba->rsa",
            selector,
            values,
            precision=lax.Precision.HIGHEST,
            preferred_element_type=jnp.float32,
        )

    def sum_rows(selector, values):
        return jnp.einsum(
            "sb,rsa->rba",
            selector,
            values,
            precision=lax.Precision.HIGHEST,
            preferred_element_type=jnp.float32,
        )

    target_blocks = to_rows(positions)
    seed_blocks = to_rows(adjoint_seed)
    earlier = (
        jnp.arange(pair_count, dtype=jnp.int32)[:, None]
        > jnp.arange(pair_count, dtype=jnp.int32)[None, :]
    )
    rank_within = jnp.sum(
        ((owner_ids[:, None] == owner_ids[None, :]) & earlier).astype(jnp.int32), axis=1
    )
    slot_index = owner_ids * capacity + rank_within
    slot_count = group_size * capacity
    slot_pick = (
        jnp.arange(slot_count, dtype=jnp.int32)[:, None] == slot_index[None, :]
    ).astype(jnp.float32)
    block_pick = (
        target_ids[:, None] == jnp.arange(blocks_here, dtype=jnp.int32)[None, :]
    ).astype(jnp.float32)
    slot_block = jnp.dot(slot_pick, block_pick, preferred_element_type=jnp.float32)
    rows_sent = pick_rows(slot_block, jnp.concatenate([target_blocks, seed_blocks], axis=0))
    ident = jnp.dot(
        slot_pick,
        (source_ids + 1).astype(jnp.float32),
        precision=lax.Precision.HIGHEST,
        preferred_element_type=jnp.float32,
    )
    outgoing = jnp.concatenate(
        [rows_sent, jnp.broadcast_to(ident[None, :, None], (1, slot_count, age_here))],
        axis=0,
    )
    received = lax.all_to_all(
        outgoing.reshape(7, group_size, capacity, age_here),
        ("turb", "age"),
        split_axis=1,
        concat_axis=1,
        tiled=True,
    ).reshape(7, slot_count, age_here)
    asked = received[6, :, 0].astype(jnp.int32) - 1
    safe_pick = (
        jnp.clip(asked, 0, blocks_here - 1)[:, None]
        == jnp.arange(blocks_here, dtype=jnp.int32)[None, :]
    ).astype(jnp.float32)
    slot_payload = pick_rows(safe_pick, payload)
    slot_answer, payload_terms = run_pairs(
        received[0:3], slot_payload, received[3:6] * time_step
    )
    payload_terms = jnp.concatenate(
        [payload_terms, jnp.zeros_like(payload_terms[:1])], axis=0
    )
    asked_pick = (
        asked[:, None] == jnp.arange(blocks_here, dtype=jnp.int32)[None, :]
    ).astype(jnp.float32)
    payload_grad = sum_rows(asked_pick, payload_terms)
    answered = lax.all_to_all(
        slot_answer.reshape(
            6, group_size, capacity, age_here
        ),
        ("turb", "age"),
        split_axis=1,
        concat_axis=1,
        tiled=True,
    ).reshape(6, slot_count, age_here)
    summed = sum_rows(slot_block, answered)
    velocity = summed[0:3]
    target_grad = summed[3:6]
    advected = positions + time_step * from_rows(velocity)
    advected = advected.at[0].add(time_step)
    grad_nodes, grad_after_age, grad_after_station, grad_strengths = build_pullback(payload_grad)
    from_prior_age = shifted_2(grad_after_age, "age", 1)
    from_prior_station = shifted_2(grad_after_station, "span", 1)
    grad_positions = adjoint_seed + grad_nodes + from_rows(target_grad)
    grad_positions = grad_positions.at[..., 0].add(from_prior_age)
    grad_positions = grad_positions.at[:, :, :, 0, :].add(from_prior_station)
    return (advected, grad_positions, grad_strengths)


def solution(mesh):
    placed = (
        P(None, "turb", None, "span", "age"),
        P(None, "turb", None, "span", "age"),
        P("turb", None, "span", "age"),
        P(None, "turb", None, "span", "age"),
        P("turb", "age", "span", None),
        P("turb", "age", "span", None),
        P("turb", "age", "span", None),
    )
    return jax.shard_map(
        local,
        mesh=mesh,
        in_specs=placed,
        out_specs=(
            P(None, "turb", None, "span", "age"),
            P(None, "turb", None, "span", "age"),
            P(None, "turb", None, "span", "age"),
        ),
        check_vma=False,
    )
```

```python
import math

import jax
import jax.numpy as jnp
from jax import lax
from jax.sharding import PartitionSpec as P
from jax.experimental import pallas as pl
from jax.experimental.pallas import tpu as pltpu

REACH = 8


time_step = 0.5
four_pi = 4.0 * math.pi
batch_rows = 16


def shifted_2(value, axis, steps):
    count = lax.axis_size(axis)
    leading, last = (max(0, -steps), min(count, count - steps))
    return lax.ppermute(value, axis, [(source, source + steps) for source in range(leading, last)])


def windows(payload):
    age_count = payload.shape[-1]
    padded = jnp.pad(payload, ((0, 0), (0, 0), (REACH, REACH)))
    stacked = jnp.stack(
        [
            padded[:, :, REACH + offset : REACH + offset + age_count]
            for offset in range(-REACH, REACH)
        ]
    )
    shifted = (
        jnp.arange(-REACH, REACH, dtype=jnp.int32)[:, None]
        + jnp.arange(age_count, dtype=jnp.int32)[None, :]
    )
    inside = ((shifted >= 0) & (shifted < age_count)).astype(payload.dtype)
    return (stacked, inside)


def induced(targets, payload):
    stacked, inside = windows(payload)
    begins = stacked[:, :, 0:3]
    end_points = jnp.stack([stacked[:, :, 3:6], stacked[:, :, 6:9]])
    gammas = jnp.stack([stacked[:, :, 9], stacked[:, :, 10]]) * inside[None, :, None, :]
    core = jnp.where(inside[:, None, :] > 0, stacked[:, :, 11], 1.0)
    core_sq = core * core
    core_quad = core_sq * core_sq
    from_begin = targets[None] - begins
    from_end = targets[None, None] - end_points
    along = end_points - begins[None]
    near = from_begin[None]
    cross_x = near[..., 1, :] * from_end[..., 2, :] - near[..., 2, :] * from_end[..., 1, :]
    cross_y = near[..., 2, :] * from_end[..., 0, :] - near[..., 0, :] * from_end[..., 2, :]
    cross_z = near[..., 0, :] * from_end[..., 1, :] - near[..., 1, :] * from_end[..., 0, :]
    cross_sq = cross_x * cross_x + cross_y * cross_y + cross_z * cross_z
    length_sq = jnp.sum(along * along, axis=-2) + core_sq
    dist_begin = jnp.sqrt(jnp.sum(from_begin * from_begin, axis=-2) + core_sq)
    dist_end = jnp.sqrt(jnp.sum(from_end * from_end, axis=-2) + core_sq)
    projected = jnp.sum(
        along * (near / dist_begin[None, :, :, None, :] - from_end / dist_end[..., None, :]),
        axis=-2,
    )
    factor = (
        gammas
        * projected
        / (four_pi * jnp.sqrt(cross_sq * cross_sq + core_quad * length_sq * length_sq))
    )
    return jnp.stack(
        [
            jnp.sum(cross_x * factor, axis=(0, 1)),
            jnp.sum(cross_y * factor, axis=(0, 1)),
            jnp.sum(cross_z * factor, axis=(0, 1)),
        ],
        axis=1,
    )


GROUP_PAIRS = 8
BLOCK_PAIRS = 64


def dot3(a, b):
    return a[0] * b[0] + a[1] * b[1] + a[2] * b[2]


def cross3(a, b):
    return (
        a[1] * b[2] - a[2] * b[1],
        a[2] * b[0] - a[0] * b[2],
        a[0] * b[1] - a[1] * b[0],
    )


def segment_pair(target, begin, ends, gammas, core, inside, weight):
    core_sq = core * core
    core_quad = core_sq * core_sq
    near = [target[i] - begin[i] for i in range(3)]
    inv_begin = lax.rsqrt(dot3(near, near) + core_sq)
    velocity = [0.0, 0.0, 0.0]
    grad_target = [0.0, 0.0, 0.0]
    grad_begin = [0.0, 0.0, 0.0]
    grad_ends = []
    grad_gammas = []
    for end_point, raw_gamma in zip(ends, gammas):
        gamma = jnp.where(inside, raw_gamma, 0.0)
        far = [target[i] - end_point[i] for i in range(3)]
        along = [end_point[i] - begin[i] for i in range(3)]
        cross = cross3(near, far)
        cross_sq = dot3(cross, cross)
        length_sq = dot3(along, along) + core_sq
        inv_end = lax.rsqrt(dot3(far, far) + core_sq)
        along_near = dot3(along, near)
        along_far = dot3(along, far)
        projected = along_near * inv_begin - along_far * inv_end
        inv_den = lax.rsqrt(cross_sq * cross_sq + core_quad * length_sq * length_sq)
        base = projected * inv_den * (1.0 / four_pi)
        factor = gamma * base
        for i in range(3):
            velocity[i] = velocity[i] + cross[i] * factor
        ct_factor = dot3(cross, weight)
        grad_gammas.append(jnp.where(inside, ct_factor * base, 0.0))
        ct_proj = ct_factor * gamma * inv_den * (1.0 / four_pi)
        ct_q = -0.5 * ct_factor * factor * inv_den * inv_den
        cross_scale = 4.0 * cross_sq * ct_q
        along_scale = 4.0 * core_quad * length_sq * ct_q
        ct_cross = [factor * weight[i] + cross_scale * cross[i] for i in range(3)]
        near_scale = ct_proj * inv_begin
        far_scale = ct_proj * inv_end
        near_radial = near_scale * along_near * inv_begin * inv_begin
        far_radial = far_scale * along_far * inv_end * inv_end
        from_far = cross3(far, ct_cross)
        from_near = cross3(ct_cross, near)
        ct_along = [
            along_scale * along[i] + near_scale * near[i] - far_scale * far[i] for i in range(3)
        ]
        ct_near = [near_scale * along[i] - near_radial * near[i] + from_far[i] for i in range(3)]
        ct_far = [-far_scale * along[i] + far_radial * far[i] + from_near[i] for i in range(3)]
        for i in range(3):
            grad_target[i] = grad_target[i] + ct_near[i] + ct_far[i]
            grad_begin[i] = grad_begin[i] - ct_near[i] - ct_along[i]
        grad_ends.append([ct_along[i] - ct_far[i] for i in range(3)])
    return velocity, grad_target, grad_begin, grad_ends, grad_gammas


def pair_group(target, cotangent, rows, lane):
    age_count = lane.shape[-1]
    velocity = [0.0] * 3
    grad_target = [0.0] * 3
    grad_rows = [0.0] * 11
    for offset in range(-REACH, REACH):
        amount = offset % age_count
        moved = [pltpu.roll(r, amount, 1) if amount else r for r in target]
        weight = [pltpu.roll(r, amount, 1) if amount else r for r in cotangent]
        inside = (lane - offset >= 0) & (lane - offset < age_count)
        u, d_t, d_b, d_ends, d_gammas = segment_pair(
            moved,
            rows[0:3],
            (rows[3:6], rows[6:9]),
            (rows[9], rows[10]),
            rows[11],
            inside,
            weight,
        )
        grads = list(d_b) + list(d_ends[0]) + list(d_ends[1]) + list(d_gammas)
        back = (-offset) % age_count
        for i in range(3):
            velocity[i] = velocity[i] + (pltpu.roll(u[i], back, 1) if back else u[i])
            grad_target[i] = grad_target[i] + (pltpu.roll(d_t[i], back, 1) if back else d_t[i])
        for i in range(11):
            grad_rows[i] = grad_rows[i] + grads[i]
    return velocity, grad_target, grad_rows


def pair_kernel(t_ref, s_ref, c_ref, v_ref, gt_ref, gs_ref):
    age_count = t_ref.shape[-1]
    lane = lax.broadcasted_iota(jnp.int32, (GROUP_PAIRS, age_count), 1)

    def body(group, carry):
        at = pl.ds(pl.multiple_of(group * GROUP_PAIRS, GROUP_PAIRS), GROUP_PAIRS)
        target = [t_ref[i, at, :] for i in range(3)]
        cotangent = [c_ref[i, at, :] * time_step for i in range(3)]
        rows = [s_ref[i, at, :] for i in range(12)]
        velocity, grad_target, grad_rows = pair_group(target, cotangent, rows, lane)
        for i in range(3):
            v_ref[i, at, :] = velocity[i]
            gt_ref[i, at, :] = grad_target[i]
        for i in range(11):
            gs_ref[i, at, :] = grad_rows[i]
        return carry

    lax.fori_loop(0, t_ref.shape[1] // GROUP_PAIRS, body, 0)


def run_pairs(targets, payload, cotangent):
    number = targets.shape[1]
    age_count = targets.shape[-1]
    step = min(number, BLOCK_PAIRS)

    def spec(rows):
        return pl.BlockSpec((rows, step, age_count), lambda i: (0, i, 0))

    return pl.pallas_call(
        pair_kernel,
        grid=(number // step,),
        in_specs=[
            spec(3),
            spec(12),
            pl.BlockSpec((3, step, age_count), lambda i: (1, i, 0)),
        ],
        out_specs=[spec(3), spec(3), spec(11)],
        out_shape=[
            jax.ShapeDtypeStruct((3, number, age_count), jnp.float32),
            jax.ShapeDtypeStruct((3, number, age_count), jnp.float32),
            jax.ShapeDtypeStruct((11, number, age_count), jnp.float32),
        ],
    )(targets, payload, cotangent)


def onehot_sum(indices, rows, values):
    selector = (jnp.arange(rows, dtype=jnp.int32)[:, None] == indices[None, :]).astype(jnp.float32)
    flat = values.reshape(values.shape[0], -1)
    summed = jnp.dot(
        selector, flat, precision=lax.Precision.HIGHEST, preferred_element_type=jnp.float32
    )
    return summed.reshape((rows,) + values.shape[1:])


def local(positions, strengths, core_radius, adjoint_seed, pair_target, pair_owner, pair_source):
    shape_here = positions.shape
    station_here = shape_here[3]
    age_here = shape_here[4]
    blocks_here = shape_here[1] * shape_here[2] * station_here
    group_size = lax.axis_size("turb") * lax.axis_size("age")
    pair_count = pair_target.shape[-1]
    capacity = 2 * pair_count // group_size
    target_ids = pair_target.reshape(pair_count)
    owner_ids = pair_owner.reshape(pair_count)
    source_ids = pair_source.reshape(pair_count)
    next_ages = shifted_2(positions[..., 0], "age", -1)
    next_stations = shifted_2(positions[:, :, :, 0, :], "span", -1)
    age_keep = (
        lax.axis_index("age") * age_here + jnp.arange(age_here, dtype=jnp.int32)
        < age_here * lax.axis_size("age") - 1
    ).astype(jnp.float32)
    station_keep = (
        lax.axis_index("span") * station_here + jnp.arange(station_here, dtype=jnp.int32)
        < station_here * lax.axis_size("span") - 1
    ).astype(jnp.float32)

    def build(nodes, after_age, after_station, circulation):
        trail_end = jnp.concatenate([nodes[..., 1:], after_age[..., None]], axis=-1)
        shed_end = jnp.concatenate([nodes[:, :, :, 1:, :], after_station[:, :, :, None, :]], axis=3)
        trail_gamma = circulation[0] * age_keep
        shed_gamma = circulation[1] * station_keep[:, None]
        stacked = jnp.concatenate(
            [nodes, trail_end, shed_end, trail_gamma[None], shed_gamma[None], core_radius[None]],
            axis=0,
        )
        return stacked.reshape(12, blocks_here, age_here)

    payload, build_pullback = jax.vjp(build, positions, next_ages, next_stations, strengths)

    def to_rows(array):
        return array.reshape(array.shape[0], blocks_here, age_here)

    def from_rows(array):
        return array.reshape(shape_here)

    def pick_rows(selector, values):
        return jnp.einsum(
            "sb,rba->rsa",
            selector,
            values,
            precision=lax.Precision.HIGHEST,
            preferred_element_type=jnp.float32,
        )

    def sum_rows(selector, values):
        return jnp.einsum(
            "sb,rsa->rba",
            selector,
            values,
            precision=lax.Precision.HIGHEST,
            preferred_element_type=jnp.float32,
        )

    target_blocks = to_rows(positions)
    seed_blocks = to_rows(adjoint_seed)
    earlier = (
        jnp.arange(pair_count, dtype=jnp.int32)[:, None]
        > jnp.arange(pair_count, dtype=jnp.int32)[None, :]
    )
    rank_within = jnp.sum(
        ((owner_ids[:, None] == owner_ids[None, :]) & earlier).astype(jnp.int32), axis=1
    )
    slot_index = owner_ids * capacity + rank_within
    slot_count = group_size * capacity
    slot_pick = (
        jnp.arange(slot_count, dtype=jnp.int32)[:, None] == slot_index[None, :]
    ).astype(jnp.float32)
    block_pick = (
        target_ids[:, None] == jnp.arange(blocks_here, dtype=jnp.int32)[None, :]
    ).astype(jnp.float32)
    slot_block = jnp.dot(slot_pick, block_pick, preferred_element_type=jnp.float32)
    rows_sent = pick_rows(slot_block, jnp.concatenate([target_blocks, seed_blocks], axis=0))
    ident = jnp.dot(
        slot_pick,
        (source_ids + 1).astype(jnp.float32),
        precision=lax.Precision.HIGHEST,
        preferred_element_type=jnp.float32,
    )
    outgoing = jnp.concatenate(
        [rows_sent, jnp.broadcast_to(ident[None, :, None], (1, slot_count, age_here))],
        axis=0,
    )
    received = lax.all_to_all(
        outgoing.reshape(7, group_size, capacity, age_here),
        ("turb", "age"),
        split_axis=1,
        concat_axis=1,
        tiled=True,
    ).reshape(7, slot_count, age_here)
    asked = received[6, :, 0].astype(jnp.int32) - 1
    safe_pick = (
        jnp.clip(asked, 0, blocks_here - 1)[:, None]
        == jnp.arange(blocks_here, dtype=jnp.int32)[None, :]
    ).astype(jnp.float32)
    slot_payload = pick_rows(safe_pick, payload)
    slot_velocity, slot_grad, payload_terms = run_pairs(
        received, slot_payload, received
    )
    payload_terms = jnp.concatenate(
        [payload_terms, jnp.zeros_like(payload_terms[:1])], axis=0
    )
    asked_pick = (
        asked[:, None] == jnp.arange(blocks_here, dtype=jnp.int32)[None, :]
    ).astype(jnp.float32)
    payload_grad = sum_rows(asked_pick, payload_terms)
    answered = lax.all_to_all(
        jnp.concatenate([slot_velocity, slot_grad], axis=0).reshape(
            6, group_size, capacity, age_here
        ),
        ("turb", "age"),
        split_axis=1,
        concat_axis=1,
        tiled=True,
    ).reshape(6, slot_count, age_here)
    summed = sum_rows(slot_block, answered)
    velocity = summed[0:3]
    target_grad = summed[3:6]
    advected = positions + time_step * from_rows(velocity)
    advected = advected.at[0].add(time_step)
    grad_nodes, grad_after_age, grad_after_station, grad_strengths = build_pullback(payload_grad)
    from_prior_age = shifted_2(grad_after_age, "age", 1)
    from_prior_station = shifted_2(grad_after_station, "span", 1)
    grad_positions = adjoint_seed + grad_nodes + from_rows(target_grad)
    grad_positions = grad_positions.at[..., 0].add(from_prior_age)
    grad_positions = grad_positions.at[:, :, :, 0, :].add(from_prior_station)
    return (advected, grad_positions, grad_strengths)


def solution(mesh):
    placed = (
        P(None, "turb", None, "span", "age"),
        P(None, "turb", None, "span", "age"),
        P("turb", None, "span", "age"),
        P(None, "turb", None, "span", "age"),
        P("turb", "age", "span", None),
        P("turb", "age", "span", None),
        P("turb", "age", "span", None),
    )
    return jax.shard_map(
        local,
        mesh=mesh,
        in_specs=placed,
        out_specs=(
            P(None, "turb", None, "span", "age"),
            P(None, "turb", None, "span", "age"),
            P(None, "turb", None, "span", "age"),
        ),
        check_vma=False,
    )
```

```python
import math

import jax
import jax.numpy as jnp
from jax import lax
from jax.sharding import PartitionSpec as P
from jax.experimental import pallas as pl
from jax.experimental.pallas import tpu as pltpu

REACH = 8


time_step = 0.5
four_pi = 4.0 * math.pi
batch_rows = 16


def shifted_2(value, axis, steps):
    count = lax.axis_size(axis)
    leading, last = (max(0, -steps), min(count, count - steps))
    return lax.ppermute(value, axis, [(source, source + steps) for source in range(leading, last)])


def windows(payload):
    age_count = payload.shape[-1]
    padded = jnp.pad(payload, ((0, 0), (0, 0), (REACH, REACH)))
    stacked = jnp.stack(
        [
            padded[:, :, REACH + offset : REACH + offset + age_count]
            for offset in range(-REACH, REACH)
        ]
    )
    shifted = (
        jnp.arange(-REACH, REACH, dtype=jnp.int32)[:, None]
        + jnp.arange(age_count, dtype=jnp.int32)[None, :]
    )
    inside = ((shifted >= 0) & (shifted < age_count)).astype(payload.dtype)
    return (stacked, inside)


def induced(targets, payload):
    stacked, inside = windows(payload)
    begins = stacked[:, :, 0:3]
    end_points = jnp.stack([stacked[:, :, 3:6], stacked[:, :, 6:9]])
    gammas = jnp.stack([stacked[:, :, 9], stacked[:, :, 10]]) * inside[None, :, None, :]
    core = jnp.where(inside[:, None, :] > 0, stacked[:, :, 11], 1.0)
    core_sq = core * core
    core_quad = core_sq * core_sq
    from_begin = targets[None] - begins
    from_end = targets[None, None] - end_points
    along = end_points - begins[None]
    near = from_begin[None]
    cross_x = near[..., 1, :] * from_end[..., 2, :] - near[..., 2, :] * from_end[..., 1, :]
    cross_y = near[..., 2, :] * from_end[..., 0, :] - near[..., 0, :] * from_end[..., 2, :]
    cross_z = near[..., 0, :] * from_end[..., 1, :] - near[..., 1, :] * from_end[..., 0, :]
    cross_sq = cross_x * cross_x + cross_y * cross_y + cross_z * cross_z
    length_sq = jnp.sum(along * along, axis=-2) + core_sq
    dist_begin = jnp.sqrt(jnp.sum(from_begin * from_begin, axis=-2) + core_sq)
    dist_end = jnp.sqrt(jnp.sum(from_end * from_end, axis=-2) + core_sq)
    projected = jnp.sum(
        along * (near / dist_begin[None, :, :, None, :] - from_end / dist_end[..., None, :]),
        axis=-2,
    )
    factor = (
        gammas
        * projected
        / (four_pi * jnp.sqrt(cross_sq * cross_sq + core_quad * length_sq * length_sq))
    )
    return jnp.stack(
        [
            jnp.sum(cross_x * factor, axis=(0, 1)),
            jnp.sum(cross_y * factor, axis=(0, 1)),
            jnp.sum(cross_z * factor, axis=(0, 1)),
        ],
        axis=1,
    )


GROUP_PAIRS = 8
BLOCK_PAIRS = 128


def dot3(a, b):
    return a[0] * b[0] + a[1] * b[1] + a[2] * b[2]


def cross3(a, b):
    return (
        a[1] * b[2] - a[2] * b[1],
        a[2] * b[0] - a[0] * b[2],
        a[0] * b[1] - a[1] * b[0],
    )


def segment_pair(target, begin, ends, gammas, core, inside, weight):
    core_sq = core * core
    core_quad = core_sq * core_sq
    near = [target[i] - begin[i] for i in range(3)]
    inv_begin = lax.rsqrt(dot3(near, near) + core_sq)
    velocity = [0.0, 0.0, 0.0]
    grad_target = [0.0, 0.0, 0.0]
    grad_begin = [0.0, 0.0, 0.0]
    grad_ends = []
    grad_gammas = []
    for end_point, raw_gamma in zip(ends, gammas):
        gamma = jnp.where(inside, raw_gamma, 0.0)
        far = [target[i] - end_point[i] for i in range(3)]
        along = [end_point[i] - begin[i] for i in range(3)]
        cross = cross3(near, far)
        cross_sq = dot3(cross, cross)
        length_sq = dot3(along, along) + core_sq
        inv_end = lax.rsqrt(dot3(far, far) + core_sq)
        along_near = dot3(along, near)
        along_far = dot3(along, far)
        projected = along_near * inv_begin - along_far * inv_end
        inv_den = lax.rsqrt(cross_sq * cross_sq + core_quad * length_sq * length_sq)
        base = projected * inv_den * (1.0 / four_pi)
        factor = gamma * base
        for i in range(3):
            velocity[i] = velocity[i] + cross[i] * factor
        ct_factor = dot3(cross, weight)
        grad_gammas.append(jnp.where(inside, ct_factor * base, 0.0))
        ct_proj = ct_factor * gamma * inv_den * (1.0 / four_pi)
        ct_q = -0.5 * ct_factor * factor * inv_den * inv_den
        cross_scale = 4.0 * cross_sq * ct_q
        along_scale = 4.0 * core_quad * length_sq * ct_q
        ct_cross = [factor * weight[i] + cross_scale * cross[i] for i in range(3)]
        near_scale = ct_proj * inv_begin
        far_scale = ct_proj * inv_end
        near_radial = near_scale * along_near * inv_begin * inv_begin
        far_radial = far_scale * along_far * inv_end * inv_end
        from_far = cross3(far, ct_cross)
        from_near = cross3(ct_cross, near)
        ct_along = [
            along_scale * along[i] + near_scale * near[i] - far_scale * far[i] for i in range(3)
        ]
        ct_near = [near_scale * along[i] - near_radial * near[i] + from_far[i] for i in range(3)]
        ct_far = [-far_scale * along[i] + far_radial * far[i] + from_near[i] for i in range(3)]
        for i in range(3):
            grad_target[i] = grad_target[i] + ct_near[i] + ct_far[i]
            grad_begin[i] = grad_begin[i] - ct_near[i] - ct_along[i]
        grad_ends.append([ct_along[i] - ct_far[i] for i in range(3)])
    return velocity, grad_target, grad_begin, grad_ends, grad_gammas


def pair_group(target, cotangent, rows, lane):
    age_count = lane.shape[-1]
    velocity = [0.0] * 3
    grad_target = [0.0] * 3
    grad_rows = [0.0] * 11
    for offset in range(-REACH, REACH):
        amount = offset % age_count
        moved = [pltpu.roll(r, amount, 1) if amount else r for r in target]
        weight = [pltpu.roll(r, amount, 1) if amount else r for r in cotangent]
        inside = (lane - offset >= 0) & (lane - offset < age_count)
        u, d_t, d_b, d_ends, d_gammas = segment_pair(
            moved,
            rows[0:3],
            (rows[3:6], rows[6:9]),
            (rows[9], rows[10]),
            rows[11],
            inside,
            weight,
        )
        grads = list(d_b) + list(d_ends[0]) + list(d_ends[1]) + list(d_gammas)
        back = (-offset) % age_count
        for i in range(3):
            velocity[i] = velocity[i] + (pltpu.roll(u[i], back, 1) if back else u[i])
            grad_target[i] = grad_target[i] + (pltpu.roll(d_t[i], back, 1) if back else d_t[i])
        for i in range(11):
            grad_rows[i] = grad_rows[i] + grads[i]
    return velocity, grad_target, grad_rows


def pair_kernel(t_ref, s_ref, c_ref, v_ref, gt_ref, gs_ref):
    age_count = t_ref.shape[-1]
    lane = lax.broadcasted_iota(jnp.int32, (GROUP_PAIRS, age_count), 1)

    def body(group, carry):
        at = pl.ds(pl.multiple_of(group * GROUP_PAIRS, GROUP_PAIRS), GROUP_PAIRS)
        target = [t_ref[i, at, :] for i in range(3)]
        cotangent = [c_ref[i, at, :] * time_step for i in range(3)]
        rows = [s_ref[i, at, :] for i in range(12)]
        velocity, grad_target, grad_rows = pair_group(target, cotangent, rows, lane)
        for i in range(3):
            v_ref[i, at, :] = velocity[i]
            gt_ref[i, at, :] = grad_target[i]
        for i in range(11):
            gs_ref[i, at, :] = grad_rows[i]
        return carry

    lax.fori_loop(0, t_ref.shape[1] // GROUP_PAIRS, body, 0)


def run_pairs(targets, payload, cotangent):
    number = targets.shape[1]
    age_count = targets.shape[-1]
    step = min(number, BLOCK_PAIRS)

    def spec(rows):
        return pl.BlockSpec((rows, step, age_count), lambda i: (0, i, 0))

    return pl.pallas_call(
        pair_kernel,
        grid=(number // step,),
        in_specs=[
            spec(3),
            spec(12),
            pl.BlockSpec((3, step, age_count), lambda i: (1, i, 0)),
        ],
        out_specs=[spec(3), spec(3), spec(11)],
        out_shape=[
            jax.ShapeDtypeStruct((3, number, age_count), jnp.float32),
            jax.ShapeDtypeStruct((3, number, age_count), jnp.float32),
            jax.ShapeDtypeStruct((11, number, age_count), jnp.float32),
        ],
    )(targets, payload, cotangent)


def onehot_sum(indices, rows, values):
    selector = (jnp.arange(rows, dtype=jnp.int32)[:, None] == indices[None, :]).astype(jnp.float32)
    flat = values.reshape(values.shape[0], -1)
    summed = jnp.dot(
        selector, flat, precision=lax.Precision.HIGHEST, preferred_element_type=jnp.float32
    )
    return summed.reshape((rows,) + values.shape[1:])


def local(positions, strengths, core_radius, adjoint_seed, pair_target, pair_owner, pair_source):
    shape_here = positions.shape
    station_here = shape_here[3]
    age_here = shape_here[4]
    blocks_here = shape_here[1] * shape_here[2] * station_here
    group_size = lax.axis_size("turb") * lax.axis_size("age")
    pair_count = pair_target.shape[-1]
    capacity = 2 * pair_count // group_size
    target_ids = pair_target.reshape(pair_count)
    owner_ids = pair_owner.reshape(pair_count)
    source_ids = pair_source.reshape(pair_count)
    next_ages = shifted_2(positions[..., 0], "age", -1)
    next_stations = shifted_2(positions[:, :, :, 0, :], "span", -1)
    age_keep = (
        lax.axis_index("age") * age_here + jnp.arange(age_here, dtype=jnp.int32)
        < age_here * lax.axis_size("age") - 1
    ).astype(jnp.float32)
    station_keep = (
        lax.axis_index("span") * station_here + jnp.arange(station_here, dtype=jnp.int32)
        < station_here * lax.axis_size("span") - 1
    ).astype(jnp.float32)

    def build(nodes, after_age, after_station, circulation):
        trail_end = jnp.concatenate([nodes[..., 1:], after_age[..., None]], axis=-1)
        shed_end = jnp.concatenate([nodes[:, :, :, 1:, :], after_station[:, :, :, None, :]], axis=3)
        trail_gamma = circulation[0] * age_keep
        shed_gamma = circulation[1] * station_keep[:, None]
        stacked = jnp.concatenate(
            [nodes, trail_end, shed_end, trail_gamma[None], shed_gamma[None], core_radius[None]],
            axis=0,
        )
        return stacked.reshape(12, blocks_here, age_here)

    payload, build_pullback = jax.vjp(build, positions, next_ages, next_stations, strengths)

    def to_rows(array):
        return array.reshape(array.shape[0], blocks_here, age_here)

    def from_rows(array):
        return array.reshape(shape_here)

    def pick_rows(selector, values):
        return jnp.einsum(
            "sb,rba->rsa",
            selector,
            values,
            precision=lax.Precision.HIGHEST,
            preferred_element_type=jnp.float32,
        )

    def sum_rows(selector, values):
        return jnp.einsum(
            "sb,rsa->rba",
            selector,
            values,
            precision=lax.Precision.HIGHEST,
            preferred_element_type=jnp.float32,
        )

    target_blocks = to_rows(positions)
    seed_blocks = to_rows(adjoint_seed)
    earlier = (
        jnp.arange(pair_count, dtype=jnp.int32)[:, None]
        > jnp.arange(pair_count, dtype=jnp.int32)[None, :]
    )
    rank_within = jnp.sum(
        ((owner_ids[:, None] == owner_ids[None, :]) & earlier).astype(jnp.int32), axis=1
    )
    slot_index = owner_ids * capacity + rank_within
    slot_count = group_size * capacity
    slot_pick = (
        jnp.arange(slot_count, dtype=jnp.int32)[:, None] == slot_index[None, :]
    ).astype(jnp.float32)
    block_pick = (
        target_ids[:, None] == jnp.arange(blocks_here, dtype=jnp.int32)[None, :]
    ).astype(jnp.float32)
    slot_block = jnp.dot(slot_pick, block_pick, preferred_element_type=jnp.float32)
    rows_sent = pick_rows(slot_block, jnp.concatenate([target_blocks, seed_blocks], axis=0))
    ident = jnp.dot(
        slot_pick,
        (source_ids + 1).astype(jnp.float32),
        precision=lax.Precision.HIGHEST,
        preferred_element_type=jnp.float32,
    )
    outgoing = jnp.concatenate(
        [rows_sent, jnp.broadcast_to(ident[None, :, None], (1, slot_count, age_here))],
        axis=0,
    )
    received = lax.all_to_all(
        outgoing.reshape(7, group_size, capacity, age_here),
        ("turb", "age"),
        split_axis=1,
        concat_axis=1,
        tiled=True,
    ).reshape(7, slot_count, age_here)
    asked = received[6, :, 0].astype(jnp.int32) - 1
    safe_pick = (
        jnp.clip(asked, 0, blocks_here - 1)[:, None]
        == jnp.arange(blocks_here, dtype=jnp.int32)[None, :]
    ).astype(jnp.float32)
    slot_payload = pick_rows(safe_pick, payload)
    slot_velocity, slot_grad, payload_terms = run_pairs(
        received, slot_payload, received
    )
    payload_terms = jnp.concatenate(
        [payload_terms, jnp.zeros_like(payload_terms[:1])], axis=0
    )
    asked_pick = (
        asked[:, None] == jnp.arange(blocks_here, dtype=jnp.int32)[None, :]
    ).astype(jnp.float32)
    payload_grad = sum_rows(asked_pick, payload_terms)
    answered = lax.all_to_all(
        jnp.concatenate([slot_velocity, slot_grad], axis=0).reshape(
            6, group_size, capacity, age_here
        ),
        ("turb", "age"),
        split_axis=1,
        concat_axis=1,
        tiled=True,
    ).reshape(6, slot_count, age_here)
    summed = sum_rows(slot_block, answered)
    velocity = summed[0:3]
    target_grad = summed[3:6]
    advected = positions + time_step * from_rows(velocity)
    advected = advected.at[0].add(time_step)
    grad_nodes, grad_after_age, grad_after_station, grad_strengths = build_pullback(payload_grad)
    from_prior_age = shifted_2(grad_after_age, "age", 1)
    from_prior_station = shifted_2(grad_after_station, "span", 1)
    grad_positions = adjoint_seed + grad_nodes + from_rows(target_grad)
    grad_positions = grad_positions.at[..., 0].add(from_prior_age)
    grad_positions = grad_positions.at[:, :, :, 0, :].add(from_prior_station)
    return (advected, grad_positions, grad_strengths)


def solution(mesh):
    placed = (
        P(None, "turb", None, "span", "age"),
        P(None, "turb", None, "span", "age"),
        P("turb", None, "span", "age"),
        P(None, "turb", None, "span", "age"),
        P("turb", "age", "span", None),
        P("turb", "age", "span", None),
        P("turb", "age", "span", None),
    )
    return jax.shard_map(
        local,
        mesh=mesh,
        in_specs=placed,
        out_specs=(
            P(None, "turb", None, "span", "age"),
            P(None, "turb", None, "span", "age"),
            P(None, "turb", None, "span", "age"),
        ),
        check_vma=False,
    )
```
